32 devices in a mesh: groups: 2 (over y), expert: 4 (over z), dp: 4 (over x, core).
Axes of the slice: x: 2, y: 2, z: 4, core: 2. Of those that a mesh axis runs over, the one named last changes fastest.
Arguments:
- out_grad: bfloat16 [4096, 2048], P(('groups', 'expert', 'dp')), parts along dimension 0, may hold values from -0.5 to 0.5
- gate_weights: bfloat16 [4096, 8], P(('groups', 'expert', 'dp')), parts along dimension 0, may hold values from 0.049804688 to 0.5
- expert_ids: int32 [4096, 8], P(('groups', 'expert', 'dp')), parts along dimension 0, may hold values from 0 to 31, all different within a row; in each aligned block of 128 rows (0 to 127, 128 to 255, ...) at most 36 rows name the same one
- hidden: bfloat16 [32, 8, 4, 36, 768], P('expert', ('groups', 'dp')), parts along dimension 1, may hold values from -6 to 6
- down_weight: bfloat16 [32, 768, 2048], P('expert', None, 'dp'), may hold values from -0.21875 to 0.21875
Outputs:
- weight_grad: float32 [64, 768, 2048], P(('groups', 'expert'), None, 'dp'), parts along dimension 0
- gate_grad: float32 [4096, 8], P(('groups', 'expert', 'dp')), parts along dimension 0
The draws below stay inside these ranges and needn't reach their ends.
There are 2 independent parts, one for each index of `groups`. The reference program is written for one: setup_inputs(seed, part) draws one part's arguments, and reference() takes and returns one part's arrays. A program takes and returns all parts, laid end to end along the dimension named above; an argument that names none is the same for every part. Nothing has to cross between parts.
Inputs may be any that keep to these rules, and one draw needn't show every extreme that they name: `expert_ids`: each token names 8 different experts; within each block of 128 tokens (one device's tokens) no expert is named by more than 36 tokens, a bound that some block reaches.
All inputs are finite; a program needn't handle non-finite values.
Results may differ from the reference program's by a relative error of at most 0.0095.
Values may be sent and summed in bfloat16 or wider, within the bound.
No kernel may reach another device: no remote copies, remote signals or barrier semaphores. Data moves between devices by JAX's collectives and lax.ppermute only.
A program may use at most 128 MiB of HBM per device.

```python
import math
import jax
import jax.numpy as jnp
import numpy as np
from jax import lax

DW = 2048
FFW = 768
TOPK = 8
TOK_DEV = 128
EXPERTS = 32
CAP = 36
TOKENS = 2048
N_EXPERT = 4
N_DP = 4


def block_levels(key, shape, shards, least, top_value):
    def one(dim, blocks):
        draws = jax.random.uniform(jax.random.fold_in(jax.random.fold_in(key, 6), dim), (blocks,), jnp.float32, least / len(shards), top_value / len(shards))
        return jnp.repeat(jnp.exp(draws), shape[dim] // blocks).reshape((-1,) + (1,) * (len(shape) - dim - 1))

    loudness = one(*shards[0])
    for cut in shards[1:]:
        loudness = loudness * one(*cut)
    return loudness


def shared_out(rng, own, number, rows, amount, top, bound, slope):
    order = jax.random.permutation(rng, amount)
    heavy_load, ordinary = shares(amount, rows * top, bound, slope, True), shares(amount, rows * top, bound, slope, False)
    places = jnp.arange(amount)

    def named(sizes, turn):
        used = int((sizes > 0).sum())
        fixed = max(1, used // 4)
        moved = fixed + (places - fixed + turn * (used - fixed)) % max(1, amount - fixed)
        return jnp.zeros((amount,), jnp.int32).at[order[jnp.where(places < fixed, places, moved)]].set(jnp.asarray(sizes, jnp.int32))

    sizes = jnp.where(number % 4 == 0, named(heavy_load, number // 4), named(ordinary, number - number // 4 - 1))
    mixed = jax.random.permutation(jax.random.fold_in(own, 3), amount)
    donor, taker = mixed[0:amount // 2 * 2:2], mixed[1:amount // 2 * 2:2]
    room = jnp.minimum(sizes[donor] - 1, bound - sizes[taker]) // 2
    room = jnp.where((donor == order[0]) | (taker == order[0]) | (sizes[taker] == 0), 0, jnp.maximum(room, 0))
    moved = jax.random.randint(jax.random.fold_in(own, 4), (amount // 2,), 0, 1 << 20) % (room + 1)
    sizes = sizes.at[donor].add(-moved).at[taker].add(moved)
    members = jnp.searchsorted(jnp.cumsum(sizes), jnp.arange(rows * top), side="right").astype(jnp.int32)
    listing = members.reshape(top, rows).T
    listing = listing[jax.random.permutation(jax.random.fold_in(own, 1), rows)]
    turn = jax.random.randint(jax.random.fold_in(own, 2), (rows, 1), 0, top)
    return jnp.take_along_axis(listing, (jnp.arange(top)[None, :] + turn) % top, axis=1)


def shares(number_of, total, bound, lean, full):
    weights = [(1 << 20) // math.isqrt(grade ** lean) + 1 for grade in range(1, number_of + 1)]
    largest = bound if full else min(bound, max(-(-total // number_of), total * weights[0] // sum(weights)))
    least = 1 if total - largest >= number_of - 1 else 0
    counts, rest = [largest] + [least] * (number_of - 1), total - largest - least * (number_of - 1)
    while rest > 0:
        movable = [i for i in range(1, number_of) if counts[i] < largest] or [i for i in range(1, number_of) if counts[i] < bound]
        mass, remaining = sum([weights[i] for i in movable]), rest
        for i in movable:
            extra = min(bound - counts[i], max(1, remaining * weights[i] // mass), rest)
            counts[i] = counts[i] + extra
            rest = rest - extra
    return np.array(counts)


def scatter_about(stream_key, extent, width, reach, shards=(), held_as=jnp.bfloat16):
    values = jax.random.normal(stream_key, extent, jnp.float32) * width
    if len(shards) > 0:
        values = block_levels(stream_key, extent, shards, -0.22, 0.18) * values
    return jnp.clip(values, min=-reach, max=reach).astype(held_as)


def setup_inputs(seed: int = 0, part: int = 0) -> dict:
    seeds = jax.random.split(jax.random.key(seed), 6)
    own_keys = jax.random.split(jax.random.fold_in(seeds[5], part), 6)
    out_grad = scatter_about(own_keys[0], (TOKENS, DW), 0.0625, 0.5, ((0, 16),))
    gate_weights = jnp.clip(0.049804688 + 0.4501953 * jax.random.uniform(own_keys[1], (TOKENS, TOPK), jnp.float32) ** block_levels(own_keys[1], (TOKENS, TOPK), ((0, 16),), -0.2, 0.2), 0.049804688, 0.5).astype(jnp.bfloat16)
    expert_ids_keys = jax.random.split(jax.random.fold_in(own_keys[2], 1), TOKENS // TOK_DEV)
    expert_ids_turns = jax.random.permutation(jax.random.fold_in(own_keys[2], 3), TOKENS // TOK_DEV)
    expert_ids = jax.vmap(lambda own, number: shared_out(jax.random.fold_in(own_keys[2], 2), own, number, TOK_DEV, EXPERTS, TOPK, CAP, 2))(expert_ids_keys, expert_ids_turns).reshape((TOKENS, TOPK))
    hidden = scatter_about(own_keys[3], (EXPERTS, N_DP, N_EXPERT, CAP, FFW), 1.0, 6.0, ((0, 4), (1, 4)))
    down_weight = scatter_about(seeds[4], (EXPERTS, FFW, DW), FFW ** -0.5, 0.21875, ((0, 4), (2, 4)))
    return dict(out_grad=out_grad, gate_weights=gate_weights, expert_ids=expert_ids, hidden=hidden, down_weight=down_weight)


def reference(out_grad, gate_weights, expert_ids, hidden, down_weight):
    blocks = TOKENS // TOK_DEV
    id_flat = expert_ids.reshape(blocks, TOK_DEV * TOPK)
    onehot = (id_flat[:, :, None] == jnp.arange(EXPERTS, dtype=jnp.int32)[None, None, :]).astype(jnp.int32)
    ranked = jnp.cumsum(onehot, axis=1) - 1
    slot_index = jnp.sum(ranked * onehot, axis=2).astype(jnp.int32)
    block_index = jnp.arange(blocks, dtype=jnp.int32)[:, None]
    source = block_index // N_DP
    replica = block_index % N_DP
    flat_index = (((id_flat * N_DP + replica) * N_EXPERT + source) * CAP + slot_index).astype(jnp.int32)
    pair_index = jnp.arange(blocks * TOK_DEV * TOPK, dtype=jnp.int32)
    table_size = EXPERTS * N_DP * N_EXPERT * CAP
    table = jnp.full((table_size,), TOKENS * TOPK, jnp.int32).at[flat_index.reshape(-1)].set(pair_index)
    table = table.reshape(EXPERTS, N_DP * N_EXPERT * CAP)
    grad_ext = jnp.concatenate([out_grad, jnp.zeros((1, DW), out_grad.dtype)], axis=0)
    gate_ext = jnp.concatenate([gate_weights.reshape(-1), jnp.zeros((1,), gate_weights.dtype)], axis=0)

    def per_expert(packed):
        source_table, hidden_e, weight_e = packed
        grad_rows = grad_ext[source_table // TOPK]
        gate_rows = gate_ext[source_table]
        scaled = (gate_rows.astype(jnp.float32)[:, None] * grad_rows.astype(jnp.float32)).astype(jnp.bfloat16)
        hidden_rows = hidden_e.reshape(N_DP, N_EXPERT * CAP, FFW)
        partial_value = jnp.einsum("irf,ird->ifd", hidden_rows.astype(jnp.float32),
                             scaled.reshape(N_DP, N_EXPERT * CAP, DW).astype(jnp.float32)).astype(jnp.bfloat16)
        weight_grad = jnp.sum(partial_value.astype(jnp.float32), axis=0)
        expert_out = jnp.dot(hidden_rows.reshape(-1, FFW), weight_e, preferred_element_type=jnp.float32)
        slot_grad = jnp.sum(grad_rows.astype(jnp.float32) * expert_out, axis=1)
        return weight_grad, slot_grad

    weight_grad, slot_grad = lax.map(per_expert, (table, hidden, down_weight))
    gate_grad = slot_grad.reshape(-1)[flat_index.reshape(-1)].reshape(TOKENS, TOPK)
    return weight_grad, gate_grad
```

```python
import jax
import jax.numpy as jnp
from jax import lax
from jax.sharding import PartitionSpec as P


def per_device(out_grad, gate_weights, expert_ids, hidden, down_weight):
    tok_rows, top_count = expert_ids.shape
    row_width = out_grad.shape[1]
    local_count = hidden.shape[0]
    source_count = hidden.shape[2]
    capacity = hidden.shape[3]
    hidden_width = hidden.shape[4]
    peer_count = lax.axis_size("expert")
    shards = lax.axis_size("dp")
    expert_count = local_count * peer_count
    col_width = row_width // shards
    block_count = peer_count * shards
    f32 = jnp.float32
    bf16 = jnp.bfloat16

    cols = out_grad.reshape(tok_rows, shards, col_width)
    cols = lax.all_to_all(cols, "dp", split_axis=1, concat_axis=0, tiled=True)
    cols = cols.reshape(shards, tok_rows, col_width)
    grad_all = lax.all_gather(cols, "expert", axis=0, tiled=False)
    grad_all = grad_all.reshape(block_count, tok_rows, col_width)

    ids_all = lax.all_gather(expert_ids, ("expert", "dp"), axis=0, tiled=True)
    ids_all = ids_all.reshape(block_count, tok_rows, top_count)
    gate_all = lax.all_gather(gate_weights, ("expert", "dp"), axis=0, tiled=True)
    gate_all = gate_all.reshape(block_count, tok_rows, top_count)

    hidden_all = lax.all_gather(hidden, "dp", axis=1, tiled=True)

    my_experts = lax.axis_index("expert") * local_count + jnp.arange(local_count, dtype=jnp.int32)
    hit = ids_all[:, :, :, None] == my_experts[None, None, None, :]
    chose = jnp.any(hit, axis=2)
    gate_hit = jnp.sum(jnp.where(hit, gate_all.astype(f32)[:, :, :, None], 0.0), axis=2)
    before = (jnp.arange(tok_rows)[:, None] < jnp.arange(tok_rows)[None, :]).astype(bf16)
    rank = jnp.einsum(
        "bul,ut->btl", chose.astype(bf16), before, preferred_element_type=f32
    ).astype(jnp.int32)
    slot_ids = jnp.arange(capacity, dtype=jnp.int32)
    chose_t = chose.transpose(0, 2, 1)
    rank_t = rank.transpose(0, 2, 1)
    gate_t = gate_hit.transpose(0, 2, 1)
    select = chose_t[:, :, None, :] & (rank_t[:, :, None, :] == slot_ids[None, None, :, None])
    select_gate = jnp.where(select, gate_t[:, :, None, :], 0.0).astype(bf16)
    grad_rows = jnp.einsum(
        "blct,btd->blcd", select.astype(bf16), grad_all, preferred_element_type=f32
    ).astype(bf16)
    scaled = jnp.einsum(
        "blct,btd->blcd", select_gate, grad_all, preferred_element_type=f32
    ).astype(bf16)
    grad_rows = grad_rows.reshape(peer_count, shards, local_count, capacity, col_width)
    scaled = scaled.reshape(peer_count, shards, local_count, capacity, col_width)

    weight_grad = None
    for replica in range(shards):
        part = jnp.einsum(
            "lscf,slcd->lfd",
            hidden_all[:, replica],
            scaled[:, replica],
            preferred_element_type=f32,
        ).astype(bf16).astype(f32)
        weight_grad = part if weight_grad is None else weight_grad + part

    expert_out = jnp.einsum(
        "liscf,lfd->silcd", hidden_all, down_weight, preferred_element_type=f32
    )
    slot_part = jnp.sum(grad_rows.astype(f32) * expert_out, axis=4)
    send_back = slot_part.reshape(block_count, local_count, capacity)
    returned = lax.all_to_all(
        send_back, ("expert", "dp"), split_axis=0, concat_axis=0, tiled=True
    )
    returned = returned.reshape(peer_count, shards, local_count, capacity)
    slot_grad = jnp.sum(returned, axis=1).reshape(expert_count * capacity)

    own_chose = jnp.any(
        expert_ids[:, :, None] == jnp.arange(expert_count, dtype=jnp.int32)[None, None, :], axis=1
    )
    own_rank = jnp.einsum(
        "ue,ut->te", own_chose.astype(bf16), before, preferred_element_type=f32
    ).astype(jnp.int32)
    own_slot = jnp.take_along_axis(own_rank, expert_ids, axis=1)
    gate_grad = slot_grad[expert_ids * capacity + own_slot]
    return (weight_grad, gate_grad)


def solution(mesh):
    return jax.shard_map(
        per_device,
        mesh=mesh,
        in_specs=(
            P(("groups", "expert", "dp"), None),
            P(("groups", "expert", "dp"), None),
            P(("groups", "expert", "dp"), None),
            P("expert", ("groups", "dp"), None, None, None),
            P("expert", None, "dp"),
        ),
        out_specs=(P(("groups", "expert"), None, "dp"), P(("groups", "expert", "dp"), None)),
        check_vma=False,
    )
```

```python
import jax
import jax.numpy as jnp
from jax import lax
from jax.sharding import PartitionSpec as P


def per_device(out_grad, gate_weights, expert_ids, hidden, down_weight):
    tok_rows, top_count = expert_ids.shape
    row_width = out_grad.shape[1]
    local_count = hidden.shape[0]
    capacity = hidden.shape[3]
    peer_count = lax.axis_size("expert")
    shards = lax.axis_size("dp")
    expert_count = local_count * peer_count
    col_width = row_width // shards
    block_count = peer_count * shards
    f32 = jnp.float32
    bf16 = jnp.bfloat16
    my_dp = lax.axis_index("dp")

    fetched = lax.ppermute(hidden, "dp", [(j, j ^ 2) for j in range(shards)])
    paired = lax.ppermute(
        jnp.concatenate([hidden, fetched], axis=1), "dp", [(j, j ^ 1) for j in range(shards)]
    )
    pieces = [hidden, fetched, paired[:, 0:1], paired[:, 1:2]]
    piece_replica = [my_dp, my_dp ^ 2, my_dp ^ 1, my_dp ^ 3]

    meta = jnp.concatenate([expert_ids.astype(bf16), gate_weights], axis=1).reshape(-1)
    meta_len = meta.shape[0]
    meta_rows = -(-meta_len // col_width)
    meta = jnp.pad(meta, (0, meta_rows * col_width - meta_len)).reshape(meta_rows, 1, col_width)
    cols = out_grad.reshape(tok_rows, shards, col_width)
    cols = jnp.concatenate([cols, jnp.broadcast_to(meta, (meta_rows, shards, col_width))], axis=0)
    cols = lax.all_to_all(cols, "dp", split_axis=1, concat_axis=0, tiled=True)
    cols = cols.reshape(shards, tok_rows + meta_rows, col_width)
    got = lax.all_gather(cols, "expert", axis=0, tiled=False)
    got = got.reshape(block_count, tok_rows + meta_rows, col_width)
    grad_all = got[:, :tok_rows]
    meta_all = got[:, tok_rows:].reshape(block_count, meta_rows * col_width)[:, :meta_len]
    meta_all = meta_all.reshape(block_count, tok_rows, 2 * top_count)
    ids_all = meta_all[:, :, :top_count].astype(jnp.int32)
    gate_all = meta_all[:, :, top_count:]

    my_experts = lax.axis_index("expert") * local_count + jnp.arange(local_count, dtype=jnp.int32)
    hit = ids_all[:, :, :, None] == my_experts[None, None, None, :]
    chose = jnp.any(hit, axis=2)
    gate_hit = jnp.sum(jnp.where(hit, gate_all.astype(f32)[:, :, :, None], 0.0), axis=2)
    before = (jnp.arange(tok_rows)[:, None] < jnp.arange(tok_rows)[None, :]).astype(bf16)
    rank = jnp.einsum(
        "bul,ut->btl", chose.astype(bf16), before, preferred_element_type=f32
    ).astype(jnp.int32)
    slot_ids = jnp.arange(capacity, dtype=jnp.int32)
    chose_t = chose.transpose(0, 2, 1)
    rank_t = rank.transpose(0, 2, 1)
    gate_t = gate_hit.transpose(0, 2, 1)
    select = chose_t[:, :, None, :] & (rank_t[:, :, None, :] == slot_ids[None, None, :, None])
    select_gate = jnp.where(select, gate_t[:, :, None, :], 0.0).astype(bf16)
    grad_rows = jnp.einsum(
        "blct,btd->blcd", select.astype(bf16), grad_all, preferred_element_type=f32
    ).astype(bf16)
    scaled = jnp.einsum(
        "blct,btd->blcd", select_gate, grad_all, preferred_element_type=f32
    ).astype(bf16)
    grad_rows = grad_rows.reshape(peer_count, shards, local_count, capacity, col_width)
    scaled = scaled.reshape(peer_count, shards, local_count, capacity, col_width)

    weight_grad = None
    slot_part = jnp.zeros((peer_count, shards, local_count, capacity), f32)
    for piece, replica in zip(pieces, piece_replica):
        piece = piece[:, 0]
        scaled_r = lax.dynamic_index_in_dim(scaled, replica, axis=1, keepdims=False)
        rows_r = lax.dynamic_index_in_dim(grad_rows, replica, axis=1, keepdims=False)
        part = jnp.einsum(
            "lscf,slcd->lfd", piece, scaled_r, preferred_element_type=f32
        ).astype(bf16).astype(f32)
        weight_grad = part if weight_grad is None else weight_grad + part
        expert_out = jnp.einsum(
            "lscf,lfd->slcd", piece, down_weight, preferred_element_type=f32
        )
        slot_r = jnp.sum(rows_r.astype(f32) * expert_out, axis=3)
        slot_part = lax.dynamic_update_index_in_dim(slot_part, slot_r, replica, axis=1)

    send_back = slot_part.reshape(block_count, local_count, capacity)
    returned = lax.all_to_all(
        send_back, ("expert", "dp"), split_axis=0, concat_axis=0, tiled=True
    )
    returned = returned.reshape(peer_count, shards, local_count, capacity)
    slot_grad = jnp.sum(returned, axis=1).reshape(expert_count, capacity)

    own_hit = expert_ids[:, :, None] == jnp.arange(expert_count, dtype=jnp.int32)[None, None, :]
    own_chose = jnp.any(own_hit, axis=1)
    own_rank = jnp.einsum(
        "ue,ut->te", own_chose.astype(bf16), before, preferred_element_type=f32
    ).astype(jnp.int32)
    own_slot = jnp.sum(jnp.where(own_hit, own_rank[:, None, :], 0), axis=2)
    by_slot = jnp.sum(jnp.where(own_hit[:, :, :, None], slot_grad[None, None], 0.0), axis=2)
    gate_grad = jnp.sum(
        jnp.where(own_slot[:, :, None] == slot_ids[None, None, :], by_slot, 0.0), axis=2
    )
    return (weight_grad, gate_grad)


def solution(mesh):
    return jax.shard_map(
        per_device,
        mesh=mesh,
        in_specs=(
            P(("groups", "expert", "dp"), None),
            P(("groups", "expert", "dp"), None),
            P(("groups", "expert", "dp"), None),
            P("expert", ("groups", "dp"), None, None, None),
            P("expert", None, "dp"),
        ),
        out_specs=(P(("groups", "expert"), None, "dp"), P(("groups", "expert", "dp"), None)),
        check_vma=False,
    )
```

```python
import jax
import jax.numpy as jnp
from jax import lax
from jax.experimental import pallas as pl
from jax.sharding import PartitionSpec as P


def expert_body(h_ref, s_ref, g_ref, w_ref, wg_ref, slot_ref):
    chunk = pl.program_id(1)
    h = h_ref[0]
    part = lax.dot_general(
        h, s_ref[0], (((0,), (0,)), ((), ())), preferred_element_type=jnp.float32
    )

    @pl.when(chunk == 0)
    def _():
        wg_ref[0] = part

    @pl.when(chunk != 0)
    def _():
        wg_ref[0] = wg_ref[0] + part

    out = jnp.dot(h, w_ref[0], preferred_element_type=jnp.float32)
    slot_ref[0] = jnp.sum(g_ref[0].astype(jnp.float32) * out, axis=1, keepdims=True)


def expert_kernel(hidden_rows, scaled_rows, grad_rows, weight):
    local_count, slot_rows, hidden_width = hidden_rows.shape
    col_width = scaled_rows.shape[2]
    chunk = slot_rows
    for size in (576, 512, 384, 256, 128):
        if slot_rows % size == 0:
            chunk = size
            break
    steps = slot_rows // chunk
    return pl.pallas_call(
        expert_body,
        grid=(local_count, steps),
        in_specs=[
            pl.BlockSpec((1, chunk, hidden_width), lambda l, r: (l, r, 0)),
            pl.BlockSpec((1, chunk, col_width), lambda l, r: (l, r, 0)),
            pl.BlockSpec((1, chunk, col_width), lambda l, r: (l, r, 0)),
            pl.BlockSpec((1, hidden_width, col_width), lambda l, r: (l, 0, 0)),
        ],
        out_specs=[
            pl.BlockSpec((1, hidden_width, col_width), lambda l, r: (l, 0, 0)),
            pl.BlockSpec((1, chunk, 1), lambda l, r: (l, r, 0)),
        ],
        out_shape=[
            jax.ShapeDtypeStruct((local_count, hidden_width, col_width), jnp.float32),
            jax.ShapeDtypeStruct((local_count, slot_rows, 1), jnp.float32),
        ],
    )(hidden_rows, scaled_rows, grad_rows, weight)


def per_device(out_grad, gate_weights, expert_ids, hidden, down_weight):
    tok_rows, top_count = expert_ids.shape
    row_width = out_grad.shape[1]
    local_count = hidden.shape[0]
    capacity = hidden.shape[3]
    hidden_width = hidden.shape[4]
    peer_count = lax.axis_size("expert")
    shards = lax.axis_size("dp")
    expert_count = local_count * peer_count
    col_width = row_width // shards
    block_count = peer_count * shards
    f32 = jnp.float32
    bf16 = jnp.bfloat16
    my_dp = lax.axis_index("dp")

    fetched = lax.ppermute(hidden, "dp", [(j, j ^ 2) for j in range(shards)])
    paired = lax.ppermute(
        jnp.concatenate([hidden, fetched], axis=1), "dp", [(j, j ^ 1) for j in range(shards)]
    )
    pieces = [hidden, fetched, paired[:, 0:1], paired[:, 1:2]]
    piece_replica = [my_dp, my_dp ^ 2, my_dp ^ 1, my_dp ^ 3]

    meta = jnp.concatenate([expert_ids.astype(bf16), gate_weights], axis=1).reshape(-1)
    meta_len = meta.shape[0]
    meta_rows = -(-meta_len // col_width)
    meta = jnp.pad(meta, (0, meta_rows * col_width - meta_len)).reshape(meta_rows, 1, col_width)
    cols = out_grad.reshape(tok_rows, shards, col_width)
    cols = jnp.concatenate([cols, jnp.broadcast_to(meta, (meta_rows, shards, col_width))], axis=0)
    cols = lax.all_to_all(cols, "dp", split_axis=1, concat_axis=0, tiled=True)
    cols = cols.reshape(shards, tok_rows + meta_rows, col_width)
    got = lax.all_gather(cols, "expert", axis=0, tiled=False)
    got = got.reshape(block_count, tok_rows + meta_rows, col_width)
    grad_all = got[:, :tok_rows]
    meta_all = got[:, tok_rows:].reshape(block_count, meta_rows * col_width)[:, :meta_len]
    meta_all = meta_all.reshape(block_count, tok_rows, 2 * top_count)
    ids_all = meta_all[:, :, :top_count].astype(jnp.int32)
    gate_all = meta_all[:, :, top_count:]

    my_experts = lax.axis_index("expert") * local_count + jnp.arange(local_count, dtype=jnp.int32)
    hit = ids_all[:, :, :, None] == my_experts[None, None, None, :]
    chose = jnp.any(hit, axis=2)
    gate_hit = jnp.sum(jnp.where(hit, gate_all.astype(f32)[:, :, :, None], 0.0), axis=2)
    before = (jnp.arange(tok_rows)[:, None] < jnp.arange(tok_rows)[None, :]).astype(bf16)
    rank = jnp.einsum(
        "bul,ut->btl", chose.astype(bf16), before, preferred_element_type=f32
    ).astype(jnp.int32)
    slot_ids = jnp.arange(capacity, dtype=jnp.int32)
    chose_t = chose.transpose(0, 2, 1)
    rank_t = rank.transpose(0, 2, 1)
    gate_t = gate_hit.transpose(0, 2, 1)
    select = chose_t[:, :, None, :] & (rank_t[:, :, None, :] == slot_ids[None, None, :, None])
    select_gate = jnp.where(select, gate_t[:, :, None, :], 0.0).astype(bf16)
    grad_rows = jnp.einsum(
        "blct,btd->blcd", select.astype(bf16), grad_all, preferred_element_type=f32
    ).astype(bf16)
    scaled = jnp.einsum(
        "blct,btd->blcd", select_gate, grad_all, preferred_element_type=f32
    ).astype(bf16)
    grad_rows = grad_rows.reshape(peer_count, shards, local_count, capacity, col_width)
    scaled = scaled.reshape(peer_count, shards, local_count, capacity, col_width)

    hidden_all = jnp.concatenate([hidden, fetched, paired], axis=1)
    piece_of = jnp.array([0, 2, 1, 3], jnp.int32)[jnp.arange(shards, dtype=jnp.int32) ^ my_dp]
    hidden_all = jnp.take(hidden_all, piece_of, axis=1)
    slot_rows = shards * peer_count * capacity
    hidden_rows = hidden_all.reshape(local_count, slot_rows, hidden_width)
    scaled_rows = scaled.transpose(2, 1, 0, 3, 4).reshape(local_count, slot_rows, col_width)
    grad_slot_rows = grad_rows.transpose(2, 1, 0, 3, 4).reshape(local_count, slot_rows, col_width)
    weight_grad, slot_part = expert_kernel(hidden_rows, scaled_rows, grad_slot_rows, down_weight)
    slot_part = slot_part.reshape(local_count, shards, peer_count, capacity).transpose(2, 1, 0, 3)
    send_back = slot_part.reshape(block_count, local_count, capacity)
    returned = lax.all_to_all(
        send_back, ("expert", "dp"), split_axis=0, concat_axis=0, tiled=True
    )
    returned = returned.reshape(peer_count, shards, local_count, capacity)
    slot_grad = jnp.sum(returned, axis=1).reshape(expert_count, capacity)

    own_hit = expert_ids[:, :, None] == jnp.arange(expert_count, dtype=jnp.int32)[None, None, :]
    own_chose = jnp.any(own_hit, axis=1)
    own_rank = jnp.einsum(
        "ue,ut->te", own_chose.astype(bf16), before, preferred_element_type=f32
    ).astype(jnp.int32)
    own_slot = jnp.sum(jnp.where(own_hit, own_rank[:, None, :], 0), axis=2)
    by_slot = jnp.sum(jnp.where(own_hit[:, :, :, None], slot_grad[None, None], 0.0), axis=2)
    gate_grad = jnp.sum(
        jnp.where(own_slot[:, :, None] == slot_ids[None, None, :], by_slot, 0.0), axis=2
    )
    return (weight_grad, gate_grad)


def solution(mesh):
    return jax.shard_map(
        per_device,
        mesh=mesh,
        in_specs=(
            P(("groups", "expert", "dp"), None),
            P(("groups", "expert", "dp"), None),
            P(("groups", "expert", "dp"), None),
            P("expert", ("groups", "dp"), None, None, None),
            P("expert", None, "dp"),
        ),
        out_specs=(P(("groups", "expert"), None, "dp"), P(("groups", "expert", "dp"), None)),
        check_vma=False,
    )
```

```python
import jax
import jax.numpy as jnp
from jax import lax
from jax.experimental import pallas as pl
from jax.sharding import PartitionSpec as P


def expert_body(h_ref, s_ref, g_ref, w_ref, wg_ref, slot_ref):
    chunk = pl.program_id(1)
    blocks, slots, hidden_width = h_ref.shape[1:]
    col_width = s_ref.shape[3]
    rows = blocks * slots
    h = h_ref[0].reshape(rows, hidden_width)
    part = lax.dot_general(
        h, s_ref[:, 0].reshape(rows, col_width), (((0,), (0,)), ((), ())),
        preferred_element_type=jnp.float32,
    )

    @pl.when(chunk == 0)
    def _():
        wg_ref[0] = part

    @pl.when(chunk != 0)
    def _():
        wg_ref[0] = wg_ref[0] + part

    out = jnp.dot(h, w_ref[0], preferred_element_type=jnp.float32)
    g = g_ref[:, 0].reshape(rows, col_width).astype(jnp.float32)
    slot_ref[0] = jnp.sum(g * out, axis=1, keepdims=True)


def expert_kernel(hidden_rows, scaled_rows, grad_rows, weight):
    local_count, block_count, slots, hidden_width = hidden_rows.shape
    col_width = scaled_rows.shape[3]
    chunk = block_count
    for size in (16, 8, 4, 2, 1):
        if block_count % size == 0:
            chunk = size
            break
    steps = block_count // chunk
    rows = chunk * slots
    return pl.pallas_call(
        expert_body,
        grid=(local_count, steps),
        in_specs=[
            pl.BlockSpec((1, chunk, slots, hidden_width), lambda l, r: (l, r, 0, 0)),
            pl.BlockSpec((chunk, 1, slots, col_width), lambda l, r: (r, l, 0, 0)),
            pl.BlockSpec((chunk, 1, slots, col_width), lambda l, r: (r, l, 0, 0)),
            pl.BlockSpec((1, hidden_width, col_width), lambda l, r: (l, 0, 0)),
        ],
        out_specs=[
            pl.BlockSpec((1, hidden_width, col_width), lambda l, r: (l, 0, 0)),
            pl.BlockSpec((1, rows, 1), lambda l, r: (l, r, 0)),
        ],
        out_shape=[
            jax.ShapeDtypeStruct((local_count, hidden_width, col_width), jnp.float32),
            jax.ShapeDtypeStruct((local_count, block_count * slots, 1), jnp.float32),
        ],
    )(hidden_rows, scaled_rows, grad_rows, weight)


def per_device(out_grad, gate_weights, expert_ids, hidden, down_weight):
    tok_rows, top_count = expert_ids.shape
    row_width = out_grad.shape[1]
    local_count = hidden.shape[0]
    capacity = hidden.shape[3]
    hidden_width = hidden.shape[4]
    peer_count = lax.axis_size("expert")
    shards = lax.axis_size("dp")
    expert_count = local_count * peer_count
    col_width = row_width // shards
    block_count = peer_count * shards
    f32 = jnp.float32
    bf16 = jnp.bfloat16
    my_dp = lax.axis_index("dp")

    meta = jnp.concatenate([expert_ids.astype(bf16), gate_weights], axis=1).reshape(-1)
    meta_len = meta.shape[0]
    meta_rows = -(-meta_len // col_width)
    meta = jnp.pad(meta, (0, meta_rows * col_width - meta_len)).reshape(meta_rows, 1, col_width)
    cols = out_grad.reshape(tok_rows, shards, col_width)
    cols = jnp.concatenate([cols, jnp.broadcast_to(meta, (meta_rows, shards, col_width))], axis=0)
    cols = lax.all_to_all(cols, "dp", split_axis=1, concat_axis=0, tiled=True)
    cols = cols.reshape(shards, tok_rows + meta_rows, col_width)

    hidden_sent, cols = lax.optimization_barrier((hidden, cols))
    fetched = lax.ppermute(hidden_sent, "dp", [(j, j ^ 2) for j in range(shards)])
    paired = lax.ppermute(
        jnp.concatenate([hidden_sent, fetched], axis=1), "dp", [(j, j ^ 1) for j in range(shards)]
    )
    got = lax.all_gather(cols, "expert", axis=0, tiled=False)
    got = got.reshape(block_count, tok_rows + meta_rows, col_width)
    grad_all = got[:, :tok_rows]
    meta_all = got[:, tok_rows:].reshape(block_count, meta_rows * col_width)[:, :meta_len]
    meta_all = meta_all.reshape(block_count, tok_rows, 2 * top_count)
    ids_all = meta_all[:, :, :top_count].astype(jnp.int32)
    gate_all = meta_all[:, :, top_count:]

    my_experts = lax.axis_index("expert") * local_count + jnp.arange(local_count, dtype=jnp.int32)
    hit = ids_all[:, :, :, None] == my_experts[None, None, None, :]
    chose = jnp.any(hit, axis=2)
    gate_hit = jnp.sum(jnp.where(hit, gate_all.astype(f32)[:, :, :, None], 0.0), axis=2)
    before = (jnp.arange(tok_rows)[:, None] < jnp.arange(tok_rows)[None, :]).astype(bf16)
    rank = jnp.einsum(
        "bul,ut->btl", chose.astype(bf16), before, preferred_element_type=f32
    ).astype(jnp.int32)
    padded = -(-capacity // 8) * 8
    slot_ids = jnp.arange(padded, dtype=jnp.int32)
    chose_t = chose.transpose(0, 2, 1)
    rank_t = rank.transpose(0, 2, 1)
    gate_t = gate_hit.transpose(0, 2, 1)
    select = chose_t[:, :, None, :] & (rank_t[:, :, None, :] == slot_ids[None, None, :, None])
    select_gate = jnp.where(select, gate_t[:, :, None, :], 0.0).astype(bf16)
    grad_rows = jnp.einsum(
        "blct,btd->blcd", select.astype(bf16), grad_all, preferred_element_type=f32
    ).astype(bf16)
    scaled = jnp.einsum(
        "blct,btd->blcd", select_gate, grad_all, preferred_element_type=f32
    ).astype(bf16)

    offset = jnp.arange(shards, dtype=jnp.int32) ^ my_dp
    own, far, near, near_far = hidden, fetched, paired[:, 0:1], paired[:, 1:2]
    off = offset[None, :, None, None, None]
    hidden_all = jnp.where(
        off == 0, own, jnp.where(off == 2, far, jnp.where(off == 1, near, near_far))
    )
    hidden_all = hidden_all.transpose(0, 2, 1, 3, 4).reshape(local_count, block_count, capacity, hidden_width)
    hidden_all = jnp.pad(hidden_all, ((0, 0), (0, 0), (0, padded - capacity), (0, 0)))
    weight_grad, slot_part = expert_kernel(hidden_all, scaled, grad_rows, down_weight)
    slot_part = slot_part.reshape(local_count, block_count, padded)[:, :, :capacity]
    slot_part = slot_part.transpose(1, 0, 2)
    send_back = slot_part.reshape(block_count, local_count, capacity)
    returned = lax.all_to_all(
        send_back, ("expert", "dp"), split_axis=0, concat_axis=0, tiled=True
    )
    returned = returned.reshape(peer_count, shards, local_count, capacity)
    slot_grad = jnp.sum(returned, axis=1).reshape(expert_count, capacity)

    own_hit = expert_ids[:, :, None] == jnp.arange(expert_count, dtype=jnp.int32)[None, None, :]
    own_chose = jnp.any(own_hit, axis=1)
    own_rank = jnp.einsum(
        "ue,ut->te", own_chose.astype(bf16), before, preferred_element_type=f32
    ).astype(jnp.int32)
    own_slot = jnp.sum(jnp.where(own_hit, own_rank[:, None, :], 0), axis=2)
    by_slot = jnp.sum(jnp.where(own_hit[:, :, :, None], slot_grad[None, None], 0.0), axis=2)
    gate_grad = jnp.sum(
        jnp.where(own_slot[:, :, None] == slot_ids[None, None, :capacity], by_slot, 0.0), axis=2
    )
    return (weight_grad, gate_grad)


def solution(mesh):
    return jax.shard_map(
        per_device,
        mesh=mesh,
        in_specs=(
            P(("groups", "expert", "dp"), None),
            P(("groups", "expert", "dp"), None),
            P(("groups", "expert", "dp"), None),
            P("expert", ("groups", "dp"), None, None, None),
            P("expert", None, "dp"),
        ),
        out_specs=(P(("groups", "expert"), None, "dp"), P(("groups", "expert", "dp"), None)),
        check_vma=False,
    )
```

```python
import jax
import jax.numpy as jnp
from jax import lax
from jax.experimental import pallas as pl
from jax.sharding import PartitionSpec as P


def expert_body(h_ref, s_ref, g_ref, w_ref, wg_ref, slot_ref):
    chunk = pl.program_id(1)
    blocks, slots, hidden_width = h_ref.shape[1:]
    col_width = s_ref.shape[3]
    rows = blocks * slots
    h = h_ref[0].reshape(rows, hidden_width)
    part = lax.dot_general(
        h, s_ref[:, 0].reshape(rows, col_width), (((0,), (0,)), ((), ())),
        preferred_element_type=jnp.float32,
    )

    @pl.when(chunk == 0)
    def _():
        wg_ref[0] = part

    @pl.when(chunk != 0)
    def _():
        wg_ref[0] = wg_ref[0] + part

    out = jnp.dot(h, w_ref[0], preferred_element_type=jnp.float32)
    g = g_ref[:, 0].reshape(rows, col_width).astype(jnp.float32)
    slot_ref[0] = jnp.sum(g * out, axis=1, keepdims=True)


def expert_kernel(hidden_rows, scaled_rows, grad_rows, weight):
    local_count, block_count, slots, hidden_width = hidden_rows.shape
    col_width = scaled_rows.shape[3]
    chunk = block_count
    for size in (16, 8, 4, 2, 1):
        if block_count % size == 0:
            chunk = size
            break
    steps = block_count // chunk
    rows = chunk * slots
    return pl.pallas_call(
        expert_body,
        grid=(local_count, steps),
        in_specs=[
            pl.BlockSpec((1, chunk, slots, hidden_width), lambda l, r: (l, r, 0, 0)),
            pl.BlockSpec((chunk, 1, slots, col_width), lambda l, r: (r, l, 0, 0)),
            pl.BlockSpec((chunk, 1, slots, col_width), lambda l, r: (r, l, 0, 0)),
            pl.BlockSpec((1, hidden_width, col_width), lambda l, r: (l, 0, 0)),
        ],
        out_specs=[
            pl.BlockSpec((1, hidden_width, col_width), lambda l, r: (l, 0, 0)),
            pl.BlockSpec((1, rows, 1), lambda l, r: (l, r, 0)),
        ],
        out_shape=[
            jax.ShapeDtypeStruct((local_count, hidden_width, col_width), jnp.float32),
            jax.ShapeDtypeStruct((local_count, block_count * slots, 1), jnp.float32),
        ],
    )(hidden_rows, scaled_rows, grad_rows, weight)


def per_device(out_grad, gate_weights, expert_ids, hidden, down_weight):
    tok_rows, top_count = expert_ids.shape
    row_width = out_grad.shape[1]
    local_count = hidden.shape[0]
    capacity = hidden.shape[3]
    hidden_width = hidden.shape[4]
    peer_count = lax.axis_size("expert")
    shards = lax.axis_size("dp")
    expert_count = local_count * peer_count
    col_width = row_width // shards
    block_count = peer_count * shards
    f32 = jnp.float32
    bf16 = jnp.bfloat16
    my_dp = lax.axis_index("dp")

    meta = jnp.concatenate([expert_ids.astype(bf16), gate_weights], axis=1).reshape(-1)
    meta_len = meta.shape[0]
    meta_rows = -(-meta_len // col_width)
    meta = jnp.pad(meta, (0, meta_rows * col_width - meta_len)).reshape(meta_rows, 1, col_width)
    cols = out_grad.reshape(tok_rows, shards, col_width)
    cols = jnp.concatenate([cols, jnp.broadcast_to(meta, (meta_rows, shards, col_width))], axis=0)
    cols = lax.all_to_all(cols, "dp", split_axis=1, concat_axis=0, tiled=True)
    cols = cols.reshape(shards, tok_rows + meta_rows, col_width)

    hidden_sent, cols = lax.optimization_barrier((hidden, cols))
    near = lax.ppermute(hidden_sent, "dp", [(j, j ^ 1) for j in range(shards)])
    far = lax.ppermute(hidden_sent, "dp", [(j, j ^ 2) for j in range(shards)])
    near_far = lax.ppermute(far, "dp", [(j, j ^ 1) for j in range(shards)])
    got = lax.all_gather(cols, "expert", axis=0, tiled=False)
    got = got.reshape(block_count, tok_rows + meta_rows, col_width)
    grad_all = got[:, :tok_rows]
    meta_all = got[:, tok_rows:].reshape(block_count, meta_rows * col_width)[:, :meta_len]
    meta_all = meta_all.reshape(block_count, tok_rows, 2 * top_count)
    ids_all = meta_all[:, :, :top_count].astype(jnp.int32)
    gate_all = meta_all[:, :, top_count:]

    my_experts = lax.axis_index("expert") * local_count + jnp.arange(local_count, dtype=jnp.int32)
    hit = ids_all[:, :, :, None] == my_experts[None, None, None, :]
    chose = jnp.any(hit, axis=2)
    gate_hit = jnp.sum(jnp.where(hit, gate_all.astype(f32)[:, :, :, None], 0.0), axis=2)
    before = (jnp.arange(tok_rows)[:, None] < jnp.arange(tok_rows)[None, :]).astype(bf16)
    rank = jnp.einsum(
        "bul,ut->btl", chose.astype(bf16), before, preferred_element_type=f32
    ).astype(jnp.int32)
    padded = -(-capacity // 8) * 8
    slot_ids = jnp.arange(padded, dtype=jnp.int32)
    chose_t = chose.transpose(0, 2, 1)
    rank_t = rank.transpose(0, 2, 1)
    gate_t = gate_hit.transpose(0, 2, 1)
    select = chose_t[:, :, None, :] & (rank_t[:, :, None, :] == slot_ids[None, None, :, None])
    select_gate = jnp.where(select, gate_t[:, :, None, :], 0.0).astype(bf16)
    grad_rows = jnp.einsum(
        "blct,btd->blcd", select.astype(bf16), grad_all, preferred_element_type=f32
    ).astype(bf16)
    scaled = jnp.einsum(
        "blct,btd->blcd", select_gate, grad_all, preferred_element_type=f32
    ).astype(bf16)

    hidden_all = jnp.zeros((local_count, peer_count, shards, padded, hidden_width), bf16)
    for piece, replica in ((hidden, my_dp), (near, my_dp ^ 1), (far, my_dp ^ 2), (near_far, my_dp ^ 3)):
        hidden_all = lax.dynamic_update_slice(
            hidden_all, piece.transpose(0, 2, 1, 3, 4), (0, 0, replica, 0, 0)
        )
    hidden_all = hidden_all.reshape(local_count, block_count, padded, hidden_width)
    weight_grad, slot_part = expert_kernel(hidden_all, scaled, grad_rows, down_weight)
    slot_part = slot_part.reshape(local_count, block_count, padded)[:, :, :capacity]
    slot_part = slot_part.transpose(1, 0, 2)
    send_back = slot_part.reshape(block_count, local_count, capacity)
    returned = lax.all_to_all(
        send_back, ("expert", "dp"), split_axis=0, concat_axis=0, tiled=True
    )
    returned = returned.reshape(peer_count, shards, local_count, capacity)
    slot_grad = jnp.sum(returned, axis=1).reshape(expert_count, capacity)

    own_hit = expert_ids[:, :, None] == jnp.arange(expert_count, dtype=jnp.int32)[None, None, :]
    own_chose = jnp.any(own_hit, axis=1)
    own_rank = jnp.einsum(
        "ue,ut->te", own_chose.astype(bf16), before, preferred_element_type=f32
    ).astype(jnp.int32)
    own_slot = jnp.sum(jnp.where(own_hit, own_rank[:, None, :], 0), axis=2)
    by_slot = jnp.sum(jnp.where(own_hit[:, :, :, None], slot_grad[None, None], 0.0), axis=2)
    gate_grad = jnp.sum(
        jnp.where(own_slot[:, :, None] == slot_ids[None, None, :capacity], by_slot, 0.0), axis=2
    )
    return (weight_grad, gate_grad)


def solution(mesh):
    return jax.shard_map(
        per_device,
        mesh=mesh,
        in_specs=(
            P(("groups", "expert", "dp"), None),
            P(("groups", "expert", "dp"), None),
            P(("groups", "expert", "dp"), None),
            P("expert", ("groups", "dp"), None, None, None),
            P("expert", None, "dp"),
        ),
        out_specs=(P(("groups", "expert"), None, "dp"), P(("groups", "expert", "dp"), None)),
        check_vma=False,
    )
```

```python
import jax
import jax.numpy as jnp
from jax import lax
from jax.experimental import pallas as pl
from jax.sharding import PartitionSpec as P


def expert_body(h_ref, s_ref, g_ref, w_ref, wg_ref, slot_ref):
    chunk = pl.program_id(1)
    blocks, slots, hidden_width = h_ref.shape[1:]
    col_width = s_ref.shape[3]
    rows = blocks * slots
    h = h_ref[0].reshape(rows, hidden_width)
    part = lax.dot_general(
        h, s_ref[:, 0].reshape(rows, col_width), (((0,), (0,)), ((), ())),
        preferred_element_type=jnp.float32,
    )

    @pl.when(chunk == 0)
    def _():
        wg_ref[0] = part

    @pl.when(chunk != 0)
    def _():
        wg_ref[0] = wg_ref[0] + part

    out = jnp.dot(h, w_ref[0], preferred_element_type=jnp.float32)
    g = g_ref[:, 0].reshape(rows, col_width).astype(jnp.float32)
    slot_ref[0] = jnp.sum(g * out, axis=1, keepdims=True)


def expert_kernel(hidden_rows, scaled_rows, grad_rows, weight):
    local_count, block_count, slots, hidden_width = hidden_rows.shape
    col_width = scaled_rows.shape[3]
    chunk = block_count
    for size in (16, 8, 4, 2, 1):
        if block_count % size == 0:
            chunk = size
            break
    steps = block_count // chunk
    rows = chunk * slots
    return pl.pallas_call(
        expert_body,
        grid=(local_count, steps),
        in_specs=[
            pl.BlockSpec((1, chunk, slots, hidden_width), lambda l, r: (l, r, 0, 0)),
            pl.BlockSpec((chunk, 1, slots, col_width), lambda l, r: (r, l, 0, 0)),
            pl.BlockSpec((chunk, 1, slots, col_width), lambda l, r: (r, l, 0, 0)),
            pl.BlockSpec((1, hidden_width, col_width), lambda l, r: (l, 0, 0)),
        ],
        out_specs=[
            pl.BlockSpec((1, hidden_width, col_width), lambda l, r: (l, 0, 0)),
            pl.BlockSpec((1, rows, 1), lambda l, r: (l, r, 0)),
        ],
        out_shape=[
            jax.ShapeDtypeStruct((local_count, hidden_width, col_width), jnp.float32),
            jax.ShapeDtypeStruct((local_count, block_count * slots, 1), jnp.float32),
        ],
    )(hidden_rows, scaled_rows, grad_rows, weight)


def per_device(out_grad, gate_weights, expert_ids, hidden, down_weight):
    tok_rows, top_count = expert_ids.shape
    row_width = out_grad.shape[1]
    local_count = hidden.shape[0]
    capacity = hidden.shape[3]
    hidden_width = hidden.shape[4]
    peer_count = lax.axis_size("expert")
    shards = lax.axis_size("dp")
    expert_count = local_count * peer_count
    col_width = row_width // shards
    block_count = peer_count * shards
    f32 = jnp.float32
    bf16 = jnp.bfloat16
    my_dp = lax.axis_index("dp")

    meta = jnp.concatenate([expert_ids.astype(bf16), gate_weights], axis=1).reshape(-1)
    meta_len = meta.shape[0]
    meta_rows = -(-meta_len // col_width)
    meta = jnp.pad(meta, (0, meta_rows * col_width - meta_len)).reshape(meta_rows, 1, col_width)
    cols = out_grad.reshape(tok_rows, shards, col_width)
    cols = jnp.concatenate([cols, jnp.broadcast_to(meta, (meta_rows, shards, col_width))], axis=0)
    cols = lax.all_to_all(cols, "dp", split_axis=1, concat_axis=0, tiled=True)
    cols = cols.reshape(shards, tok_rows + meta_rows, col_width)
    piece_xor = jnp.array([0, 2, 1, 3], jnp.int32)
    cols = jnp.take(cols, piece_xor ^ my_dp, axis=0)

    hidden_sent, cols = lax.optimization_barrier((hidden, cols))
    halves = [hidden_sent[: local_count // 2], hidden_sent[local_count // 2 :]]
    if local_count < 2:
        halves = [hidden_sent]
    near = [lax.ppermute(h, "dp", [(j, j ^ 1) for j in range(shards)]) for h in halves]
    far = [lax.ppermute(h, "dp", [(j, j ^ 2) for j in range(shards)]) for h in halves]
    near_far = [lax.ppermute(h, "dp", [(j, j ^ 1) for j in range(shards)]) for h in far]
    near = jnp.concatenate(near, axis=0)
    far = jnp.concatenate(far, axis=0)
    near_far = jnp.concatenate(near_far, axis=0)
    got = lax.all_gather(cols, "expert", axis=0, tiled=False)
    got = got.reshape(block_count, tok_rows + meta_rows, col_width)
    grad_all = got[:, :tok_rows]
    meta_all = got[:, tok_rows:].reshape(block_count, meta_rows * col_width)[:, :meta_len]
    meta_all = meta_all.reshape(block_count, tok_rows, 2 * top_count)
    ids_all = meta_all[:, :, :top_count].astype(jnp.int32)
    gate_all = meta_all[:, :, top_count:]

    my_experts = lax.axis_index("expert") * local_count + jnp.arange(local_count, dtype=jnp.int32)
    hit = ids_all[:, :, :, None] == my_experts[None, None, None, :]
    chose = jnp.any(hit, axis=2)
    gate_hit = jnp.sum(jnp.where(hit, gate_all.astype(f32)[:, :, :, None], 0.0), axis=2)
    before = (jnp.arange(tok_rows)[:, None] < jnp.arange(tok_rows)[None, :]).astype(bf16)
    rank = jnp.einsum(
        "bul,ut->btl", chose.astype(bf16), before, preferred_element_type=f32
    ).astype(jnp.int32)
    padded = -(-capacity // 8) * 8
    slot_ids = jnp.arange(padded, dtype=jnp.int32)
    chose_t = chose.transpose(0, 2, 1)
    rank_t = rank.transpose(0, 2, 1)
    gate_t = gate_hit.transpose(0, 2, 1)
    select = chose_t[:, :, None, :] & (rank_t[:, :, None, :] == slot_ids[None, None, :, None])
    select_gate = jnp.where(select, gate_t[:, :, None, :], 0.0).astype(bf16)
    grad_rows = jnp.einsum(
        "blct,btd->blcd", select.astype(bf16), grad_all, preferred_element_type=f32
    ).astype(bf16)
    scaled = jnp.einsum(
        "blct,btd->blcd", select_gate, grad_all, preferred_element_type=f32
    ).astype(bf16)

    hidden_all = jnp.concatenate([hidden, far, near, near_far], axis=1)
    hidden_all = hidden_all.transpose(0, 2, 1, 3, 4).reshape(local_count, block_count, capacity, hidden_width)
    hidden_all = jnp.pad(hidden_all, ((0, 0), (0, 0), (0, padded - capacity), (0, 0)))
    weight_grad, slot_part = expert_kernel(hidden_all, scaled, grad_rows, down_weight)
    slot_part = slot_part.reshape(local_count, block_count, padded)[:, :, :capacity]
    slot_part = slot_part.transpose(1, 0, 2).reshape(peer_count, shards, local_count, capacity)
    piece_of = jnp.array([0, 2, 1, 3], jnp.int32)[jnp.arange(shards, dtype=jnp.int32) ^ my_dp]
    slot_part = jnp.take(slot_part, piece_of, axis=1)
    send_back = slot_part.reshape(block_count, local_count, capacity)
    returned = lax.all_to_all(
        send_back, ("expert", "dp"), split_axis=0, concat_axis=0, tiled=True
    )
    returned = returned.reshape(peer_count, shards, local_count, capacity)
    slot_grad = jnp.sum(returned, axis=1).reshape(expert_count, capacity)

    own_hit = expert_ids[:, :, None] == jnp.arange(expert_count, dtype=jnp.int32)[None, None, :]
    own_chose = jnp.any(own_hit, axis=1)
    own_rank = jnp.einsum(
        "ue,ut->te", own_chose.astype(bf16), before, preferred_element_type=f32
    ).astype(jnp.int32)
    own_slot = jnp.sum(jnp.where(own_hit, own_rank[:, None, :], 0), axis=2)
    by_slot = jnp.sum(jnp.where(own_hit[:, :, :, None], slot_grad[None, None], 0.0), axis=2)
    gate_grad = jnp.sum(
        jnp.where(own_slot[:, :, None] == slot_ids[None, None, :capacity], by_slot, 0.0), axis=2
    )
    return (weight_grad, gate_grad)


def solution(mesh):
    return jax.shard_map(
        per_device,
        mesh=mesh,
        in_specs=(
            P(("groups", "expert", "dp"), None),
            P(("groups", "expert", "dp"), None),
            P(("groups", "expert", "dp"), None),
            P("expert", ("groups", "dp"), None, None, None),
            P("expert", None, "dp"),
        ),
        out_specs=(P(("groups", "expert"), None, "dp"), P(("groups", "expert", "dp"), None)),
        check_vma=False,
    )
```

```python
import jax
import jax.numpy as jnp
from jax import lax
from jax.experimental import pallas as pl
from jax.sharding import PartitionSpec as P


def expert_body(h_ref, s_ref, g_ref, w_ref, wg_ref, slot_ref):
    chunk = pl.program_id(1)
    blocks, slots, hidden_width = h_ref.shape[1:]
    col_width = s_ref.shape[3]
    rows = blocks * slots
    h = h_ref[0].reshape(rows, hidden_width)
    part = lax.dot_general(
        h, s_ref[:, 0].reshape(rows, col_width), (((0,), (0,)), ((), ())),
        preferred_element_type=jnp.float32,
    )

    @pl.when(chunk == 0)
    def _():
        wg_ref[0] = part

    @pl.when(chunk != 0)
    def _():
        wg_ref[0] = wg_ref[0] + part

    out = jnp.dot(h, w_ref[0], preferred_element_type=jnp.float32)
    g = g_ref[:, 0].reshape(rows, col_width).astype(jnp.float32)
    slot_ref[0] = jnp.sum(g * out, axis=1, keepdims=True)


def expert_kernel(hidden_rows, scaled_rows, grad_rows, weight):
    local_count, block_count, slots, hidden_width = hidden_rows.shape
    col_width = scaled_rows.shape[3]
    chunk = block_count
    for size in (16, 8, 4, 2, 1):
        if block_count % size == 0:
            chunk = size
            break
    steps = block_count // chunk
    rows = chunk * slots
    return pl.pallas_call(
        expert_body,
        grid=(local_count, steps),
        in_specs=[
            pl.BlockSpec((1, chunk, slots, hidden_width), lambda l, r: (l, r, 0, 0)),
            pl.BlockSpec((chunk, 1, slots, col_width), lambda l, r: (r, l, 0, 0)),
            pl.BlockSpec((chunk, 1, slots, col_width), lambda l, r: (r, l, 0, 0)),
            pl.BlockSpec((1, hidden_width, col_width), lambda l, r: (l, 0, 0)),
        ],
        out_specs=[
            pl.BlockSpec((1, hidden_width, col_width), lambda l, r: (l, 0, 0)),
            pl.BlockSpec((1, rows, 1), lambda l, r: (l, r, 0)),
        ],
        out_shape=[
            jax.ShapeDtypeStruct((local_count, hidden_width, col_width), jnp.float32),
            jax.ShapeDtypeStruct((local_count, block_count * slots, 1), jnp.float32),
        ],
    )(hidden_rows, scaled_rows, grad_rows, weight)


def per_device(out_grad, gate_weights, expert_ids, hidden, down_weight):
    tok_rows, top_count = expert_ids.shape
    row_width = out_grad.shape[1]
    local_count = hidden.shape[0]
    capacity = hidden.shape[3]
    hidden_width = hidden.shape[4]
    peer_count = lax.axis_size("expert")
    shards = lax.axis_size("dp")
    expert_count = local_count * peer_count
    col_width = row_width // shards
    block_count = peer_count * shards
    f32 = jnp.float32
    bf16 = jnp.bfloat16
    my_dp = lax.axis_index("dp")

    meta = jnp.concatenate([expert_ids.astype(bf16), gate_weights], axis=1).reshape(-1)
    meta_len = meta.shape[0]
    meta_rows = -(-meta_len // col_width)
    meta = jnp.pad(meta, (0, meta_rows * col_width - meta_len)).reshape(meta_rows, 1, col_width)
    cols = out_grad.reshape(tok_rows, shards, col_width)
    cols = jnp.concatenate([cols, jnp.broadcast_to(meta, (meta_rows, shards, col_width))], axis=0)
    cols = lax.all_to_all(cols, "dp", split_axis=1, concat_axis=0, tiled=True)
    cols = cols.reshape(shards, tok_rows + meta_rows, col_width)
    piece_xor = jnp.array([0, 2, 1, 3], jnp.int32)
    cols = jnp.take(cols, piece_xor ^ my_dp, axis=0)

    hidden_sent, cols = lax.optimization_barrier((hidden, cols))
    near = lax.ppermute(hidden_sent, "dp", [(j, j ^ 1) for j in range(shards)])
    far = lax.ppermute(hidden_sent, "dp", [(j, j ^ 2) for j in range(shards)])
    near_far = lax.ppermute(far, "dp", [(j, j ^ 1) for j in range(shards)])
    got = lax.all_gather(cols, "expert", axis=0, tiled=False)
    got = got.reshape(block_count, tok_rows + meta_rows, col_width)
    grad_all = got[:, :tok_rows]
    meta_all = got[:, tok_rows:].reshape(block_count, meta_rows * col_width)[:, :meta_len]
    meta_all = meta_all.reshape(block_count, tok_rows, 2 * top_count)
    ids_all = meta_all[:, :, :top_count].astype(jnp.int32)
    gate_all = meta_all[:, :, top_count:]

    my_experts = lax.axis_index("expert") * local_count + jnp.arange(local_count, dtype=jnp.int32)
    hit = ids_all[:, :, :, None] == my_experts[None, None, None, :]
    chose = jnp.any(hit, axis=2)
    gate_hit = jnp.sum(jnp.where(hit, gate_all.astype(f32)[:, :, :, None], 0.0), axis=2)
    before = (jnp.arange(tok_rows)[:, None] < jnp.arange(tok_rows)[None, :]).astype(bf16)
    rank = jnp.einsum(
        "bul,ut->btl", chose.astype(bf16), before, preferred_element_type=f32
    ).astype(jnp.int32)
    padded = -(-capacity // 8) * 8
    slot_ids = jnp.arange(padded, dtype=jnp.int32)
    chose_t = chose.transpose(0, 2, 1)
    rank_t = rank.transpose(0, 2, 1)
    gate_t = gate_hit.transpose(0, 2, 1)
    select = chose_t[:, :, None, :] & (rank_t[:, :, None, :] == slot_ids[None, None, :, None])
    select_gate = jnp.where(select, gate_t[:, :, None, :], 0.0).astype(bf16)
    grad_rows = jnp.einsum(
        "blct,btd->blcd", select.astype(bf16), grad_all, preferred_element_type=f32
    ).astype(bf16)
    scaled = jnp.einsum(
        "blct,btd->blcd", select_gate, grad_all, preferred_element_type=f32
    ).astype(bf16)

    hidden_all = jnp.stack([p[:, 0] for p in (hidden, far, near, near_far)], axis=2)
    hidden_all = jnp.pad(hidden_all, ((0, 0), (0, 0), (0, 0), (0, padded - capacity), (0, 0)))
    hidden_all = hidden_all.reshape(local_count, block_count, padded, hidden_width)
    weight_grad, slot_part = expert_kernel(hidden_all, scaled, grad_rows, down_weight)
    slot_part = slot_part.reshape(local_count, block_count, padded)[:, :, :capacity]
    slot_part = slot_part.transpose(1, 0, 2).reshape(peer_count, shards, local_count, capacity)
    piece_of = jnp.array([0, 2, 1, 3], jnp.int32)[jnp.arange(shards, dtype=jnp.int32) ^ my_dp]
    slot_part = jnp.take(slot_part, piece_of, axis=1)
    send_back = slot_part.reshape(block_count, local_count, capacity)
    returned = lax.all_to_all(
        send_back, ("expert", "dp"), split_axis=0, concat_axis=0, tiled=True
    )
    returned = returned.reshape(peer_count, shards, local_count, capacity)
    slot_grad = jnp.sum(returned, axis=1).reshape(expert_count, capacity)

    own_hit = expert_ids[:, :, None] == jnp.arange(expert_count, dtype=jnp.int32)[None, None, :]
    own_chose = jnp.any(own_hit, axis=1)
    own_rank = jnp.einsum(
        "ue,ut->te", own_chose.astype(bf16), before, preferred_element_type=f32
    ).astype(jnp.int32)
    own_slot = jnp.sum(jnp.where(own_hit, own_rank[:, None, :], 0), axis=2)
    by_slot = jnp.sum(jnp.where(own_hit[:, :, :, None], slot_grad[None, None], 0.0), axis=2)
    gate_grad = jnp.sum(
        jnp.where(own_slot[:, :, None] == slot_ids[None, None, :capacity], by_slot, 0.0), axis=2
    )
    return (weight_grad, gate_grad)


def solution(mesh):
    return jax.shard_map(
        per_device,
        mesh=mesh,
        in_specs=(
            P(("groups", "expert", "dp"), None),
            P(("groups", "expert", "dp"), None),
            P(("groups", "expert", "dp"), None),
            P("expert", ("groups", "dp"), None, None, None),
            P("expert", None, "dp"),
        ),
        out_specs=(P(("groups", "expert"), None, "dp"), P(("groups", "expert", "dp"), None)),
        check_vma=False,
    )
```

```python
import jax
import jax.numpy as jnp
from jax import lax
from jax.experimental import pallas as pl
from jax.experimental.pallas import tpu as pltpu
from jax.sharding import PartitionSpec as P


def expert_body(own_ref, far_ref, near_ref, near_far_ref, s_ref, g_ref, w_ref, wg_ref, slot_ref, h_scr):
    expert = pl.program_id(0)
    chunk = pl.program_id(1)
    sources, capacity, hidden_width = own_ref.shape[2:]
    blocks, padded = s_ref.shape[0], s_ref.shape[2]
    col_width = s_ref.shape[3]
    rows = blocks * padded
    pieces = (own_ref, far_ref, near_ref, near_far_ref)

    @pl.when((expert == 0) & (chunk == 0))
    def _():
        h_scr[...] = jnp.zeros(h_scr.shape, h_scr.dtype)

    for src in range(sources):
        for j, ref in enumerate(pieces):
            row = (src * len(pieces) + j) * padded
            h_scr[row:row + capacity, :] = ref[0, 0, src]

    h = h_scr[...]
    part = lax.dot_general(
        h, s_ref[:, 0].reshape(rows, col_width), (((0,), (0,)), ((), ())),
        preferred_element_type=jnp.float32,
    )

    @pl.when(chunk == 0)
    def _():
        wg_ref[0] = part

    @pl.when(chunk != 0)
    def _():
        wg_ref[0] = wg_ref[0] + part

    out = jnp.dot(h, w_ref[0], preferred_element_type=jnp.float32)
    g = g_ref[:, 0].reshape(rows, col_width).astype(jnp.float32)
    slot_ref[0] = jnp.sum(g * out, axis=1, keepdims=True)


def expert_kernel(pieces, scaled_rows, grad_rows, weight):
    local_count, _, source_count, capacity, hidden_width = pieces[0].shape
    block_count, _, padded, col_width = scaled_rows.shape
    per_source = block_count // source_count
    chunk = source_count
    for size in (4, 2, 1):
        if source_count % size == 0:
            chunk = size
            break
    steps = source_count // chunk
    rows = chunk * per_source * padded
    piece_spec = pl.BlockSpec(
        (1, 1, chunk, capacity, hidden_width), lambda l, r: (l, 0, r, 0, 0)
    )
    row_spec = pl.BlockSpec(
        (chunk * per_source, 1, padded, col_width), lambda l, r: (r, l, 0, 0)
    )
    return pl.pallas_call(
        expert_body,
        grid=(local_count, steps),
        in_specs=[piece_spec] * len(pieces) + [
            row_spec,
            row_spec,
            pl.BlockSpec((1, hidden_width, col_width), lambda l, r: (l, 0, 0)),
        ],
        out_specs=[
            pl.BlockSpec((1, hidden_width, col_width), lambda l, r: (l, 0, 0)),
            pl.BlockSpec((1, rows, 1), lambda l, r: (l, r, 0)),
        ],
        out_shape=[
            jax.ShapeDtypeStruct((local_count, hidden_width, col_width), jnp.float32),
            jax.ShapeDtypeStruct((local_count, block_count * padded, 1), jnp.float32),
        ],
        scratch_shapes=[pltpu.VMEM((rows, hidden_width), jnp.bfloat16)],
    )(*pieces, scaled_rows, grad_rows, weight)


def per_device(out_grad, gate_weights, expert_ids, hidden, down_weight):
    tok_rows, top_count = expert_ids.shape
    row_width = out_grad.shape[1]
    local_count = hidden.shape[0]
    capacity = hidden.shape[3]
    hidden_width = hidden.shape[4]
    peer_count = lax.axis_size("expert")
    shards = lax.axis_size("dp")
    expert_count = local_count * peer_count
    col_width = row_width // shards
    block_count = peer_count * shards
    f32 = jnp.float32
    bf16 = jnp.bfloat16
    my_dp = lax.axis_index("dp")

    meta = jnp.concatenate([expert_ids.astype(bf16), gate_weights], axis=1).reshape(-1)
    meta_len = meta.shape[0]
    meta_rows = -(-meta_len // col_width)
    meta = jnp.pad(meta, (0, meta_rows * col_width - meta_len)).reshape(meta_rows, 1, col_width)
    cols = out_grad.reshape(tok_rows, shards, col_width)
    cols = jnp.concatenate([cols, jnp.broadcast_to(meta, (meta_rows, shards, col_width))], axis=0)
    cols = lax.all_to_all(cols, "dp", split_axis=1, concat_axis=0, tiled=True)
    cols = cols.reshape(shards, tok_rows + meta_rows, col_width)
    piece_xor = jnp.array([0, 2, 1, 3], jnp.int32)
    cols = jnp.take(cols, piece_xor ^ my_dp, axis=0)

    hidden_sent, cols = lax.optimization_barrier((hidden, cols))
    near = lax.ppermute(hidden_sent, "dp", [(j, j ^ 1) for j in range(shards)])
    far = lax.ppermute(hidden_sent, "dp", [(j, j ^ 2) for j in range(shards)])
    near_far = lax.ppermute(far, "dp", [(j, j ^ 1) for j in range(shards)])
    got = lax.all_gather(cols, "expert", axis=0, tiled=False)
    got = got.reshape(block_count, tok_rows + meta_rows, col_width)
    grad_all = got[:, :tok_rows]
    meta_all = got[:, tok_rows:].reshape(block_count, meta_rows * col_width)[:, :meta_len]
    meta_all = meta_all.reshape(block_count, tok_rows, 2 * top_count)
    ids_all = meta_all[:, :, :top_count].astype(jnp.int32)
    gate_all = meta_all[:, :, top_count:]

    my_experts = lax.axis_index("expert") * local_count + jnp.arange(local_count, dtype=jnp.int32)
    hit = ids_all[:, :, :, None] == my_experts[None, None, None, :]
    chose = jnp.any(hit, axis=2)
    gate_hit = jnp.sum(jnp.where(hit, gate_all.astype(f32)[:, :, :, None], 0.0), axis=2)
    before = (jnp.arange(tok_rows)[:, None] < jnp.arange(tok_rows)[None, :]).astype(bf16)
    rank = jnp.einsum(
        "bul,ut->btl", chose.astype(bf16), before, preferred_element_type=f32
    ).astype(jnp.int32)
    padded = -(-capacity // 16) * 16
    slot_ids = jnp.arange(padded, dtype=jnp.int32)
    chose_t = chose.transpose(0, 2, 1)
    rank_t = rank.transpose(0, 2, 1)
    gate_t = gate_hit.transpose(0, 2, 1)
    select = chose_t[:, :, None, :] & (rank_t[:, :, None, :] == slot_ids[None, None, :, None])
    select_gate = jnp.where(select, gate_t[:, :, None, :], 0.0).astype(bf16)
    grad_rows = jnp.einsum(
        "blct,btd->blcd", select.astype(bf16), grad_all, preferred_element_type=f32
    ).astype(bf16)
    scaled = jnp.einsum(
        "blct,btd->blcd", select_gate, grad_all, preferred_element_type=f32
    ).astype(bf16)

    weight_grad, slot_part = expert_kernel((hidden, far, near, near_far), scaled, grad_rows, down_weight)
    slot_part = slot_part.reshape(local_count, block_count, padded)[:, :, :capacity]
    slot_part = slot_part.transpose(1, 0, 2).reshape(peer_count, shards, local_count, capacity)
    piece_of = jnp.array([0, 2, 1, 3], jnp.int32)[jnp.arange(shards, dtype=jnp.int32) ^ my_dp]
    slot_part = jnp.take(slot_part, piece_of, axis=1)
    send_back = slot_part.reshape(block_count, local_count, capacity)
    returned = lax.all_to_all(
        send_back, ("expert", "dp"), split_axis=0, concat_axis=0, tiled=True
    )
    returned = returned.reshape(peer_count, shards, local_count, capacity)
    slot_grad = jnp.sum(returned, axis=1).reshape(expert_count, capacity)

    own_hit = expert_ids[:, :, None] == jnp.arange(expert_count, dtype=jnp.int32)[None, None, :]
    own_chose = jnp.any(own_hit, axis=1)
    own_rank = jnp.einsum(
        "ue,ut->te", own_chose.astype(bf16), before, preferred_element_type=f32
    ).astype(jnp.int32)
    own_slot = jnp.sum(jnp.where(own_hit, own_rank[:, None, :], 0), axis=2)
    by_slot = jnp.sum(jnp.where(own_hit[:, :, :, None], slot_grad[None, None], 0.0), axis=2)
    gate_grad = jnp.sum(
        jnp.where(own_slot[:, :, None] == slot_ids[None, None, :capacity], by_slot, 0.0), axis=2
    )
    return (weight_grad, gate_grad)


def solution(mesh):
    return jax.shard_map(
        per_device,
        mesh=mesh,
        in_specs=(
            P(("groups", "expert", "dp"), None),
            P(("groups", "expert", "dp"), None),
            P(("groups", "expert", "dp"), None),
            P("expert", ("groups", "dp"), None, None, None),
            P("expert", None, "dp"),
        ),
        out_specs=(P(("groups", "expert"), None, "dp"), P(("groups", "expert", "dp"), None)),
        check_vma=False,
    )
```

```python
import jax
import jax.numpy as jnp
from jax import lax
from jax.experimental import pallas as pl
from jax.experimental.pallas import tpu as pltpu
from jax.sharding import PartitionSpec as P


def expert_body(own_ref, far_ref, near_ref, near_far_ref, tok_ref, sel_ref, gate_ref, w_ref,
                wg_ref, slot_ref, h_scr, s_scr, g_scr):
    expert = pl.program_id(0)
    chunk = pl.program_id(1)
    sources, capacity, hidden_width = own_ref.shape[2:]
    blocks, _, padded, _ = sel_ref.shape
    col_width = tok_ref.shape[2]
    pieces = (own_ref, far_ref, near_ref, near_far_ref)

    @pl.when((expert == 0) & (chunk == 0))
    def _():
        h_scr[...] = jnp.zeros(h_scr.shape, h_scr.dtype)

    for src in range(sources):
        for j, ref in enumerate(pieces):
            row = (src * len(pieces) + j) * padded
            h_scr[row:row + capacity, :] = ref[0, 0, src]

    for blk in range(blocks):
        rows = jnp.dot(sel_ref[blk, 0], tok_ref[blk], preferred_element_type=jnp.float32)
        g_scr[blk * padded:(blk + 1) * padded, :] = rows.astype(jnp.bfloat16)
        s_scr[blk * padded:(blk + 1) * padded, :] = (gate_ref[blk, 0] * rows).astype(jnp.bfloat16)

    h = h_scr[...]
    part = lax.dot_general(
        h, s_scr[...], (((0,), (0,)), ((), ())), preferred_element_type=jnp.float32
    )

    @pl.when(chunk == 0)
    def _():
        wg_ref[0] = part

    @pl.when(chunk != 0)
    def _():
        wg_ref[0] = wg_ref[0] + part

    out = jnp.dot(h, w_ref[0], preferred_element_type=jnp.float32)
    slot_ref[0] = jnp.sum(g_scr[...].astype(jnp.float32) * out, axis=1, keepdims=True)


def expert_kernel(pieces, tokens, select, gate_slot, weight):
    local_count, _, source_count, capacity, hidden_width = pieces[0].shape
    block_count, tok_rows, col_width = tokens.shape
    padded = select.shape[2]
    per_source = block_count // source_count
    chunk = source_count
    for size in (4, 2, 1):
        if source_count % size == 0:
            chunk = size
            break
    steps = source_count // chunk
    blocks = chunk * per_source
    rows = blocks * padded
    piece_spec = pl.BlockSpec(
        (1, 1, chunk, capacity, hidden_width), lambda l, r: (l, 0, r, 0, 0)
    )
    return pl.pallas_call(
        expert_body,
        grid=(local_count, steps),
        in_specs=[piece_spec] * len(pieces) + [
            pl.BlockSpec((blocks, tok_rows, col_width), lambda l, r: (r, 0, 0)),
            pl.BlockSpec((blocks, 1, padded, tok_rows), lambda l, r: (r, l, 0, 0)),
            pl.BlockSpec((blocks, 1, padded, 1), lambda l, r: (r, l, 0, 0)),
            pl.BlockSpec((1, hidden_width, col_width), lambda l, r: (l, 0, 0)),
        ],
        out_specs=[
            pl.BlockSpec((1, hidden_width, col_width), lambda l, r: (l, 0, 0)),
            pl.BlockSpec((1, rows, 1), lambda l, r: (l, r, 0)),
        ],
        out_shape=[
            jax.ShapeDtypeStruct((local_count, hidden_width, col_width), jnp.float32),
            jax.ShapeDtypeStruct((local_count, block_count * padded, 1), jnp.float32),
        ],
        scratch_shapes=[
            pltpu.VMEM((rows, hidden_width), jnp.bfloat16),
            pltpu.VMEM((rows, col_width), jnp.bfloat16),
            pltpu.VMEM((rows, col_width), jnp.bfloat16),
        ],
    )(*pieces, tokens, select, gate_slot, weight)


def per_device(out_grad, gate_weights, expert_ids, hidden, down_weight):
    tok_rows, top_count = expert_ids.shape
    row_width = out_grad.shape[1]
    local_count = hidden.shape[0]
    capacity = hidden.shape[3]
    hidden_width = hidden.shape[4]
    peer_count = lax.axis_size("expert")
    shards = lax.axis_size("dp")
    expert_count = local_count * peer_count
    col_width = row_width // shards
    block_count = peer_count * shards
    f32 = jnp.float32
    bf16 = jnp.bfloat16
    my_dp = lax.axis_index("dp")

    meta = jnp.concatenate([expert_ids.astype(bf16), gate_weights], axis=1).reshape(-1)
    meta_len = meta.shape[0]
    meta_rows = -(-meta_len // col_width)
    meta = jnp.pad(meta, (0, meta_rows * col_width - meta_len)).reshape(meta_rows, 1, col_width)
    cols = out_grad.reshape(tok_rows, shards, col_width)
    cols = jnp.concatenate([cols, jnp.broadcast_to(meta, (meta_rows, shards, col_width))], axis=0)
    cols = lax.all_to_all(cols, "dp", split_axis=1, concat_axis=0, tiled=True)
    cols = cols.reshape(shards, tok_rows + meta_rows, col_width)
    piece_xor = jnp.array([0, 2, 1, 3], jnp.int32)
    cols = jnp.take(cols, piece_xor ^ my_dp, axis=0)

    hidden_sent, cols = lax.optimization_barrier((hidden, cols))
    near = lax.ppermute(hidden_sent, "dp", [(j, j ^ 1) for j in range(shards)])
    far = lax.ppermute(hidden_sent, "dp", [(j, j ^ 2) for j in range(shards)])
    near_far = lax.ppermute(far, "dp", [(j, j ^ 1) for j in range(shards)])
    got = lax.all_gather(cols, "expert", axis=0, tiled=False)
    got = got.reshape(block_count, tok_rows + meta_rows, col_width)
    grad_all = got[:, :tok_rows]
    meta_all = got[:, tok_rows:].reshape(block_count, meta_rows * col_width)[:, :meta_len]
    meta_all = meta_all.reshape(block_count, tok_rows, 2 * top_count)
    ids_all = meta_all[:, :, :top_count].astype(jnp.int32)
    gate_all = meta_all[:, :, top_count:]

    my_experts = lax.axis_index("expert") * local_count + jnp.arange(local_count, dtype=jnp.int32)
    hit = ids_all[:, :, :, None] == my_experts[None, None, None, :]
    chose = jnp.any(hit, axis=2)
    gate_hit = jnp.sum(jnp.where(hit, gate_all.astype(f32)[:, :, :, None], 0.0), axis=2)
    before = (jnp.arange(tok_rows)[:, None] < jnp.arange(tok_rows)[None, :]).astype(bf16)
    rank = jnp.einsum(
        "bul,ut->btl", chose.astype(bf16), before, preferred_element_type=f32
    ).astype(jnp.int32)
    padded = -(-capacity // 16) * 16
    slot_ids = jnp.arange(padded, dtype=jnp.int32)
    chose_t = chose.transpose(0, 2, 1)
    rank_t = rank.transpose(0, 2, 1)
    gate_t = gate_hit.transpose(0, 2, 1)
    select = chose_t[:, :, None, :] & (rank_t[:, :, None, :] == slot_ids[None, None, :, None])
    gate_slot = jnp.sum(jnp.where(select, gate_t[:, :, None, :], 0.0), axis=3, keepdims=True)
    weight_grad, slot_part = expert_kernel(
        (hidden, far, near, near_far), grad_all, select.astype(bf16), gate_slot, down_weight
    )
    slot_part = slot_part.reshape(local_count, block_count, padded)[:, :, :capacity]
    slot_part = slot_part.transpose(1, 0, 2).reshape(peer_count, shards, local_count, capacity)
    piece_of = jnp.array([0, 2, 1, 3], jnp.int32)[jnp.arange(shards, dtype=jnp.int32) ^ my_dp]
    slot_part = jnp.take(slot_part, piece_of, axis=1)
    send_back = slot_part.reshape(block_count, local_count, capacity)
    returned = lax.all_to_all(
        send_back, ("expert", "dp"), split_axis=0, concat_axis=0, tiled=True
    )
    returned = returned.reshape(peer_count, shards, local_count, capacity)
    slot_grad = jnp.sum(returned, axis=1).reshape(expert_count, capacity)

    own_hit = expert_ids[:, :, None] == jnp.arange(expert_count, dtype=jnp.int32)[None, None, :]
    own_chose = jnp.any(own_hit, axis=1)
    own_rank = jnp.einsum(
        "ue,ut->te", own_chose.astype(bf16), before, preferred_element_type=f32
    ).astype(jnp.int32)
    own_slot = jnp.sum(jnp.where(own_hit, own_rank[:, None, :], 0), axis=2)
    by_slot = jnp.sum(jnp.where(own_hit[:, :, :, None], slot_grad[None, None], 0.0), axis=2)
    gate_grad = jnp.sum(
        jnp.where(own_slot[:, :, None] == slot_ids[None, None, :capacity], by_slot, 0.0), axis=2
    )
    return (weight_grad, gate_grad)


def solution(mesh):
    return jax.shard_map(
        per_device,
        mesh=mesh,
        in_specs=(
            P(("groups", "expert", "dp"), None),
            P(("groups", "expert", "dp"), None),
            P(("groups", "expert", "dp"), None),
            P("expert", ("groups", "dp"), None, None, None),
            P("expert", None, "dp"),
        ),
        out_specs=(P(("groups", "expert"), None, "dp"), P(("groups", "expert", "dp"), None)),
        check_vma=False,
    )
```

```python
import jax
import jax.numpy as jnp
from jax import lax
from jax.experimental import pallas as pl
from jax.experimental.pallas import tpu as pltpu
from jax.sharding import PartitionSpec as P


def expert_body(own_ref, far_ref, near_ref, near_far_ref, mine_ref, rest_ref, sel_ref, gate_ref, w_ref,
                wg_ref, slot_ref, h_scr, s_scr, g_scr):
    expert = pl.program_id(0)
    chunk = pl.program_id(1)
    sources, capacity, hidden_width = own_ref.shape[2:]
    blocks, _, padded, _ = sel_ref.shape
    col_width = mine_ref.shape[2]
    pieces = (own_ref, far_ref, near_ref, near_far_ref)

    @pl.when((expert == 0) & (chunk == 0))
    def _():
        h_scr[...] = jnp.zeros(h_scr.shape, h_scr.dtype)

    for src in range(sources):
        for j, ref in enumerate(pieces):
            row = (src * len(pieces) + j) * padded
            h_scr[row:row + capacity, :] = ref[0, 0, src]

    for blk in range(blocks):
        src, j = divmod(blk, len(pieces))
        tok = mine_ref[src] if j == 0 else rest_ref[src, j - 1]
        rows = jnp.dot(sel_ref[blk, 0], tok, preferred_element_type=jnp.float32)
        g_scr[blk * padded:(blk + 1) * padded, :] = rows.astype(jnp.bfloat16)
        s_scr[blk * padded:(blk + 1) * padded, :] = (gate_ref[blk, 0] * rows).astype(jnp.bfloat16)

    h = h_scr[...]
    part = lax.dot_general(
        h, s_scr[...], (((0,), (0,)), ((), ())), preferred_element_type=jnp.float32
    )

    @pl.when(chunk == 0)
    def _():
        wg_ref[0] = part

    @pl.when(chunk != 0)
    def _():
        wg_ref[0] = wg_ref[0] + part

    out = jnp.dot(h, w_ref[0], preferred_element_type=jnp.float32)
    prod = g_scr[...].astype(jnp.float32) * out
    ones = jnp.ones((8, col_width), jnp.float32)
    sums = lax.dot_general(
        ones, prod, (((1,), (1,)), ((), ())),
        precision=lax.Precision.HIGHEST, preferred_element_type=jnp.float32,
    )
    slot_ref[0] = sums[0:1]


def expert_kernel(pieces, mine, rest, select, gate_slot, weight):
    local_count, _, source_count, capacity, hidden_width = pieces[0].shape
    col_width = mine.shape[2]
    block_count, _, padded, tok_rows = select.shape
    per_source = block_count // source_count
    chunk = source_count
    for size in (4, 2, 1):
        if source_count % size == 0:
            chunk = size
            break
    steps = source_count // chunk
    blocks = chunk * per_source
    rows = blocks * padded
    piece_spec = pl.BlockSpec(
        (1, 1, chunk, capacity, hidden_width), lambda l, r: (l, 0, r, 0, 0)
    )
    return pl.pallas_call(
        expert_body,
        grid=(local_count, steps),
        in_specs=[piece_spec] * len(pieces) + [
            pl.BlockSpec((chunk, tok_rows, col_width), lambda l, r: (r, 0, 0)),
            pl.BlockSpec((chunk, per_source - 1, tok_rows, col_width), lambda l, r: (r, 0, 0, 0)),
            pl.BlockSpec((blocks, 1, padded, tok_rows), lambda l, r: (r, l, 0, 0)),
            pl.BlockSpec((blocks, 1, padded, 1), lambda l, r: (r, l, 0, 0)),
            pl.BlockSpec((1, hidden_width, col_width), lambda l, r: (l, 0, 0)),
        ],
        out_specs=[
            pl.BlockSpec((1, hidden_width, col_width), lambda l, r: (l, 0, 0)),
            pl.BlockSpec((1, 1, rows), lambda l, r: (l, 0, r)),
        ],
        out_shape=[
            jax.ShapeDtypeStruct((local_count, hidden_width, col_width), jnp.float32),
            jax.ShapeDtypeStruct((local_count, 1, block_count * padded), jnp.float32),
        ],
        scratch_shapes=[
            pltpu.VMEM((rows, hidden_width), jnp.bfloat16),
            pltpu.VMEM((rows, col_width), jnp.bfloat16),
            pltpu.VMEM((rows, col_width), jnp.bfloat16),
        ],
    )(*pieces, mine, rest, select, gate_slot, weight)


def per_device(out_grad, gate_weights, expert_ids, hidden, down_weight):
    tok_rows, top_count = expert_ids.shape
    row_width = out_grad.shape[1]
    local_count = hidden.shape[0]
    capacity = hidden.shape[3]
    hidden_width = hidden.shape[4]
    peer_count = lax.axis_size("expert")
    shards = lax.axis_size("dp")
    expert_count = local_count * peer_count
    col_width = row_width // shards
    block_count = peer_count * shards
    f32 = jnp.float32
    bf16 = jnp.bfloat16
    my_dp = lax.axis_index("dp")

    meta = jnp.concatenate([expert_ids.astype(bf16), gate_weights], axis=1).reshape(-1)
    meta_len = meta.shape[0]
    meta_rows = -(-meta_len // col_width)
    meta = jnp.pad(meta, (0, meta_rows * col_width - meta_len)).reshape(meta_rows, 1, col_width)
    cols = out_grad.reshape(tok_rows, shards, col_width)
    cols = jnp.concatenate([cols, jnp.broadcast_to(meta, (meta_rows, shards, col_width))], axis=0)
    mine = lax.dynamic_index_in_dim(cols, my_dp, axis=1, keepdims=False)
    mine_all = lax.all_gather(mine, "expert", axis=0, tiled=False)
    cols = lax.all_to_all(cols, "dp", split_axis=1, concat_axis=0, tiled=True)
    cols = cols.reshape(shards, tok_rows + meta_rows, col_width)
    piece_xor = jnp.array([2, 1, 3], jnp.int32)
    cols = jnp.take(cols, piece_xor ^ my_dp, axis=0)

    hidden_sent, cols = lax.optimization_barrier((hidden, cols))
    near = lax.ppermute(hidden_sent, "dp", [(j, j ^ 1) for j in range(shards)])
    far = lax.ppermute(hidden_sent, "dp", [(j, j ^ 2) for j in range(shards)])
    near_far = lax.ppermute(far, "dp", [(j, j ^ 1) for j in range(shards)])
    rest_all = lax.all_gather(cols, "expert", axis=0, tiled=False)
    meta_all = jnp.concatenate([mine_all[:, None, tok_rows:], rest_all[:, :, tok_rows:]], axis=1)
    meta_all = meta_all.reshape(block_count, meta_rows * col_width)[:, :meta_len]
    meta_all = meta_all.reshape(block_count, tok_rows, 2 * top_count)
    ids_all = meta_all[:, :, :top_count].astype(jnp.int32)
    gate_all = meta_all[:, :, top_count:]

    my_experts = lax.axis_index("expert") * local_count + jnp.arange(local_count, dtype=jnp.int32)
    hit = ids_all[:, :, :, None] == my_experts[None, None, None, :]
    chose = jnp.any(hit, axis=2)
    gate_hit = jnp.sum(jnp.where(hit, gate_all.astype(f32)[:, :, :, None], 0.0), axis=2)
    before = (jnp.arange(tok_rows)[:, None] < jnp.arange(tok_rows)[None, :]).astype(bf16)
    rank = jnp.einsum(
        "bul,ut->btl", chose.astype(bf16), before, preferred_element_type=f32
    ).astype(jnp.int32)
    padded = -(-capacity // 16) * 16
    slot_ids = jnp.arange(padded, dtype=jnp.int32)
    chose_t = chose.transpose(0, 2, 1)
    rank_t = rank.transpose(0, 2, 1)
    gate_t = gate_hit.transpose(0, 2, 1)
    select = chose_t[:, :, None, :] & (rank_t[:, :, None, :] == slot_ids[None, None, :, None])
    gate_slot = jnp.sum(jnp.where(select, gate_t[:, :, None, :], 0.0), axis=3, keepdims=True)
    weight_grad, slot_part = expert_kernel(
        (hidden, far, near, near_far), mine_all, rest_all, select.astype(bf16), gate_slot, down_weight
    )
    slot_part = slot_part.reshape(local_count, block_count, padded)[:, :, :capacity]
    slot_part = slot_part.transpose(1, 0, 2).reshape(peer_count, shards, local_count, capacity)
    piece_of = jnp.array([0, 2, 1, 3], jnp.int32)[jnp.arange(shards, dtype=jnp.int32) ^ my_dp]
    slot_part = jnp.take(slot_part, piece_of, axis=1)
    send_back = slot_part.reshape(block_count, local_count, capacity)
    returned = lax.all_to_all(
        send_back, ("expert", "dp"), split_axis=0, concat_axis=0, tiled=True
    )
    returned = returned.reshape(peer_count, shards, local_count, capacity)
    slot_grad = jnp.sum(returned, axis=1).reshape(expert_count, capacity)

    own_hit = expert_ids[:, :, None] == jnp.arange(expert_count, dtype=jnp.int32)[None, None, :]
    own_chose = jnp.any(own_hit, axis=1)
    own_rank = jnp.einsum(
        "ue,ut->te", own_chose.astype(bf16), before, preferred_element_type=f32
    ).astype(jnp.int32)
    own_slot = jnp.sum(jnp.where(own_hit, own_rank[:, None, :], 0), axis=2)
    by_slot = jnp.sum(jnp.where(own_hit[:, :, :, None], slot_grad[None, None], 0.0), axis=2)
    gate_grad = jnp.sum(
        jnp.where(own_slot[:, :, None] == slot_ids[None, None, :capacity], by_slot, 0.0), axis=2
    )
    return (weight_grad, gate_grad)


def solution(mesh):
    return jax.shard_map(
        per_device,
        mesh=mesh,
        in_specs=(
            P(("groups", "expert", "dp"), None),
            P(("groups", "expert", "dp"), None),
            P(("groups", "expert", "dp"), None),
            P("expert", ("groups", "dp"), None, None, None),
            P("expert", None, "dp"),
        ),
        out_specs=(P(("groups", "expert"), None, "dp"), P(("groups", "expert", "dp"), None)),
        check_vma=False,
    )
```

```python
import jax
import jax.numpy as jnp
from jax import lax
from jax.experimental import pallas as pl
from jax.experimental.pallas import tpu as pltpu
from jax.sharding import PartitionSpec as P


def expert_body(own_ref, far_ref, near_ref, near_far_ref, mine_ref, rest_ref, sel_ref, gate_ref, w_ref,
                wg_ref, slot_ref, h_scr, s_scr, g_scr):
    expert = pl.program_id(0)
    chunk = pl.program_id(1)
    sources, capacity, hidden_width = own_ref.shape[2:]
    blocks, _, padded, _ = sel_ref.shape
    col_width = mine_ref.shape[2]
    pieces = (own_ref, far_ref, near_ref, near_far_ref)

    @pl.when((expert == 0) & (chunk == 0))
    def _():
        h_scr[...] = jnp.zeros(h_scr.shape, h_scr.dtype)

    for src in range(sources):
        for j, ref in enumerate(pieces):
            row = (src * len(pieces) + j) * padded
            h_scr[row:row + capacity, :] = ref[0, 0, src]

    for blk in range(blocks):
        src, j = divmod(blk, len(pieces))
        tok = mine_ref[src] if j == 0 else rest_ref[src, j - 1]
        rows = jnp.dot(sel_ref[blk, 0], tok, preferred_element_type=jnp.float32)
        g_scr[blk * padded:(blk + 1) * padded, :] = rows.astype(jnp.bfloat16)
        s_scr[blk * padded:(blk + 1) * padded, :] = (gate_ref[blk, 0] * rows).astype(jnp.bfloat16)

    h = h_scr[...]
    part = lax.dot_general(
        h, s_scr[...], (((0,), (0,)), ((), ())), preferred_element_type=jnp.float32
    )

    @pl.when(chunk == 0)
    def _():
        wg_ref[0] = part

    @pl.when(chunk != 0)
    def _():
        wg_ref[0] = wg_ref[0] + part

    out = jnp.dot(h, w_ref[0], preferred_element_type=jnp.float32)
    slot_ref[0] = jnp.sum(g_scr[...].astype(jnp.float32) * out, axis=1, keepdims=True)


def expert_kernel(pieces, mine, rest, select, gate_slot, weight):
    local_count, _, source_count, capacity, hidden_width = pieces[0].shape
    col_width = mine.shape[2]
    block_count, _, padded, tok_rows = select.shape
    per_source = block_count // source_count
    chunk = source_count
    for size in (4, 2, 1):
        if source_count % size == 0:
            chunk = size
            break
    steps = source_count // chunk
    blocks = chunk * per_source
    rows = blocks * padded
    piece_spec = pl.BlockSpec(
        (1, 1, chunk, capacity, hidden_width), lambda l, r: (l, 0, r, 0, 0)
    )
    return pl.pallas_call(
        expert_body,
        grid=(local_count, steps),
        in_specs=[piece_spec] * len(pieces) + [
            pl.BlockSpec((chunk, tok_rows, col_width), lambda l, r: (r, 0, 0)),
            pl.BlockSpec((chunk, per_source - 1, tok_rows, col_width), lambda l, r: (r, 0, 0, 0)),
            pl.BlockSpec((blocks, 1, padded, tok_rows), lambda l, r: (r, l, 0, 0)),
            pl.BlockSpec((blocks, 1, padded, 1), lambda l, r: (r, l, 0, 0)),
            pl.BlockSpec((1, hidden_width, col_width), lambda l, r: (l, 0, 0)),
        ],
        out_specs=[
            pl.BlockSpec((1, hidden_width, col_width), lambda l, r: (l, 0, 0)),
            pl.BlockSpec((1, rows, 1), lambda l, r: (l, r, 0)),
        ],
        out_shape=[
            jax.ShapeDtypeStruct((local_count, hidden_width, col_width), jnp.float32),
            jax.ShapeDtypeStruct((local_count, block_count * padded, 1), jnp.float32),
        ],
        scratch_shapes=[
            pltpu.VMEM((rows, hidden_width), jnp.bfloat16),
            pltpu.VMEM((rows, col_width), jnp.bfloat16),
            pltpu.VMEM((rows, col_width), jnp.bfloat16),
        ],
    )(*pieces, mine, rest, select, gate_slot, weight)


def per_device(out_grad, gate_weights, expert_ids, hidden, down_weight):
    tok_rows, top_count = expert_ids.shape
    row_width = out_grad.shape[1]
    local_count = hidden.shape[0]
    capacity = hidden.shape[3]
    hidden_width = hidden.shape[4]
    peer_count = lax.axis_size("expert")
    shards = lax.axis_size("dp")
    expert_count = local_count * peer_count
    col_width = row_width // shards
    block_count = peer_count * shards
    f32 = jnp.float32
    bf16 = jnp.bfloat16
    my_dp = lax.axis_index("dp")

    meta = jnp.concatenate([expert_ids.astype(bf16), gate_weights], axis=1).reshape(-1)
    meta_len = meta.shape[0]
    meta_rows = -(-meta_len // col_width)
    meta = jnp.pad(meta, (0, meta_rows * col_width - meta_len)).reshape(meta_rows, 1, col_width)
    cols = out_grad.reshape(tok_rows, shards, col_width)
    cols = jnp.concatenate([cols, jnp.broadcast_to(meta, (meta_rows, shards, col_width))], axis=0)
    mine = lax.dynamic_slice_in_dim(out_grad, my_dp * col_width, col_width, axis=1)
    mine = jnp.concatenate([mine, meta[:, 0, :]], axis=0)[:, None, :]
    if peer_count <= 8:
        recv = [mine] + [
            lax.ppermute(mine, "expert", [(j, (j + k) % peer_count) for j in range(peer_count)])
            for k in range(1, peer_count)
        ]
        order = (lax.axis_index("expert") - jnp.arange(peer_count, dtype=jnp.int32)) % peer_count
        mine_all = jnp.take(jnp.stack(recv), order, axis=0)
    else:
        mine_all = lax.all_gather(mine, "expert", axis=0, tiled=False)
    mine_all = mine_all.reshape(peer_count, tok_rows + meta_rows, col_width)
    cols, mine_all = lax.optimization_barrier((cols, mine_all))
    cols = lax.all_to_all(cols, "dp", split_axis=1, concat_axis=0, tiled=True)
    cols = cols.reshape(shards, tok_rows + meta_rows, col_width)
    piece_xor = jnp.array([2, 1, 3], jnp.int32)
    cols = jnp.take(cols, piece_xor ^ my_dp, axis=0)

    hidden_sent, cols = lax.optimization_barrier((hidden, cols))
    near = lax.ppermute(hidden_sent, "dp", [(j, j ^ 1) for j in range(shards)])
    far = lax.ppermute(hidden_sent, "dp", [(j, j ^ 2) for j in range(shards)])
    near_far = lax.ppermute(far, "dp", [(j, j ^ 1) for j in range(shards)])
    rest_all = lax.all_gather(cols, "expert", axis=0, tiled=False)
    meta_all = jnp.concatenate([mine_all[:, None, tok_rows:], rest_all[:, :, tok_rows:]], axis=1)
    meta_all = meta_all.reshape(block_count, meta_rows * col_width)[:, :meta_len]
    meta_all = meta_all.reshape(block_count, tok_rows, 2 * top_count)
    ids_all = meta_all[:, :, :top_count].astype(jnp.int32)
    gate_all = meta_all[:, :, top_count:]

    my_experts = lax.axis_index("expert") * local_count + jnp.arange(local_count, dtype=jnp.int32)
    hit = ids_all[:, :, :, None] == my_experts[None, None, None, :]
    chose = jnp.any(hit, axis=2)
    gate_hit = jnp.sum(jnp.where(hit, gate_all.astype(f32)[:, :, :, None], 0.0), axis=2)
    before = (jnp.arange(tok_rows)[:, None] < jnp.arange(tok_rows)[None, :]).astype(bf16)
    rank = jnp.einsum(
        "bul,ut->btl", chose.astype(bf16), before, preferred_element_type=f32
    ).astype(jnp.int32)
    padded = -(-capacity // 16) * 16
    slot_ids = jnp.arange(padded, dtype=jnp.int32)
    chose_t = chose.transpose(0, 2, 1)
    rank_t = rank.transpose(0, 2, 1)
    gate_t = gate_hit.transpose(0, 2, 1)
    select = chose_t[:, :, None, :] & (rank_t[:, :, None, :] == slot_ids[None, None, :, None])
    gate_slot = jnp.sum(jnp.where(select, gate_t[:, :, None, :], 0.0), axis=3, keepdims=True)
    weight_grad, slot_part = expert_kernel(
        (hidden, far, near, near_far), mine_all, rest_all, select.astype(bf16), gate_slot, down_weight
    )
    slot_part = slot_part.reshape(local_count, block_count, padded)[:, :, :capacity]
    slot_part = slot_part.transpose(1, 0, 2).reshape(peer_count, shards, local_count, capacity)
    piece_of = jnp.array([0, 2, 1, 3], jnp.int32)[jnp.arange(shards, dtype=jnp.int32) ^ my_dp]
    slot_part = jnp.take(slot_part, piece_of, axis=1)
    send_back = slot_part.reshape(block_count, local_count, capacity)
    returned = lax.all_to_all(
        send_back, ("expert", "dp"), split_axis=0, concat_axis=0, tiled=True
    )
    returned = returned.reshape(peer_count, shards, local_count, capacity)
    slot_grad = jnp.sum(returned, axis=1).reshape(expert_count, capacity)

    own_hit = expert_ids[:, :, None] == jnp.arange(expert_count, dtype=jnp.int32)[None, None, :]
    own_chose = jnp.any(own_hit, axis=1)
    own_rank = jnp.einsum(
        "ue,ut->te", own_chose.astype(bf16), before, preferred_element_type=f32
    ).astype(jnp.int32)
    own_slot = jnp.sum(jnp.where(own_hit, own_rank[:, None, :], 0), axis=2)
    by_slot = jnp.sum(jnp.where(own_hit[:, :, :, None], slot_grad[None, None], 0.0), axis=2)
    gate_grad = jnp.sum(
        jnp.where(own_slot[:, :, None] == slot_ids[None, None, :capacity], by_slot, 0.0), axis=2
    )
    return (weight_grad, gate_grad)


def solution(mesh):
    return jax.shard_map(
        per_device,
        mesh=mesh,
        in_specs=(
            P(("groups", "expert", "dp"), None),
            P(("groups", "expert", "dp"), None),
            P(("groups", "expert", "dp"), None),
            P("expert", ("groups", "dp"), None, None, None),
            P("expert", None, "dp"),
        ),
        out_specs=(P(("groups", "expert"), None, "dp"), P(("groups", "expert", "dp"), None)),
        check_vma=False,
    )
```

```python
import jax
import jax.numpy as jnp
from jax import lax
from jax.experimental import pallas as pl
from jax.experimental.pallas import tpu as pltpu
from jax.sharding import PartitionSpec as P


def expert_body(own_ref, far_ref, near_ref, near_far_ref, tok_ref, sel_ref, gate_ref, w_ref,
                wg_ref, slot_ref, h_scr, s_scr, g_scr):
    expert = pl.program_id(0)
    chunk = pl.program_id(1)
    sources, capacity, hidden_width = own_ref.shape[2:]
    blocks, _, padded, _ = sel_ref.shape
    col_width = tok_ref.shape[2]
    pieces = (own_ref, far_ref, near_ref, near_far_ref)

    @pl.when((expert == 0) & (chunk == 0))
    def _():
        h_scr[...] = jnp.zeros(h_scr.shape, h_scr.dtype)

    for src in range(sources):
        for j, ref in enumerate(pieces):
            row = (src * len(pieces) + j) * padded
            h_scr[row:row + capacity, :] = ref[0, 0, src]

    for blk in range(blocks):
        sel = sel_ref[blk, 0]
        rows = jnp.dot(sel, tok_ref[blk], preferred_element_type=jnp.float32)
        gate = jnp.sum(sel.astype(jnp.float32) * gate_ref[blk, 0], axis=1, keepdims=True)
        g_scr[blk * padded:(blk + 1) * padded, :] = rows.astype(jnp.bfloat16)
        s_scr[blk * padded:(blk + 1) * padded, :] = (gate * rows).astype(jnp.bfloat16)

    h = h_scr[...]
    part = lax.dot_general(
        h, s_scr[...], (((0,), (0,)), ((), ())), preferred_element_type=jnp.float32
    )

    @pl.when(chunk == 0)
    def _():
        wg_ref[0] = part

    @pl.when(chunk != 0)
    def _():
        wg_ref[0] = wg_ref[0] + part

    out = jnp.dot(h, w_ref[0], preferred_element_type=jnp.float32)
    slot_ref[0] = jnp.sum(g_scr[...].astype(jnp.float32) * out, axis=1, keepdims=True)


def expert_kernel(pieces, tokens, select, gate_row, weight):
    local_count, _, source_count, capacity, hidden_width = pieces[0].shape
    col_width = tokens.shape[2]
    block_count, _, padded, tok_rows = select.shape
    per_source = block_count // source_count
    chunk = source_count
    for size in (4, 2, 1):
        if source_count % size == 0:
            chunk = size
            break
    steps = source_count // chunk
    blocks = chunk * per_source
    rows = blocks * padded
    piece_spec = pl.BlockSpec(
        (1, 1, chunk, capacity, hidden_width), lambda l, r: (l, 0, r, 0, 0)
    )
    return pl.pallas_call(
        expert_body,
        grid=(local_count, steps),
        in_specs=[piece_spec] * len(pieces) + [
            pl.BlockSpec((blocks, tok_rows, col_width), lambda l, r: (r, 0, 0)),
            pl.BlockSpec((blocks, 1, padded, tok_rows), lambda l, r: (r, l, 0, 0)),
            pl.BlockSpec((blocks, 1, 1, tok_rows), lambda l, r: (r, l, 0, 0)),
            pl.BlockSpec((1, hidden_width, col_width), lambda l, r: (l, 0, 0)),
        ],
        out_specs=[
            pl.BlockSpec((1, hidden_width, col_width), lambda l, r: (l, 0, 0)),
            pl.BlockSpec((1, rows, 1), lambda l, r: (l, r, 0)),
        ],
        out_shape=[
            jax.ShapeDtypeStruct((local_count, hidden_width, col_width), jnp.float32),
            jax.ShapeDtypeStruct((local_count, block_count * padded, 1), jnp.float32),
        ],
        scratch_shapes=[
            pltpu.VMEM((rows, hidden_width), jnp.bfloat16),
            pltpu.VMEM((rows, col_width), jnp.bfloat16),
            pltpu.VMEM((rows, col_width), jnp.bfloat16),
        ],
    )(*pieces, tokens, select, gate_row, weight)


def per_device(out_grad, gate_weights, expert_ids, hidden, down_weight):
    tok_rows, top_count = expert_ids.shape
    row_width = out_grad.shape[1]
    local_count = hidden.shape[0]
    capacity = hidden.shape[3]
    hidden_width = hidden.shape[4]
    peer_count = lax.axis_size("expert")
    shards = lax.axis_size("dp")
    expert_count = local_count * peer_count
    col_width = row_width // shards
    block_count = peer_count * shards
    f32 = jnp.float32
    bf16 = jnp.bfloat16
    my_dp = lax.axis_index("dp")

    meta = jnp.concatenate([expert_ids.astype(bf16), gate_weights], axis=1).reshape(-1)
    meta_len = meta.shape[0]
    meta_rows = -(-meta_len // col_width)
    meta = jnp.pad(meta, (0, meta_rows * col_width - meta_len)).reshape(meta_rows, 1, col_width)
    cols = out_grad.reshape(tok_rows, shards, col_width)
    cols = jnp.concatenate([cols, jnp.broadcast_to(meta, (meta_rows, shards, col_width))], axis=0)
    cols = lax.all_to_all(cols, "dp", split_axis=1, concat_axis=0, tiled=True)
    cols = cols.reshape(shards, tok_rows + meta_rows, col_width)
    piece_xor = jnp.array([0, 2, 1, 3], jnp.int32)
    cols = jnp.take(cols, piece_xor ^ my_dp, axis=0)

    hidden_sent, cols = lax.optimization_barrier((hidden, cols))
    near = lax.ppermute(hidden_sent, "dp", [(j, j ^ 1) for j in range(shards)])
    far = lax.ppermute(hidden_sent, "dp", [(j, j ^ 2) for j in range(shards)])
    near_far = lax.ppermute(far, "dp", [(j, j ^ 1) for j in range(shards)])
    got = lax.all_gather(cols, "expert", axis=0, tiled=False)
    got = got.reshape(block_count, tok_rows + meta_rows, col_width)
    grad_all = got[:, :tok_rows]
    meta_all = got[:, tok_rows:].reshape(block_count, meta_rows * col_width)[:, :meta_len]
    meta_all = meta_all.reshape(block_count, tok_rows, 2 * top_count)
    ids_all = meta_all[:, :, :top_count].astype(jnp.int32)
    gate_all = meta_all[:, :, top_count:]

    my_experts = lax.axis_index("expert") * local_count + jnp.arange(local_count, dtype=jnp.int32)
    hit = ids_all[:, :, :, None] == my_experts[None, None, None, :]
    chose = jnp.any(hit, axis=2)
    gate_hit = jnp.sum(jnp.where(hit, gate_all.astype(f32)[:, :, :, None], 0.0), axis=2)
    before = (jnp.arange(tok_rows)[:, None] < jnp.arange(tok_rows)[None, :]).astype(bf16)
    rank = jnp.einsum(
        "bul,ut->btl", chose.astype(bf16), before, preferred_element_type=f32
    ).astype(jnp.int32)
    padded = -(-capacity // 16) * 16
    slot_ids = jnp.arange(padded, dtype=jnp.int32)
    chose_t = chose.transpose(0, 2, 1)
    rank_t = rank.transpose(0, 2, 1)
    gate_t = gate_hit.transpose(0, 2, 1)
    select = chose_t[:, :, None, :] & (rank_t[:, :, None, :] == slot_ids[None, None, :, None])
    gate_row = gate_t[:, :, None, :]
    weight_grad, slot_part = expert_kernel(
        (hidden, far, near, near_far), got, select.astype(bf16), gate_row, down_weight
    )
    slot_part = slot_part.reshape(local_count, block_count, padded)[:, :, :capacity]
    slot_part = slot_part.transpose(1, 0, 2).reshape(peer_count, shards, local_count, capacity)
    piece_of = jnp.array([0, 2, 1, 3], jnp.int32)[jnp.arange(shards, dtype=jnp.int32) ^ my_dp]
    slot_part = jnp.take(slot_part, piece_of, axis=1)
    send_back = slot_part.reshape(block_count, local_count, capacity)
    returned = lax.all_to_all(
        send_back, ("expert", "dp"), split_axis=0, concat_axis=0, tiled=True
    )
    returned = returned.reshape(peer_count, shards, local_count, capacity)
    slot_grad = jnp.sum(returned, axis=1).reshape(expert_count, capacity)

    own_hit = expert_ids[:, :, None] == jnp.arange(expert_count, dtype=jnp.int32)[None, None, :]
    own_chose = jnp.any(own_hit, axis=1)
    own_rank = jnp.einsum(
        "ue,ut->te", own_chose.astype(bf16), before, preferred_element_type=f32
    ).astype(jnp.int32)
    own_slot = jnp.sum(jnp.where(own_hit, own_rank[:, None, :], 0), axis=2)
    by_slot = jnp.sum(jnp.where(own_hit[:, :, :, None], slot_grad[None, None], 0.0), axis=2)
    gate_grad = jnp.sum(
        jnp.where(own_slot[:, :, None] == slot_ids[None, None, :capacity], by_slot, 0.0), axis=2
    )
    return (weight_grad, gate_grad)


def solution(mesh):
    return jax.shard_map(
        per_device,
        mesh=mesh,
        in_specs=(
            P(("groups", "expert", "dp"), None),
            P(("groups", "expert", "dp"), None),
            P(("groups", "expert", "dp"), None),
            P("expert", ("groups", "dp"), None, None, None),
            P("expert", None, "dp"),
        ),
        out_specs=(P(("groups", "expert"), None, "dp"), P(("groups", "expert", "dp"), None)),
        check_vma=False,
    )
```

```python
import jax
import jax.numpy as jnp
from jax import lax
from jax.experimental import pallas as pl
from jax.experimental.pallas import tpu as pltpu
from jax.sharding import PartitionSpec as P


def expert_body(own_ref, far_ref, near_ref, near_far_ref, tok_ref, sel_ref, gate_ref, w_ref,
                wg_ref, slot_ref, h_scr, s_scr, g_scr):
    expert = pl.program_id(0)
    chunk = pl.program_id(1)
    sources, capacity, hidden_width = own_ref.shape[2:]
    blocks, _, padded, _ = sel_ref.shape
    col_width = tok_ref.shape[2]
    pieces = (own_ref, far_ref, near_ref, near_far_ref)

    @pl.when((expert == 0) & (chunk == 0))
    def _():
        h_scr[...] = jnp.zeros(h_scr.shape, h_scr.dtype)

    for src in range(sources):
        for j, ref in enumerate(pieces):
            row = (src * len(pieces) + j) * padded
            h_scr[row:row + capacity, :] = ref[0, 0, src]

    for blk in range(blocks):
        sel = sel_ref[blk, 0]
        rows = jnp.dot(sel, tok_ref[blk], preferred_element_type=jnp.float32)
        gate = jnp.sum(sel.astype(jnp.float32) * gate_ref[blk, 0], axis=1, keepdims=True)
        g_scr[blk * padded:(blk + 1) * padded, :] = rows.astype(jnp.bfloat16)
        s_scr[blk * padded:(blk + 1) * padded, :] = (gate * rows).astype(jnp.bfloat16)

    h = h_scr[...]
    part = lax.dot_general(
        h, s_scr[...], (((0,), (0,)), ((), ())), preferred_element_type=jnp.float32
    )

    @pl.when(chunk == 0)
    def _():
        wg_ref[0] = part

    @pl.when(chunk != 0)
    def _():
        wg_ref[0] = wg_ref[0] + part

    out = jnp.dot(h, w_ref[0], preferred_element_type=jnp.float32)
    slot_ref[0] = jnp.sum(g_scr[...].astype(jnp.float32) * out, axis=1, keepdims=True)


def expert_kernel(pieces, tokens, select, gate_row, weight):
    local_count, _, source_count, capacity, hidden_width = pieces[0].shape
    col_width = tokens.shape[2]
    block_count, _, padded, tok_rows = select.shape
    per_source = block_count // source_count
    chunk = source_count
    for size in (4, 2, 1):
        if source_count % size == 0:
            chunk = size
            break
    steps = source_count // chunk
    blocks = chunk * per_source
    rows = blocks * padded
    piece_spec = pl.BlockSpec(
        (1, 1, chunk, capacity, hidden_width), lambda l, r: (l, 0, r, 0, 0)
    )
    return pl.pallas_call(
        expert_body,
        grid=(local_count, steps),
        in_specs=[piece_spec] * len(pieces) + [
            pl.BlockSpec((blocks, tok_rows, col_width), lambda l, r: (r, 0, 0)),
            pl.BlockSpec((blocks, 1, padded, tok_rows), lambda l, r: (r, l, 0, 0)),
            pl.BlockSpec((blocks, 1, 1, tok_rows), lambda l, r: (r, l, 0, 0)),
            pl.BlockSpec((1, hidden_width, col_width), lambda l, r: (l, 0, 0)),
        ],
        out_specs=[
            pl.BlockSpec((1, hidden_width, col_width), lambda l, r: (l, 0, 0)),
            pl.BlockSpec((1, rows, 1), lambda l, r: (l, r, 0)),
        ],
        out_shape=[
            jax.ShapeDtypeStruct((local_count, hidden_width, col_width), jnp.float32),
            jax.ShapeDtypeStruct((local_count, block_count * padded, 1), jnp.float32),
        ],
        scratch_shapes=[
            pltpu.VMEM((rows, hidden_width), jnp.bfloat16),
            pltpu.VMEM((rows, col_width), jnp.bfloat16),
            pltpu.VMEM((rows, col_width), jnp.bfloat16),
        ],
    )(*pieces, tokens, select, gate_row, weight)


def per_device(out_grad, gate_weights, expert_ids, hidden, down_weight):
    tok_rows, top_count = expert_ids.shape
    row_width = out_grad.shape[1]
    local_count = hidden.shape[0]
    capacity = hidden.shape[3]
    hidden_width = hidden.shape[4]
    peer_count = lax.axis_size("expert")
    shards = lax.axis_size("dp")
    expert_count = local_count * peer_count
    col_width = row_width // shards
    block_count = peer_count * shards
    f32 = jnp.float32
    bf16 = jnp.bfloat16
    my_dp = lax.axis_index("dp")

    meta = jnp.concatenate([expert_ids.astype(bf16), gate_weights], axis=1).reshape(-1)
    meta_len = meta.shape[0]
    meta_rows = -(-meta_len // col_width)
    meta = jnp.pad(meta, (0, meta_rows * col_width - meta_len)).reshape(meta_rows, 1, col_width)
    cols = out_grad.reshape(tok_rows, shards, col_width)
    cols = jnp.concatenate([cols, jnp.broadcast_to(meta, (meta_rows, shards, col_width))], axis=0)
    cols = lax.all_to_all(cols, "dp", split_axis=1, concat_axis=0, tiled=True)
    cols = cols.reshape(shards, tok_rows + meta_rows, col_width)
    piece_xor = jnp.array([0, 2, 1, 3], jnp.int32)
    cols = jnp.take(cols, piece_xor ^ my_dp, axis=0)

    hidden_sent, cols = lax.optimization_barrier((hidden, cols))
    near = lax.ppermute(hidden_sent, "dp", [(j, j ^ 1) for j in range(shards)])
    cut = local_count // 2 if local_count > 1 else local_count
    far_parts = [
        lax.ppermute(part, "dp", [(j, j ^ 2) for j in range(shards)])
        for part in (hidden_sent[:cut], hidden_sent[cut:]) if part.shape[0] > 0
    ]
    near_far = jnp.concatenate(
        [lax.ppermute(part, "dp", [(j, j ^ 1) for j in range(shards)]) for part in far_parts], axis=0
    )
    far = jnp.concatenate(far_parts, axis=0)
    got = lax.all_gather(cols, "expert", axis=0, tiled=False)
    got = got.reshape(block_count, tok_rows + meta_rows, col_width)
    grad_all = got[:, :tok_rows]
    meta_all = got[:, tok_rows:].reshape(block_count, meta_rows * col_width)[:, :meta_len]
    meta_all = meta_all.reshape(block_count, tok_rows, 2 * top_count)
    ids_all = meta_all[:, :, :top_count].astype(jnp.int32)
    gate_all = meta_all[:, :, top_count:]

    my_experts = lax.axis_index("expert") * local_count + jnp.arange(local_count, dtype=jnp.int32)
    hit = ids_all[:, :, :, None] == my_experts[None, None, None, :]
    chose = jnp.any(hit, axis=2)
    gate_hit = jnp.sum(jnp.where(hit, gate_all.astype(f32)[:, :, :, None], 0.0), axis=2)
    before = (jnp.arange(tok_rows)[:, None] < jnp.arange(tok_rows)[None, :]).astype(bf16)
    rank = jnp.einsum(
        "bul,ut->btl", chose.astype(bf16), before, preferred_element_type=f32
    ).astype(jnp.int32)
    padded = -(-capacity // 16) * 16
    slot_ids = jnp.arange(padded, dtype=jnp.int32)
    chose_t = chose.transpose(0, 2, 1)
    rank_t = rank.transpose(0, 2, 1)
    gate_t = gate_hit.transpose(0, 2, 1)
    select = chose_t[:, :, None, :] & (rank_t[:, :, None, :] == slot_ids[None, None, :, None])
    gate_row = gate_t[:, :, None, :]
    weight_grad, slot_part = expert_kernel(
        (hidden, far, near, near_far), got, select.astype(bf16), gate_row, down_weight
    )
    slot_part = slot_part.reshape(local_count, block_count, padded)[:, :, :capacity]
    slot_part = slot_part.transpose(1, 0, 2).reshape(peer_count, shards, local_count, capacity)
    piece_of = jnp.array([0, 2, 1, 3], jnp.int32)[jnp.arange(shards, dtype=jnp.int32) ^ my_dp]
    slot_part = jnp.take(slot_part, piece_of, axis=1)
    send_back = slot_part.reshape(block_count, local_count, capacity)
    returned = lax.all_to_all(
        send_back, ("expert", "dp"), split_axis=0, concat_axis=0, tiled=True
    )
    returned = returned.reshape(peer_count, shards, local_count, capacity)
    slot_grad = jnp.sum(returned, axis=1).reshape(expert_count, capacity)

    own_hit = expert_ids[:, :, None] == jnp.arange(expert_count, dtype=jnp.int32)[None, None, :]
    own_chose = jnp.any(own_hit, axis=1)
    own_rank = jnp.einsum(
        "ue,ut->te", own_chose.astype(bf16), before, preferred_element_type=f32
    ).astype(jnp.int32)
    own_slot = jnp.sum(jnp.where(own_hit, own_rank[:, None, :], 0), axis=2)
    by_slot = jnp.sum(jnp.where(own_hit[:, :, :, None], slot_grad[None, None], 0.0), axis=2)
    gate_grad = jnp.sum(
        jnp.where(own_slot[:, :, None] == slot_ids[None, None, :capacity], by_slot, 0.0), axis=2
    )
    return (weight_grad, gate_grad)


def solution(mesh):
    return jax.shard_map(
        per_device,
        mesh=mesh,
        in_specs=(
            P(("groups", "expert", "dp"), None),
            P(("groups", "expert", "dp"), None),
            P(("groups", "expert", "dp"), None),
            P("expert", ("groups", "dp"), None, None, None),
            P("expert", None, "dp"),
        ),
        out_specs=(P(("groups", "expert"), None, "dp"), P(("groups", "expert", "dp"), None)),
        check_vma=False,
    )
```

```python
import jax
import jax.numpy as jnp
from jax import lax
from jax.experimental import pallas as pl
from jax.experimental.pallas import tpu as pltpu
from jax.sharding import PartitionSpec as P


def expert_body(own_ref, far_ref, near_ref, near_far_ref, tok_ref, sel_ref, gate_ref, w_ref,
                wg_ref, slot_ref, h_scr, s_scr, g_scr):
    expert = pl.program_id(0)
    chunk = pl.program_id(1)
    sources, capacity, hidden_width = own_ref.shape[2:]
    blocks = sel_ref.shape[0]
    padded = s_scr.shape[0] // blocks
    col_width = tok_ref.shape[2]
    pieces = (own_ref, far_ref, near_ref, near_far_ref)

    @pl.when((expert == 0) & (chunk == 0))
    def _():
        h_scr[...] = jnp.zeros(h_scr.shape, h_scr.dtype)

    for src in range(sources):
        for j, ref in enumerate(pieces):
            row = (src * len(pieces) + j) * padded
            h_scr[row:row + capacity, :] = ref[0, 0, src]

    slot_iota = lax.broadcasted_iota(jnp.int32, (padded, tok_ref.shape[1]), 0)
    for blk in range(blocks):
        hit = sel_ref[blk, 0] == slot_iota
        sel = hit.astype(jnp.bfloat16)
        rows = jnp.dot(sel, tok_ref[blk], preferred_element_type=jnp.float32)
        gate = jnp.sum(jnp.where(hit, gate_ref[blk, 0], 0.0), axis=1, keepdims=True)
        g_scr[blk * padded:(blk + 1) * padded, :] = rows.astype(jnp.bfloat16)
        s_scr[blk * padded:(blk + 1) * padded, :] = (gate * rows).astype(jnp.bfloat16)

    h = h_scr[...]
    part = lax.dot_general(
        h, s_scr[...], (((0,), (0,)), ((), ())), preferred_element_type=jnp.float32
    )

    @pl.when(chunk == 0)
    def _():
        wg_ref[0] = part

    @pl.when(chunk != 0)
    def _():
        wg_ref[0] = wg_ref[0] + part

    out = jnp.dot(h, w_ref[0], preferred_element_type=jnp.float32)
    col = jnp.sum(g_scr[...].astype(jnp.float32) * out, axis=1, keepdims=True)
    wide = jnp.broadcast_to(col, (col.shape[0], 128))
    slot_ref[0] = jnp.transpose(wide)[0:1, :]


def expert_kernel(pieces, tokens, slot_row, gate_row, weight, padded):
    local_count, _, source_count, capacity, hidden_width = pieces[0].shape
    col_width = tokens.shape[2]
    block_count, _, _, tok_rows = slot_row.shape
    per_source = block_count // source_count
    chunk = source_count
    for size in (4, 2, 1):
        if source_count % size == 0:
            chunk = size
            break
    steps = source_count // chunk
    blocks = chunk * per_source
    rows = blocks * padded
    piece_spec = pl.BlockSpec(
        (1, 1, chunk, capacity, hidden_width), lambda l, r: (l, 0, r, 0, 0)
    )
    return pl.pallas_call(
        expert_body,
        grid=(local_count, steps),
        in_specs=[piece_spec] * len(pieces) + [
            pl.BlockSpec((blocks, tok_rows, col_width), lambda l, r: (r, 0, 0)),
            pl.BlockSpec((blocks, 1, 1, tok_rows), lambda l, r: (r, l, 0, 0)),
            pl.BlockSpec((blocks, 1, 1, tok_rows), lambda l, r: (r, l, 0, 0)),
            pl.BlockSpec((1, hidden_width, col_width), lambda l, r: (l, 0, 0)),
        ],
        out_specs=[
            pl.BlockSpec((1, hidden_width, col_width), lambda l, r: (l, 0, 0)),
            pl.BlockSpec((1, 1, rows), lambda l, r: (l, 0, r)),
        ],
        out_shape=[
            jax.ShapeDtypeStruct((local_count, hidden_width, col_width), jnp.float32),
            jax.ShapeDtypeStruct((local_count, 1, block_count * padded), jnp.float32),
        ],
        scratch_shapes=[
            pltpu.VMEM((rows, hidden_width), jnp.bfloat16),
            pltpu.VMEM((rows, col_width), jnp.bfloat16),
            pltpu.VMEM((rows, col_width), jnp.bfloat16),
        ],
    )(*pieces, tokens, slot_row, gate_row, weight)


def per_device(out_grad, gate_weights, expert_ids, hidden, down_weight):
    tok_rows, top_count = expert_ids.shape
    row_width = out_grad.shape[1]
    local_count = hidden.shape[0]
    capacity = hidden.shape[3]
    hidden_width = hidden.shape[4]
    peer_count = lax.axis_size("expert")
    shards = lax.axis_size("dp")
    expert_count = local_count * peer_count
    col_width = row_width // shards
    block_count = peer_count * shards
    f32 = jnp.float32
    bf16 = jnp.bfloat16
    my_dp = lax.axis_index("dp")

    meta = jnp.concatenate([expert_ids.astype(bf16), gate_weights], axis=1).reshape(-1)
    meta_len = meta.shape[0]
    meta_rows = -(-meta_len // col_width)
    meta = jnp.pad(meta, (0, meta_rows * col_width - meta_len)).reshape(meta_rows, 1, col_width)
    cols = out_grad.reshape(tok_rows, shards, col_width)
    cols = jnp.concatenate([cols, jnp.broadcast_to(meta, (meta_rows, shards, col_width))], axis=0)
    cols = lax.all_to_all(cols, "dp", split_axis=1, concat_axis=0, tiled=True)
    cols = cols.reshape(shards, tok_rows + meta_rows, col_width)
    piece_xor = jnp.array([0, 2, 1, 3], jnp.int32)
    cols = jnp.take(cols, piece_xor ^ my_dp, axis=0)

    hidden_sent, cols = lax.optimization_barrier((hidden, cols))
    near = lax.ppermute(hidden_sent, "dp", [(j, j ^ 1) for j in range(shards)])
    far = lax.ppermute(hidden_sent, "dp", [(j, j ^ 2) for j in range(shards)])
    near_far = lax.ppermute(far, "dp", [(j, j ^ 1) for j in range(shards)])
    got = lax.all_gather(cols, "expert", axis=0, tiled=False)
    got = got.reshape(block_count, tok_rows + meta_rows, col_width)
    grad_all = got[:, :tok_rows]
    meta_all = got[:, tok_rows:].reshape(block_count, meta_rows * col_width)[:, :meta_len]
    meta_all = meta_all.reshape(block_count, tok_rows, 2 * top_count)
    ids_all = meta_all[:, :, :top_count].astype(jnp.int32)
    gate_all = meta_all[:, :, top_count:]

    my_experts = lax.axis_index("expert") * local_count + jnp.arange(local_count, dtype=jnp.int32)
    hit = ids_all[:, :, :, None] == my_experts[None, None, None, :]
    chose = jnp.any(hit, axis=2)
    gate_hit = jnp.sum(jnp.where(hit, gate_all.astype(f32)[:, :, :, None], 0.0), axis=2)
    before = (jnp.arange(tok_rows)[:, None] < jnp.arange(tok_rows)[None, :]).astype(bf16)
    rank = jnp.einsum(
        "bul,ut->btl", chose.astype(bf16), before, preferred_element_type=f32
    ).astype(jnp.int32)
    padded = -(-capacity // 16) * 16
    slot_ids = jnp.arange(padded, dtype=jnp.int32)
    chose_t = chose.transpose(0, 2, 1)
    rank_t = rank.transpose(0, 2, 1)
    gate_t = gate_hit.transpose(0, 2, 1)
    slot_row = jnp.where(chose_t, rank_t, -1)[:, :, None, :]
    gate_row = gate_t[:, :, None, :]
    weight_grad, slot_part = expert_kernel(
        (hidden, far, near, near_far), got, slot_row, gate_row, down_weight, padded
    )
    slot_part = slot_part.reshape(local_count, block_count, padded)[:, :, :capacity]
    slot_part = slot_part.transpose(1, 0, 2).reshape(peer_count, shards, local_count, capacity)
    piece_of = jnp.array([0, 2, 1, 3], jnp.int32)[jnp.arange(shards, dtype=jnp.int32) ^ my_dp]
    slot_part = jnp.take(slot_part, piece_of, axis=1)
    send_back = slot_part.reshape(block_count, local_count, capacity)
    returned = lax.all_to_all(
        send_back, ("expert", "dp"), split_axis=0, concat_axis=0, tiled=True
    )
    returned = returned.reshape(peer_count, shards, local_count, capacity)
    slot_grad = jnp.sum(returned, axis=1).reshape(expert_count, capacity)

    own_hit = expert_ids[:, :, None] == jnp.arange(expert_count, dtype=jnp.int32)[None, None, :]
    own_chose = jnp.any(own_hit, axis=1)
    own_rank = jnp.einsum(
        "ue,ut->te", own_chose.astype(bf16), before, preferred_element_type=f32
    ).astype(jnp.int32)
    own_slot = jnp.sum(jnp.where(own_hit, own_rank[:, None, :], 0), axis=2)
    by_slot = jnp.sum(jnp.where(own_hit[:, :, :, None], slot_grad[None, None], 0.0), axis=2)
    gate_grad = jnp.sum(
        jnp.where(own_slot[:, :, None] == slot_ids[None, None, :capacity], by_slot, 0.0), axis=2
    )
    return (weight_grad, gate_grad)


def solution(mesh):
    return jax.shard_map(
        per_device,
        mesh=mesh,
        in_specs=(
            P(("groups", "expert", "dp"), None),
            P(("groups", "expert", "dp"), None),
            P(("groups", "expert", "dp"), None),
            P("expert", ("groups", "dp"), None, None, None),
            P("expert", None, "dp"),
        ),
        out_specs=(P(("groups", "expert"), None, "dp"), P(("groups", "expert", "dp"), None)),
        check_vma=False,
    )
```

```python
import jax
import jax.numpy as jnp
from jax import lax
from jax.experimental import pallas as pl
from jax.experimental.pallas import tpu as pltpu
from jax.sharding import PartitionSpec as P


def expert_body(own_ref, far_ref, near_ref, near_far_ref, tok_ref, sel_ref, gate_ref, w_ref,
                wg_ref, slot_ref, h_scr, s_scr, g_scr):
    expert = pl.program_id(0)
    chunk = pl.program_id(1)
    sources, capacity, hidden_width = own_ref.shape[2:]
    blocks = sel_ref.shape[0]
    padded = s_scr.shape[0] // blocks
    col_width = tok_ref.shape[2]
    pieces = (own_ref, far_ref, near_ref, near_far_ref)

    @pl.when((expert == 0) & (chunk == 0))
    def _():
        h_scr[...] = jnp.zeros(h_scr.shape, h_scr.dtype)

    for src in range(sources):
        for j, ref in enumerate(pieces):
            row = (src * len(pieces) + j) * padded
            h_scr[row:row + capacity, :] = ref[0, 0, src].astype(jnp.float32)

    slot_iota = lax.broadcasted_iota(jnp.int32, (padded, tok_ref.shape[1]), 0)
    for blk in range(blocks):
        hit = sel_ref[blk, 0] == slot_iota
        sel = hit.astype(jnp.bfloat16)
        rows = jnp.dot(sel, tok_ref[blk], preferred_element_type=jnp.float32)
        gate = jnp.sum(jnp.where(hit, gate_ref[blk, 0], 0.0), axis=1, keepdims=True)
        g_scr[blk * padded:(blk + 1) * padded, :] = rows
        s_scr[blk * padded:(blk + 1) * padded, :] = (
            (gate * rows).astype(jnp.bfloat16).astype(jnp.float32)
        )

    h = h_scr[...].astype(jnp.bfloat16)
    part = lax.dot_general(
        h, s_scr[...].astype(jnp.bfloat16), (((0,), (0,)), ((), ())),
        preferred_element_type=jnp.float32,
    )

    @pl.when(chunk == 0)
    def _():
        wg_ref[0] = part

    @pl.when(chunk != 0)
    def _():
        wg_ref[0] = wg_ref[0] + part

    out = jnp.dot(h, w_ref[0], preferred_element_type=jnp.float32)
    col = jnp.sum(g_scr[...] * out, axis=1, keepdims=True)
    wide = jnp.broadcast_to(col, (col.shape[0], 128))
    slot_ref[0] = jnp.transpose(wide)[0:1, :]


def expert_kernel(pieces, tokens, slot_row, gate_row, weight, padded):
    local_count, _, source_count, capacity, hidden_width = pieces[0].shape
    col_width = tokens.shape[2]
    block_count, _, _, tok_rows = slot_row.shape
    per_source = block_count // source_count
    chunk = source_count
    for size in (4, 2, 1):
        if source_count % size == 0:
            chunk = size
            break
    steps = source_count // chunk
    blocks = chunk * per_source
    rows = blocks * padded
    piece_spec = pl.BlockSpec(
        (1, 1, chunk, capacity, hidden_width), lambda l, r: (l, 0, r, 0, 0)
    )
    return pl.pallas_call(
        expert_body,
        grid=(local_count, steps),
        in_specs=[piece_spec] * len(pieces) + [
            pl.BlockSpec((blocks, tok_rows, col_width), lambda l, r: (r, 0, 0)),
            pl.BlockSpec((blocks, 1, 1, tok_rows), lambda l, r: (r, l, 0, 0)),
            pl.BlockSpec((blocks, 1, 1, tok_rows), lambda l, r: (r, l, 0, 0)),
            pl.BlockSpec((1, hidden_width, col_width), lambda l, r: (l, 0, 0)),
        ],
        out_specs=[
            pl.BlockSpec((1, hidden_width, col_width), lambda l, r: (l, 0, 0)),
            pl.BlockSpec((1, 1, rows), lambda l, r: (l, 0, r)),
        ],
        out_shape=[
            jax.ShapeDtypeStruct((local_count, hidden_width, col_width), jnp.float32),
            jax.ShapeDtypeStruct((local_count, 1, block_count * padded), jnp.float32),
        ],
        scratch_shapes=[
            pltpu.VMEM((rows, hidden_width), jnp.float32),
            pltpu.VMEM((rows, col_width), jnp.float32),
            pltpu.VMEM((rows, col_width), jnp.float32),
        ],
    )(*pieces, tokens, slot_row, gate_row, weight)


def per_device(out_grad, gate_weights, expert_ids, hidden, down_weight):
    tok_rows, top_count = expert_ids.shape
    row_width = out_grad.shape[1]
    local_count = hidden.shape[0]
    capacity = hidden.shape[3]
    hidden_width = hidden.shape[4]
    peer_count = lax.axis_size("expert")
    shards = lax.axis_size("dp")
    expert_count = local_count * peer_count
    col_width = row_width // shards
    block_count = peer_count * shards
    f32 = jnp.float32
    bf16 = jnp.bfloat16
    my_dp = lax.axis_index("dp")

    meta = jnp.concatenate([expert_ids.astype(bf16), gate_weights], axis=1).reshape(-1)
    meta_len = meta.shape[0]
    meta_rows = -(-meta_len // col_width)
    meta = jnp.pad(meta, (0, meta_rows * col_width - meta_len)).reshape(meta_rows, 1, col_width)
    cols = out_grad.reshape(tok_rows, shards, col_width)
    cols = jnp.concatenate([cols, jnp.broadcast_to(meta, (meta_rows, shards, col_width))], axis=0)
    cols = lax.all_to_all(cols, "dp", split_axis=1, concat_axis=0, tiled=True)
    cols = cols.reshape(shards, tok_rows + meta_rows, col_width)
    piece_xor = jnp.array([0, 2, 1, 3], jnp.int32)
    cols = jnp.take(cols, piece_xor ^ my_dp, axis=0)

    hidden_sent, cols = lax.optimization_barrier((hidden, cols))
    near = lax.ppermute(hidden_sent, "dp", [(j, j ^ 1) for j in range(shards)])
    far = lax.ppermute(hidden_sent, "dp", [(j, j ^ 2) for j in range(shards)])
    near_far = lax.ppermute(far, "dp", [(j, j ^ 1) for j in range(shards)])
    got = lax.all_gather(cols, "expert", axis=0, tiled=False)
    got = got.reshape(block_count, tok_rows + meta_rows, col_width)
    grad_all = got[:, :tok_rows]
    meta_all = got[:, tok_rows:].reshape(block_count, meta_rows * col_width)[:, :meta_len]
    meta_all = meta_all.reshape(block_count, tok_rows, 2 * top_count)
    ids_all = meta_all[:, :, :top_count].astype(jnp.int32)
    gate_all = meta_all[:, :, top_count:]

    my_experts = lax.axis_index("expert") * local_count + jnp.arange(local_count, dtype=jnp.int32)
    hit = ids_all[:, :, :, None] == my_experts[None, None, None, :]
    chose = jnp.any(hit, axis=2)
    gate_hit = jnp.sum(jnp.where(hit, gate_all.astype(f32)[:, :, :, None], 0.0), axis=2)
    before = (jnp.arange(tok_rows)[:, None] < jnp.arange(tok_rows)[None, :]).astype(bf16)
    rank = jnp.einsum(
        "bul,ut->btl", chose.astype(bf16), before, preferred_element_type=f32
    ).astype(jnp.int32)
    padded = -(-capacity // 8) * 8
    slot_ids = jnp.arange(padded, dtype=jnp.int32)
    chose_t = chose.transpose(0, 2, 1)
    rank_t = rank.transpose(0, 2, 1)
    gate_t = gate_hit.transpose(0, 2, 1)
    slot_row = jnp.where(chose_t, rank_t, -1)[:, :, None, :]
    gate_row = gate_t[:, :, None, :]
    weight_grad, slot_part = expert_kernel(
        (hidden, far, near, near_far), got, slot_row, gate_row, down_weight, padded
    )
    slot_part = slot_part.reshape(local_count, block_count, padded)[:, :, :capacity]
    slot_part = slot_part.transpose(1, 0, 2).reshape(peer_count, shards, local_count, capacity)
    piece_of = jnp.array([0, 2, 1, 3], jnp.int32)[jnp.arange(shards, dtype=jnp.int32) ^ my_dp]
    slot_part = jnp.take(slot_part, piece_of, axis=1)
    send_back = slot_part.reshape(block_count, local_count, capacity)
    returned = lax.all_to_all(
        send_back, ("expert", "dp"), split_axis=0, concat_axis=0, tiled=True
    )
    returned = returned.reshape(peer_count, shards, local_count, capacity)
    slot_grad = jnp.sum(returned, axis=1).reshape(expert_count, capacity)

    own_hit = expert_ids[:, :, None] == jnp.arange(expert_count, dtype=jnp.int32)[None, None, :]
    own_chose = jnp.any(own_hit, axis=1)
    own_rank = jnp.einsum(
        "ue,ut->te", own_chose.astype(bf16), before, preferred_element_type=f32
    ).astype(jnp.int32)
    own_slot = jnp.sum(jnp.where(own_hit, own_rank[:, None, :], 0), axis=2)
    by_slot = jnp.sum(jnp.where(own_hit[:, :, :, None], slot_grad[None, None], 0.0), axis=2)
    gate_grad = jnp.sum(
        jnp.where(own_slot[:, :, None] == slot_ids[None, None, :capacity], by_slot, 0.0), axis=2
    )
    return (weight_grad, gate_grad)


def solution(mesh):
    return jax.shard_map(
        per_device,
        mesh=mesh,
        in_specs=(
            P(("groups", "expert", "dp"), None),
            P(("groups", "expert", "dp"), None),
            P(("groups", "expert", "dp"), None),
            P("expert", ("groups", "dp"), None, None, None),
            P("expert", None, "dp"),
        ),
        out_specs=(P(("groups", "expert"), None, "dp"), P(("groups", "expert", "dp"), None)),
        check_vma=False,
    )
```

```python
import jax
import jax.numpy as jnp
from jax import lax
from jax.experimental import pallas as pl
from jax.experimental.pallas import tpu as pltpu
from jax.sharding import PartitionSpec as P


def expert_body(own_ref, far_ref, near_ref, near_far_ref, tok_ref, sel_ref, gate_ref, w_ref,
                wg_ref, slot_ref, h_scr, s_scr, g_scr):
    expert = pl.program_id(0)
    chunk = pl.program_id(1)
    sources, capacity, hidden_width = own_ref.shape[2:]
    blocks = sel_ref.shape[0]
    padded = s_scr.shape[0] // blocks
    col_width = tok_ref.shape[2]
    pieces = (own_ref, far_ref, near_ref, near_far_ref)

    @pl.when((expert == 0) & (chunk == 0))
    def _():
        h_scr[...] = jnp.zeros(h_scr.shape, h_scr.dtype)

    for src in range(sources):
        for j, ref in enumerate(pieces):
            row = (src * len(pieces) + j) * padded
            h_scr[row:row + capacity, :] = ref[0, 0, src].astype(jnp.float32)

    slot_iota = lax.broadcasted_iota(jnp.int32, (padded, tok_ref.shape[1]), 0)
    for blk in range(blocks):
        hit = sel_ref[blk, 0] == slot_iota
        sel = hit.astype(jnp.bfloat16)
        rows = jnp.dot(sel, tok_ref[blk], preferred_element_type=jnp.float32)
        gate = jnp.sum(jnp.where(hit, gate_ref[blk, 0], 0.0), axis=1, keepdims=True)
        g_scr[blk * padded:(blk + 1) * padded, :] = rows
        s_scr[blk * padded:(blk + 1) * padded, :] = (
            (gate * rows).astype(jnp.bfloat16).astype(jnp.float32)
        )

    h = h_scr[...].astype(jnp.bfloat16)
    part = lax.dot_general(
        h, s_scr[...].astype(jnp.bfloat16), (((0,), (0,)), ((), ())),
        preferred_element_type=jnp.float32,
    )

    @pl.when(chunk == 0)
    def _():
        wg_ref[0] = part

    @pl.when(chunk != 0)
    def _():
        wg_ref[0] = wg_ref[0] + part

    out = jnp.dot(h, w_ref[0], preferred_element_type=jnp.float32)
    col = jnp.sum(g_scr[...] * out, axis=1, keepdims=True)
    wide = jnp.broadcast_to(col, (col.shape[0], 128))
    slot_ref[0] = jnp.transpose(wide)[0:1, :]


def expert_kernel(pieces, tokens, slot_row, gate_row, weight, padded):
    local_count, _, source_count, capacity, hidden_width = pieces[0].shape
    col_width = tokens.shape[2]
    block_count, _, _, tok_rows = slot_row.shape
    per_source = block_count // source_count
    chunk = source_count
    for size in (4, 2, 1):
        if source_count % size == 0:
            chunk = size
            break
    steps = source_count // chunk
    blocks = chunk * per_source
    rows = blocks * padded
    piece_spec = pl.BlockSpec(
        (1, 1, chunk, capacity, hidden_width), lambda l, r: (l, 0, r, 0, 0)
    )
    return pl.pallas_call(
        expert_body,
        grid=(local_count, steps),
        in_specs=[piece_spec] * len(pieces) + [
            pl.BlockSpec((blocks, tok_rows, col_width), lambda l, r: (r, 0, 0)),
            pl.BlockSpec((blocks, 1, 1, tok_rows), lambda l, r: (r, l, 0, 0)),
            pl.BlockSpec((blocks, 1, 1, tok_rows), lambda l, r: (r, l, 0, 0)),
            pl.BlockSpec((1, hidden_width, col_width), lambda l, r: (l, 0, 0)),
        ],
        out_specs=[
            pl.BlockSpec((1, hidden_width, col_width), lambda l, r: (l, 0, 0)),
            pl.BlockSpec((1, 1, rows), lambda l, r: (l, 0, r)),
        ],
        out_shape=[
            jax.ShapeDtypeStruct((local_count, hidden_width, col_width), jnp.float32),
            jax.ShapeDtypeStruct((local_count, 1, block_count * padded), jnp.float32),
        ],
        scratch_shapes=[
            pltpu.VMEM((rows, hidden_width), jnp.float32),
            pltpu.VMEM((rows, col_width), jnp.float32),
            pltpu.VMEM((rows, col_width), jnp.float32),
        ],
    )(*pieces, tokens, slot_row, gate_row, weight)


def per_device(out_grad, gate_weights, expert_ids, hidden, down_weight):
    tok_rows, top_count = expert_ids.shape
    row_width = out_grad.shape[1]
    local_count = hidden.shape[0]
    capacity = hidden.shape[3]
    hidden_width = hidden.shape[4]
    peer_count = lax.axis_size("expert")
    shards = lax.axis_size("dp")
    expert_count = local_count * peer_count
    col_width = row_width // shards
    block_count = peer_count * shards
    f32 = jnp.float32
    bf16 = jnp.bfloat16
    my_dp = lax.axis_index("dp")

    meta = jnp.concatenate([expert_ids.astype(bf16), gate_weights], axis=1).reshape(-1)
    meta_len = meta.shape[0]
    meta_rows = -(-meta_len // col_width)
    meta = jnp.pad(meta, (0, meta_rows * col_width - meta_len)).reshape(meta_rows, 1, col_width)
    cols = out_grad.reshape(tok_rows, shards, col_width)
    cols = jnp.concatenate([cols, jnp.broadcast_to(meta, (meta_rows, shards, col_width))], axis=0)
    cols = lax.all_to_all(cols, "dp", split_axis=1, concat_axis=0, tiled=True)
    cols = cols.reshape(shards, tok_rows + meta_rows, col_width)
    piece_xor = jnp.array([0, 2, 1, 3], jnp.int32)
    cols = jnp.take(cols, piece_xor ^ my_dp, axis=0)

    hidden_sent, cols = lax.optimization_barrier((hidden, cols))
    near = lax.ppermute(hidden_sent, "dp", [(j, j ^ 1) for j in range(shards)])
    far = lax.ppermute(hidden_sent, "dp", [(j, j ^ 2) for j in range(shards)])
    near_far = lax.ppermute(far, "dp", [(j, j ^ 1) for j in range(shards)])
    got = lax.all_gather(cols, "expert", axis=0, tiled=False)
    got = got.reshape(block_count, tok_rows + meta_rows, col_width)
    grad_all = got[:, :tok_rows]
    meta_all = got[:, tok_rows:].reshape(block_count, meta_rows * col_width)[:, :meta_len]
    meta_all = meta_all.reshape(block_count, tok_rows, 2 * top_count)
    ids_all = meta_all[:, :, :top_count].astype(jnp.int32)
    gate_all = meta_all[:, :, top_count:]

    my_experts = lax.axis_index("expert") * local_count + jnp.arange(local_count, dtype=jnp.int32)
    hit = ids_all[:, :, :, None] == my_experts[None, None, None, :]
    chose = jnp.any(hit, axis=2)
    gate_hit = jnp.sum(jnp.where(hit, gate_all.astype(f32)[:, :, :, None], 0.0), axis=2)
    before = (jnp.arange(tok_rows)[:, None] < jnp.arange(tok_rows)[None, :]).astype(bf16)
    rank = jnp.einsum(
        "bul,ut->btl", chose.astype(bf16), before, preferred_element_type=f32
    ).astype(jnp.int32)
    padded = -(-capacity // 8) * 8
    slot_ids = jnp.arange(padded, dtype=jnp.int32)
    chose_t = chose.transpose(0, 2, 1)
    rank_t = rank.transpose(0, 2, 1)
    gate_t = gate_hit.transpose(0, 2, 1)
    slot_row = jnp.where(chose_t, rank_t, -1)[:, :, None, :]
    gate_row = gate_t[:, :, None, :]
    weight_grad, slot_part = expert_kernel(
        (hidden, far, near, near_far), got, slot_row, gate_row, down_weight, padded
    )
    slot_part = slot_part.reshape(local_count, block_count, padded)[:, :, :capacity]
    slot_part = slot_part.transpose(1, 0, 2).reshape(peer_count, shards, local_count, capacity)
    piece_of = jnp.array([0, 2, 1, 3], jnp.int32)[jnp.arange(shards, dtype=jnp.int32) ^ my_dp]
    slot_part = jnp.take(slot_part, piece_of, axis=1)
    returned = lax.all_to_all(slot_part, "expert", split_axis=0, concat_axis=0, tiled=True)
    returned = lax.all_to_all(returned, "dp", split_axis=1, concat_axis=1, tiled=True)
    slot_grad = jnp.sum(returned, axis=1).reshape(expert_count, capacity)

    own_hit = expert_ids[:, :, None] == jnp.arange(expert_count, dtype=jnp.int32)[None, None, :]
    own_chose = jnp.any(own_hit, axis=1)
    own_rank = jnp.einsum(
        "ue,ut->te", own_chose.astype(bf16), before, preferred_element_type=f32
    ).astype(jnp.int32)
    own_slot = jnp.sum(jnp.where(own_hit, own_rank[:, None, :], 0), axis=2)
    by_slot = jnp.sum(jnp.where(own_hit[:, :, :, None], slot_grad[None, None], 0.0), axis=2)
    gate_grad = jnp.sum(
        jnp.where(own_slot[:, :, None] == slot_ids[None, None, :capacity], by_slot, 0.0), axis=2
    )
    return (weight_grad, gate_grad)


def solution(mesh):
    return jax.shard_map(
        per_device,
        mesh=mesh,
        in_specs=(
            P(("groups", "expert", "dp"), None),
            P(("groups", "expert", "dp"), None),
            P(("groups", "expert", "dp"), None),
            P("expert", ("groups", "dp"), None, None, None),
            P("expert", None, "dp"),
        ),
        out_specs=(P(("groups", "expert"), None, "dp"), P(("groups", "expert", "dp"), None)),
        check_vma=False,
    )
```

```python
import jax
import jax.numpy as jnp
from jax import lax
from jax.experimental import pallas as pl
from jax.experimental.pallas import tpu as pltpu
from jax.sharding import PartitionSpec as P


def expert_body(own_ref, far_ref, near_ref, near_far_ref, tok_ref, sel_ref, gate_ref, w_ref,
                wg_ref, slot_ref, h_scr, s_scr, g_scr):
    expert = pl.program_id(0)
    chunk = pl.program_id(1)
    blocks = sel_ref.shape[0]
    padded = s_scr.shape[0] // blocks
    sources = blocks // 4
    capacity = own_ref.shape[0] // sources
    col_width = tok_ref.shape[2]
    pieces = (own_ref, far_ref, near_ref, near_far_ref)

    @pl.when((expert == 0) & (chunk == 0))
    def _():
        h_scr[...] = jnp.zeros(h_scr.shape, h_scr.dtype)

    for src in range(sources):
        for j, ref in enumerate(pieces):
            row = (src * len(pieces) + j) * padded
            h_scr[row:row + capacity, :] = ref[src * capacity:(src + 1) * capacity, :].astype(jnp.float32)

    slot_iota = lax.broadcasted_iota(jnp.int32, (padded, tok_ref.shape[1]), 0)
    for blk in range(blocks):
        hit = sel_ref[blk, 0] == slot_iota
        sel = hit.astype(jnp.bfloat16)
        rows = jnp.dot(sel, tok_ref[blk], preferred_element_type=jnp.float32)
        gate = jnp.sum(jnp.where(hit, gate_ref[blk, 0], 0.0), axis=1, keepdims=True)
        g_scr[blk * padded:(blk + 1) * padded, :] = rows
        s_scr[blk * padded:(blk + 1) * padded, :] = (
            (gate * rows).astype(jnp.bfloat16).astype(jnp.float32)
        )

    h = h_scr[...].astype(jnp.bfloat16)
    part = lax.dot_general(
        h, s_scr[...].astype(jnp.bfloat16), (((0,), (0,)), ((), ())),
        preferred_element_type=jnp.float32,
    )

    @pl.when(chunk == 0)
    def _():
        wg_ref[0] = part

    @pl.when(chunk != 0)
    def _():
        wg_ref[0] = wg_ref[0] + part

    out = jnp.dot(h, w_ref[0], preferred_element_type=jnp.float32)
    col = jnp.sum(g_scr[...] * out, axis=1, keepdims=True)
    wide = jnp.broadcast_to(col, (col.shape[0], 128))
    slot_ref[0] = jnp.transpose(wide)[0:1, :]


def expert_kernel(pieces, tokens, slot_row, gate_row, weight, padded, shape):
    local_count, _, source_count, capacity, hidden_width = shape
    col_width = tokens.shape[2]
    block_count, _, _, tok_rows = slot_row.shape
    per_source = block_count // source_count
    chunk = source_count
    for size in (4, 2, 1):
        if source_count % size == 0:
            chunk = size
            break
    steps = source_count // chunk
    blocks = chunk * per_source
    rows = blocks * padded
    piece_spec = pl.BlockSpec(
        (chunk * capacity, hidden_width), lambda l, r: (l * steps + r, 0)
    )
    return pl.pallas_call(
        expert_body,
        grid=(local_count, steps),
        in_specs=[piece_spec] * len(pieces) + [
            pl.BlockSpec((blocks, tok_rows, col_width), lambda l, r: (r, 0, 0)),
            pl.BlockSpec((blocks, 1, 1, tok_rows), lambda l, r: (r, l, 0, 0)),
            pl.BlockSpec((blocks, 1, 1, tok_rows), lambda l, r: (r, l, 0, 0)),
            pl.BlockSpec((1, hidden_width, col_width), lambda l, r: (l, 0, 0)),
        ],
        out_specs=[
            pl.BlockSpec((1, hidden_width, col_width), lambda l, r: (l, 0, 0)),
            pl.BlockSpec((1, 1, rows), lambda l, r: (l, 0, r)),
        ],
        out_shape=[
            jax.ShapeDtypeStruct((local_count, hidden_width, col_width), jnp.float32),
            jax.ShapeDtypeStruct((local_count, 1, block_count * padded), jnp.float32),
        ],
        scratch_shapes=[
            pltpu.VMEM((rows, hidden_width), jnp.float32),
            pltpu.VMEM((rows, col_width), jnp.float32),
            pltpu.VMEM((rows, col_width), jnp.float32),
        ],
    )(*pieces, tokens, slot_row, gate_row, weight)


def per_device(out_grad, gate_weights, expert_ids, hidden, down_weight):
    tok_rows, top_count = expert_ids.shape
    row_width = out_grad.shape[1]
    local_count = hidden.shape[0]
    capacity = hidden.shape[3]
    hidden_width = hidden.shape[4]
    peer_count = lax.axis_size("expert")
    shards = lax.axis_size("dp")
    expert_count = local_count * peer_count
    col_width = row_width // shards
    block_count = peer_count * shards
    f32 = jnp.float32
    bf16 = jnp.bfloat16
    my_dp = lax.axis_index("dp")

    meta = jnp.concatenate([expert_ids.astype(bf16), gate_weights], axis=1).reshape(-1)
    meta_len = meta.shape[0]
    meta_rows = -(-meta_len // col_width)
    meta = jnp.pad(meta, (0, meta_rows * col_width - meta_len)).reshape(meta_rows, 1, col_width)
    cols = out_grad.reshape(tok_rows, shards, col_width)
    cols = jnp.concatenate([cols, jnp.broadcast_to(meta, (meta_rows, shards, col_width))], axis=0)
    cols = lax.all_to_all(cols, "dp", split_axis=1, concat_axis=0, tiled=True)
    cols = cols.reshape(shards, tok_rows + meta_rows, col_width)
    piece_xor = jnp.array([0, 2, 1, 3], jnp.int32)
    cols = jnp.take(cols, piece_xor ^ my_dp, axis=0)

    hidden_shape = hidden.shape
    hidden = hidden.reshape(-1, hidden_width)
    hidden_sent, cols = lax.optimization_barrier((hidden, cols))
    near = lax.ppermute(hidden_sent, "dp", [(j, j ^ 1) for j in range(shards)])
    far = lax.ppermute(hidden_sent, "dp", [(j, j ^ 2) for j in range(shards)])
    near_far = lax.ppermute(far, "dp", [(j, j ^ 1) for j in range(shards)])
    got = lax.all_gather(cols, "expert", axis=0, tiled=False)
    got = got.reshape(block_count, tok_rows + meta_rows, col_width)
    grad_all = got[:, :tok_rows]
    meta_all = got[:, tok_rows:].reshape(block_count, meta_rows * col_width)[:, :meta_len]
    meta_all = meta_all.reshape(block_count, tok_rows, 2 * top_count)
    ids_all = meta_all[:, :, :top_count].astype(jnp.int32)
    gate_all = meta_all[:, :, top_count:]

    my_experts = lax.axis_index("expert") * local_count + jnp.arange(local_count, dtype=jnp.int32)
    hit = ids_all[:, :, :, None] == my_experts[None, None, None, :]
    chose = jnp.any(hit, axis=2)
    gate_hit = jnp.sum(jnp.where(hit, gate_all.astype(f32)[:, :, :, None], 0.0), axis=2)
    before = (jnp.arange(tok_rows)[:, None] < jnp.arange(tok_rows)[None, :]).astype(bf16)
    rank = jnp.einsum(
        "bul,ut->btl", chose.astype(bf16), before, preferred_element_type=f32
    ).astype(jnp.int32)
    padded = -(-capacity // 8) * 8
    slot_ids = jnp.arange(padded, dtype=jnp.int32)
    chose_t = chose.transpose(0, 2, 1)
    rank_t = rank.transpose(0, 2, 1)
    gate_t = gate_hit.transpose(0, 2, 1)
    slot_row = jnp.where(chose_t, rank_t, -1)[:, :, None, :]
    gate_row = gate_t[:, :, None, :]
    weight_grad, slot_part = expert_kernel(
        (hidden, far, near, near_far), got, slot_row, gate_row, down_weight, padded, hidden_shape
    )
    slot_part = slot_part.reshape(local_count, block_count, padded)[:, :, :capacity]
    slot_part = slot_part.transpose(1, 0, 2).reshape(peer_count, shards, local_count, capacity)
    piece_of = jnp.array([0, 2, 1, 3], jnp.int32)[jnp.arange(shards, dtype=jnp.int32) ^ my_dp]
    slot_part = jnp.take(slot_part, piece_of, axis=1)
    send_back = slot_part.reshape(block_count, local_count, capacity)
    returned = lax.all_to_all(
        send_back, ("expert", "dp"), split_axis=0, concat_axis=0, tiled=True
    )
    returned = returned.reshape(peer_count, shards, local_count, capacity)
    slot_grad = jnp.sum(returned, axis=1).reshape(expert_count, capacity)

    own_hit = expert_ids[:, :, None] == jnp.arange(expert_count, dtype=jnp.int32)[None, None, :]
    own_chose = jnp.any(own_hit, axis=1)
    own_rank = jnp.einsum(
        "ue,ut->te", own_chose.astype(bf16), before, preferred_element_type=f32
    ).astype(jnp.int32)
    own_slot = jnp.sum(jnp.where(own_hit, own_rank[:, None, :], 0), axis=2)
    by_slot = jnp.sum(jnp.where(own_hit[:, :, :, None], slot_grad[None, None], 0.0), axis=2)
    gate_grad = jnp.sum(
        jnp.where(own_slot[:, :, None] == slot_ids[None, None, :capacity], by_slot, 0.0), axis=2
    )
    return (weight_grad, gate_grad)


def solution(mesh):
    return jax.shard_map(
        per_device,
        mesh=mesh,
        in_specs=(
            P(("groups", "expert", "dp"), None),
            P(("groups", "expert", "dp"), None),
            P(("groups", "expert", "dp"), None),
            P("expert", ("groups", "dp"), None, None, None),
            P("expert", None, "dp"),
        ),
        out_specs=(P(("groups", "expert"), None, "dp"), P(("groups", "expert", "dp"), None)),
        check_vma=False,
    )
```

```python
import jax
import jax.numpy as jnp
from jax import lax
from jax.experimental import pallas as pl
from jax.experimental.pallas import tpu as pltpu
from jax.sharding import PartitionSpec as P


def expert_body(own_ref, far_ref, near_ref, near_far_ref, tok_ref, sel_ref, gate_ref, w_ref,
                wg_ref, slot_ref, h_scr, s_scr, g_scr):
    expert = pl.program_id(0)
    chunk = pl.program_id(1)
    blocks = sel_ref.shape[0]
    padded = s_scr.shape[0] // blocks
    sources = blocks // 4
    capacity = own_ref.shape[0] // sources
    col_width = tok_ref.shape[2]
    pieces = (own_ref, far_ref, near_ref, near_far_ref)

    @pl.when((expert == 0) & (chunk == 0))
    def _():
        h_scr[...] = jnp.zeros(h_scr.shape, h_scr.dtype)

    my_dp = lax.axis_index("dp")
    for src in range(sources):
        for j, ref in enumerate(pieces):
            replica = my_dp ^ (0, 2, 1, 3)[j]
            row = pl.multiple_of((src * len(pieces) + replica) * padded, 8)
            h_scr[pl.ds(row, capacity), :] = ref[src * capacity:(src + 1) * capacity, :].astype(jnp.float32)

    slot_iota = lax.broadcasted_iota(jnp.int32, (padded, tok_ref.shape[1]), 0)
    for blk in range(blocks):
        hit = sel_ref[blk, 0] == slot_iota
        sel = hit.astype(jnp.bfloat16)
        rows = jnp.dot(sel, tok_ref[blk], preferred_element_type=jnp.float32)
        gate = jnp.sum(jnp.where(hit, gate_ref[blk, 0], 0.0), axis=1, keepdims=True)
        g_scr[blk * padded:(blk + 1) * padded, :] = rows
        s_scr[blk * padded:(blk + 1) * padded, :] = (
            (gate * rows).astype(jnp.bfloat16).astype(jnp.float32)
        )

    h = h_scr[...].astype(jnp.bfloat16)
    part = lax.dot_general(
        h, s_scr[...].astype(jnp.bfloat16), (((0,), (0,)), ((), ())),
        preferred_element_type=jnp.float32,
    )

    @pl.when(chunk == 0)
    def _():
        wg_ref[0] = part

    @pl.when(chunk != 0)
    def _():
        wg_ref[0] = wg_ref[0] + part

    out = jnp.dot(h, w_ref[0], preferred_element_type=jnp.float32)
    col = jnp.sum(g_scr[...] * out, axis=1, keepdims=True)
    wide = jnp.broadcast_to(col, (col.shape[0], 128))
    slot_ref[0] = jnp.transpose(wide)[0:1, :]


def expert_kernel(pieces, tokens, slot_row, gate_row, weight, padded, shape):
    local_count, _, source_count, capacity, hidden_width = shape
    col_width = tokens.shape[2]
    block_count, _, _, tok_rows = slot_row.shape
    per_source = block_count // source_count
    chunk = source_count
    for size in (4, 2, 1):
        if source_count % size == 0:
            chunk = size
            break
    steps = source_count // chunk
    blocks = chunk * per_source
    rows = blocks * padded
    piece_spec = pl.BlockSpec(
        (chunk * capacity, hidden_width), lambda l, r: (l * steps + r, 0)
    )
    return pl.pallas_call(
        expert_body,
        grid=(local_count, steps),
        in_specs=[piece_spec] * len(pieces) + [
            pl.BlockSpec((blocks, tok_rows, col_width), lambda l, r: (r, 0, 0)),
            pl.BlockSpec((blocks, 1, 1, tok_rows), lambda l, r: (r, l, 0, 0)),
            pl.BlockSpec((blocks, 1, 1, tok_rows), lambda l, r: (r, l, 0, 0)),
            pl.BlockSpec((1, hidden_width, col_width), lambda l, r: (l, 0, 0)),
        ],
        out_specs=[
            pl.BlockSpec((1, hidden_width, col_width), lambda l, r: (l, 0, 0)),
            pl.BlockSpec((1, 1, rows), lambda l, r: (l, 0, r)),
        ],
        out_shape=[
            jax.ShapeDtypeStruct((local_count, hidden_width, col_width), jnp.float32),
            jax.ShapeDtypeStruct((local_count, 1, block_count * padded), jnp.float32),
        ],
        scratch_shapes=[
            pltpu.VMEM((rows, hidden_width), jnp.float32),
            pltpu.VMEM((rows, col_width), jnp.float32),
            pltpu.VMEM((rows, col_width), jnp.float32),
        ],
    )(*pieces, tokens, slot_row, gate_row, weight)


def per_device(out_grad, gate_weights, expert_ids, hidden, down_weight):
    tok_rows, top_count = expert_ids.shape
    row_width = out_grad.shape[1]
    local_count = hidden.shape[0]
    capacity = hidden.shape[3]
    hidden_width = hidden.shape[4]
    peer_count = lax.axis_size("expert")
    shards = lax.axis_size("dp")
    expert_count = local_count * peer_count
    col_width = row_width // shards
    block_count = peer_count * shards
    f32 = jnp.float32
    bf16 = jnp.bfloat16
    my_dp = lax.axis_index("dp")

    meta = jnp.concatenate([expert_ids.astype(bf16), gate_weights], axis=1).reshape(-1)
    meta_len = meta.shape[0]
    meta_rows = -(-meta_len // col_width)
    meta = jnp.pad(meta, (0, meta_rows * col_width - meta_len)).reshape(meta_rows, 1, col_width)
    cols = out_grad.reshape(tok_rows, shards, col_width)
    cols = jnp.concatenate([cols, jnp.broadcast_to(meta, (meta_rows, shards, col_width))], axis=0)
    cols = lax.all_to_all(cols, "dp", split_axis=1, concat_axis=0, tiled=True)
    cols = cols.reshape(shards, tok_rows + meta_rows, col_width)

    hidden_shape = hidden.shape
    hidden = hidden.reshape(-1, hidden_width)
    hidden_sent, cols = lax.optimization_barrier((hidden, cols))
    near = lax.ppermute(hidden_sent, "dp", [(j, j ^ 1) for j in range(shards)])
    far = lax.ppermute(hidden_sent, "dp", [(j, j ^ 2) for j in range(shards)])
    near_far = lax.ppermute(far, "dp", [(j, j ^ 1) for j in range(shards)])
    got = lax.all_gather(cols, "expert", axis=0, tiled=False)
    got = got.reshape(block_count, tok_rows + meta_rows, col_width)
    grad_all = got[:, :tok_rows]
    meta_all = got[:, tok_rows:].reshape(block_count, meta_rows * col_width)[:, :meta_len]
    meta_all = meta_all.reshape(block_count, tok_rows, 2 * top_count)
    ids_all = meta_all[:, :, :top_count].astype(jnp.int32)
    gate_all = meta_all[:, :, top_count:]

    my_experts = lax.axis_index("expert") * local_count + jnp.arange(local_count, dtype=jnp.int32)
    hit = ids_all[:, :, :, None] == my_experts[None, None, None, :]
    chose = jnp.any(hit, axis=2)
    gate_hit = jnp.sum(jnp.where(hit, gate_all.astype(f32)[:, :, :, None], 0.0), axis=2)
    before = (jnp.arange(tok_rows)[:, None] < jnp.arange(tok_rows)[None, :]).astype(bf16)
    rank = jnp.einsum(
        "bul,ut->btl", chose.astype(bf16), before, preferred_element_type=f32
    ).astype(jnp.int32)
    padded = -(-capacity // 8) * 8
    slot_ids = jnp.arange(padded, dtype=jnp.int32)
    chose_t = chose.transpose(0, 2, 1)
    rank_t = rank.transpose(0, 2, 1)
    gate_t = gate_hit.transpose(0, 2, 1)
    slot_row = jnp.where(chose_t, rank_t, -1)[:, :, None, :]
    gate_row = gate_t[:, :, None, :]
    weight_grad, slot_part = expert_kernel(
        (hidden, far, near, near_far), got, slot_row, gate_row, down_weight, padded, hidden_shape
    )
    slot_part = slot_part.reshape(local_count, block_count, padded)[:, :, :capacity]
    slot_part = slot_part.transpose(1, 0, 2).reshape(peer_count, shards, local_count, capacity)
    send_back = slot_part.reshape(block_count, local_count, capacity)
    returned = lax.all_to_all(
        send_back, ("expert", "dp"), split_axis=0, concat_axis=0, tiled=True
    )
    returned = returned.reshape(peer_count, shards, local_count, capacity)
    slot_grad = jnp.sum(returned, axis=1).reshape(expert_count, capacity)

    own_hit = expert_ids[:, :, None] == jnp.arange(expert_count, dtype=jnp.int32)[None, None, :]
    own_chose = jnp.any(own_hit, axis=1)
    own_rank = jnp.einsum(
        "ue,ut->te", own_chose.astype(bf16), before, preferred_element_type=f32
    ).astype(jnp.int32)
    own_slot = jnp.sum(jnp.where(own_hit, own_rank[:, None, :], 0), axis=2)
    by_slot = jnp.sum(jnp.where(own_hit[:, :, :, None], slot_grad[None, None], 0.0), axis=2)
    gate_grad = jnp.sum(
        jnp.where(own_slot[:, :, None] == slot_ids[None, None, :capacity], by_slot, 0.0), axis=2
    )
    return (weight_grad, gate_grad)


def solution(mesh):
    return jax.shard_map(
        per_device,
        mesh=mesh,
        in_specs=(
            P(("groups", "expert", "dp"), None),
            P(("groups", "expert", "dp"), None),
            P(("groups", "expert", "dp"), None),
            P("expert", ("groups", "dp"), None, None, None),
            P("expert", None, "dp"),
        ),
        out_specs=(P(("groups", "expert"), None, "dp"), P(("groups", "expert", "dp"), None)),
        check_vma=False,
    )
```

```python
import jax
import jax.numpy as jnp
from jax import lax
from jax.experimental import pallas as pl
from jax.experimental.pallas import tpu as pltpu
from jax.sharding import PartitionSpec as P


def expert_body(own_ref, far_ref, near_ref, near_far_ref, tok_ref, sel_ref, gate_ref, w_ref,
                wg_ref, slot_ref, h_scr, s_scr, g_scr):
    expert = pl.program_id(0)
    chunk = pl.program_id(1)
    blocks = sel_ref.shape[0]
    padded = s_scr.shape[0] // blocks
    sources = blocks // 4
    capacity = own_ref.shape[0] // sources
    col_width = tok_ref.shape[2]
    pieces = (own_ref, far_ref, near_ref, near_far_ref)

    @pl.when((expert == 0) & (chunk == 0))
    def _():
        h_scr[...] = jnp.zeros(h_scr.shape, h_scr.dtype)

    for src in range(sources):
        for j, ref in enumerate(pieces):
            row = (src * len(pieces) + j) * padded
            h_scr[row:row + capacity, :] = ref[src * capacity:(src + 1) * capacity, :]

    slot_iota = lax.broadcasted_iota(jnp.int32, (padded, tok_ref.shape[1]), 0)
    for blk in range(blocks):
        hit = sel_ref[blk, 0] == slot_iota
        sel = hit.astype(jnp.bfloat16)
        rows = jnp.dot(sel, tok_ref[blk], preferred_element_type=jnp.float32)
        gate = jnp.sum(jnp.where(hit, gate_ref[blk, 0], 0.0), axis=1, keepdims=True)
        g_scr[blk * padded:(blk + 1) * padded, :] = rows
        s_scr[blk * padded:(blk + 1) * padded, :] = (
            (gate * rows).astype(jnp.bfloat16).astype(jnp.float32)
        )

    h = h_scr[...]
    part = lax.dot_general(
        h, s_scr[...].astype(jnp.bfloat16), (((0,), (0,)), ((), ())),
        preferred_element_type=jnp.float32,
    )

    @pl.when(chunk == 0)
    def _():
        wg_ref[0] = part

    @pl.when(chunk != 0)
    def _():
        wg_ref[0] = wg_ref[0] + part

    out = jnp.dot(h, w_ref[0], preferred_element_type=jnp.float32)
    col = jnp.sum(g_scr[...] * out, axis=1, keepdims=True)
    wide = jnp.broadcast_to(col, (col.shape[0], 128))
    slot_ref[0] = jnp.transpose(wide)[0:1, :]


def expert_kernel(pieces, tokens, slot_row, gate_row, weight, padded, shape):
    local_count, _, source_count, capacity, hidden_width = shape
    col_width = tokens.shape[2]
    block_count, _, _, tok_rows = slot_row.shape
    per_source = block_count // source_count
    chunk = source_count
    for size in (4, 2, 1):
        if source_count % size == 0:
            chunk = size
            break
    steps = source_count // chunk
    blocks = chunk * per_source
    rows = blocks * padded
    piece_spec = pl.BlockSpec(
        (chunk * capacity, hidden_width), lambda l, r: (l * steps + r, 0)
    )
    return pl.pallas_call(
        expert_body,
        grid=(local_count, steps),
        in_specs=[piece_spec] * len(pieces) + [
            pl.BlockSpec((blocks, tok_rows, col_width), lambda l, r: (r, 0, 0)),
            pl.BlockSpec((blocks, 1, 1, tok_rows), lambda l, r: (r, l, 0, 0)),
            pl.BlockSpec((blocks, 1, 1, tok_rows), lambda l, r: (r, l, 0, 0)),
            pl.BlockSpec((1, hidden_width, col_width), lambda l, r: (l, 0, 0)),
        ],
        out_specs=[
            pl.BlockSpec((1, hidden_width, col_width), lambda l, r: (l, 0, 0)),
            pl.BlockSpec((1, 1, rows), lambda l, r: (l, 0, r)),
        ],
        out_shape=[
            jax.ShapeDtypeStruct((local_count, hidden_width, col_width), jnp.float32),
            jax.ShapeDtypeStruct((local_count, 1, block_count * padded), jnp.float32),
        ],
        scratch_shapes=[
            pltpu.VMEM((rows, hidden_width), jnp.bfloat16),
            pltpu.VMEM((rows, col_width), jnp.float32),
            pltpu.VMEM((rows, col_width), jnp.float32),
        ],
    )(*pieces, tokens, slot_row, gate_row, weight)


def per_device(out_grad, gate_weights, expert_ids, hidden, down_weight):
    tok_rows, top_count = expert_ids.shape
    row_width = out_grad.shape[1]
    local_count = hidden.shape[0]
    capacity = hidden.shape[3]
    hidden_width = hidden.shape[4]
    peer_count = lax.axis_size("expert")
    shards = lax.axis_size("dp")
    expert_count = local_count * peer_count
    col_width = row_width // shards
    block_count = peer_count * shards
    f32 = jnp.float32
    bf16 = jnp.bfloat16
    my_dp = lax.axis_index("dp")

    meta = jnp.concatenate([expert_ids.astype(bf16), gate_weights], axis=1).reshape(-1)
    meta_len = meta.shape[0]
    meta_rows = -(-meta_len // col_width)
    meta = jnp.pad(meta, (0, meta_rows * col_width - meta_len)).reshape(meta_rows, 1, col_width)
    cols = out_grad.reshape(tok_rows, shards, col_width)
    cols = jnp.concatenate([cols, jnp.broadcast_to(meta, (meta_rows, shards, col_width))], axis=0)
    cols = lax.all_to_all(cols, "dp", split_axis=1, concat_axis=0, tiled=True)
    cols = cols.reshape(shards, tok_rows + meta_rows, col_width)
    piece_xor = jnp.array([0, 2, 1, 3], jnp.int32)
    cols = jnp.take(cols, piece_xor ^ my_dp, axis=0)

    hidden_shape = hidden.shape
    hidden = hidden.reshape(-1, hidden_width)
    hidden_sent, cols = lax.optimization_barrier((hidden, cols))
    near = lax.ppermute(hidden_sent, "dp", [(j, j ^ 1) for j in range(shards)])
    far = lax.ppermute(hidden_sent, "dp", [(j, j ^ 2) for j in range(shards)])
    near_far = lax.ppermute(far, "dp", [(j, j ^ 1) for j in range(shards)])
    got = lax.all_gather(cols, "expert", axis=0, tiled=False)
    got = got.reshape(block_count, tok_rows + meta_rows, col_width)
    grad_all = got[:, :tok_rows]
    meta_all = got[:, tok_rows:].reshape(block_count, meta_rows * col_width)[:, :meta_len]
    meta_all = meta_all.reshape(block_count, tok_rows, 2 * top_count)
    ids_all = meta_all[:, :, :top_count].astype(jnp.int32)
    gate_all = meta_all[:, :, top_count:]

    my_experts = lax.axis_index("expert") * local_count + jnp.arange(local_count, dtype=jnp.int32)
    hit = ids_all[:, :, :, None] == my_experts[None, None, None, :]
    chose = jnp.any(hit, axis=2)
    gate_hit = jnp.sum(jnp.where(hit, gate_all.astype(f32)[:, :, :, None], 0.0), axis=2)
    before = (jnp.arange(tok_rows)[:, None] < jnp.arange(tok_rows)[None, :]).astype(bf16)
    rank = jnp.einsum(
        "bul,ut->btl", chose.astype(bf16), before, preferred_element_type=f32
    ).astype(jnp.int32)
    padded = -(-capacity // 8) * 8
    slot_ids = jnp.arange(padded, dtype=jnp.int32)
    chose_t = chose.transpose(0, 2, 1)
    rank_t = rank.transpose(0, 2, 1)
    gate_t = gate_hit.transpose(0, 2, 1)
    slot_row = jnp.where(chose_t, rank_t, -1)[:, :, None, :]
    gate_row = gate_t[:, :, None, :]
    weight_grad, slot_part = expert_kernel(
        (hidden, far, near, near_far), got, slot_row, gate_row, down_weight, padded, hidden_shape
    )
    slot_part = slot_part.reshape(local_count, block_count, padded)[:, :, :capacity]
    slot_part = slot_part.transpose(1, 0, 2).reshape(peer_count, shards, local_count, capacity)
    piece_of = jnp.array([0, 2, 1, 3], jnp.int32)[jnp.arange(shards, dtype=jnp.int32) ^ my_dp]
    slot_part = jnp.take(slot_part, piece_of, axis=1)
    send_back = slot_part.reshape(block_count, local_count, capacity)
    returned = lax.all_to_all(
        send_back, ("expert", "dp"), split_axis=0, concat_axis=0, tiled=True
    )
    returned = returned.reshape(peer_count, shards, local_count, capacity)
    slot_grad = jnp.sum(returned, axis=1).reshape(expert_count, capacity)

    own_hit = expert_ids[:, :, None] == jnp.arange(expert_count, dtype=jnp.int32)[None, None, :]
    own_chose = jnp.any(own_hit, axis=1)
    own_rank = jnp.einsum(
        "ue,ut->te", own_chose.astype(bf16), before, preferred_element_type=f32
    ).astype(jnp.int32)
    own_slot = jnp.sum(jnp.where(own_hit, own_rank[:, None, :], 0), axis=2)
    by_slot = jnp.sum(jnp.where(own_hit[:, :, :, None], slot_grad[None, None], 0.0), axis=2)
    gate_grad = jnp.sum(
        jnp.where(own_slot[:, :, None] == slot_ids[None, None, :capacity], by_slot, 0.0), axis=2
    )
    return (weight_grad, gate_grad)


def solution(mesh):
    return jax.shard_map(
        per_device,
        mesh=mesh,
        in_specs=(
            P(("groups", "expert", "dp"), None),
            P(("groups", "expert", "dp"), None),
            P(("groups", "expert", "dp"), None),
            P("expert", ("groups", "dp"), None, None, None),
            P("expert", None, "dp"),
        ),
        out_specs=(P(("groups", "expert"), None, "dp"), P(("groups", "expert", "dp"), None)),
        check_vma=False,
    )
```

```python
import jax
import jax.numpy as jnp
from jax import lax
from jax.experimental import pallas as pl
from jax.experimental.pallas import tpu as pltpu
from jax.sharding import PartitionSpec as P


def expert_body(own_ref, far_ref, near_ref, near_far_ref, tok_ref, sel_ref, gate_ref, w_ref,
                wg_ref, slot_ref, h_scr, s_scr, g_scr):
    expert = pl.program_id(0)
    chunk = pl.program_id(1)
    blocks = sel_ref.shape[0]
    padded = s_scr.shape[0] // blocks
    sources = blocks // 4
    capacity = own_ref.shape[0] // sources
    col_width = tok_ref.shape[2]
    pieces = (own_ref, far_ref, near_ref, near_far_ref)

    @pl.when((expert == 0) & (chunk == 0))
    def _():
        h_scr[...] = jnp.zeros(h_scr.shape, h_scr.dtype)

    for src in range(sources):
        for j, ref in enumerate(pieces):
            row = (src * len(pieces) + j) * padded
            h_scr[row:row + capacity, :] = ref[src * capacity:(src + 1) * capacity, :]

    slot_iota = lax.broadcasted_iota(jnp.int32, (padded, tok_ref.shape[1]), 0)
    for blk in range(blocks):
        hit = sel_ref[blk, 0] == slot_iota
        sel = hit.astype(jnp.bfloat16)
        rows = jnp.dot(sel, tok_ref[blk], preferred_element_type=jnp.float32)
        gate = jnp.sum(jnp.where(hit, gate_ref[blk, 0], 0.0), axis=1, keepdims=True)
        g_scr[blk * padded:(blk + 1) * padded, :] = rows
        s_scr[blk * padded:(blk + 1) * padded, :] = (gate * rows).astype(jnp.bfloat16)

    h = h_scr[...]
    part = lax.dot_general(
        h, s_scr[...], (((0,), (0,)), ((), ())),
        preferred_element_type=jnp.float32,
    )

    @pl.when(chunk == 0)
    def _():
        wg_ref[0] = part

    @pl.when(chunk != 0)
    def _():
        wg_ref[0] = wg_ref[0] + part

    out = jnp.dot(h, w_ref[0], preferred_element_type=jnp.float32)
    col = jnp.sum(g_scr[...] * out, axis=1, keepdims=True)
    wide = jnp.broadcast_to(col, (col.shape[0], 128))
    slot_ref[0] = jnp.transpose(wide)[0:1, :]


def expert_kernel(pieces, tokens, slot_row, gate_row, weight, padded, shape):
    local_count, _, source_count, capacity, hidden_width = shape
    col_width = tokens.shape[2]
    block_count, _, _, tok_rows = slot_row.shape
    per_source = block_count // source_count
    chunk = source_count
    for size in (4, 2, 1):
        if source_count % size == 0:
            chunk = size
            break
    steps = source_count // chunk
    blocks = chunk * per_source
    rows = blocks * padded
    piece_spec = pl.BlockSpec(
        (chunk * capacity, hidden_width), lambda l, r: (l * steps + r, 0)
    )
    return pl.pallas_call(
        expert_body,
        grid=(local_count, steps),
        in_specs=[piece_spec] * len(pieces) + [
            pl.BlockSpec((blocks, tok_rows, col_width), lambda l, r: (r, 0, 0)),
            pl.BlockSpec((blocks, 1, 1, tok_rows), lambda l, r: (r, l, 0, 0)),
            pl.BlockSpec((blocks, 1, 1, tok_rows), lambda l, r: (r, l, 0, 0)),
            pl.BlockSpec((1, hidden_width, col_width), lambda l, r: (l, 0, 0)),
        ],
        out_specs=[
            pl.BlockSpec((1, hidden_width, col_width), lambda l, r: (l, 0, 0)),
            pl.BlockSpec((1, 1, rows), lambda l, r: (l, 0, r)),
        ],
        out_shape=[
            jax.ShapeDtypeStruct((local_count, hidden_width, col_width), jnp.float32),
            jax.ShapeDtypeStruct((local_count, 1, block_count * padded), jnp.float32),
        ],
        scratch_shapes=[
            pltpu.VMEM((rows, hidden_width), jnp.bfloat16),
            pltpu.VMEM((rows, col_width), jnp.bfloat16),
            pltpu.VMEM((rows, col_width), jnp.float32),
        ],
    )(*pieces, tokens, slot_row, gate_row, weight)


def per_device(out_grad, gate_weights, expert_ids, hidden, down_weight):
    tok_rows, top_count = expert_ids.shape
    row_width = out_grad.shape[1]
    local_count = hidden.shape[0]
    capacity = hidden.shape[3]
    hidden_width = hidden.shape[4]
    peer_count = lax.axis_size("expert")
    shards = lax.axis_size("dp")
    expert_count = local_count * peer_count
    col_width = row_width // shards
    block_count = peer_count * shards
    f32 = jnp.float32
    bf16 = jnp.bfloat16
    my_dp = lax.axis_index("dp")

    meta = jnp.concatenate([expert_ids.astype(bf16), gate_weights], axis=1).reshape(-1)
    meta_len = meta.shape[0]
    meta_rows = -(-meta_len // col_width)
    meta = jnp.pad(meta, (0, meta_rows * col_width - meta_len)).reshape(meta_rows, 1, col_width)
    cols = out_grad.reshape(tok_rows, shards, col_width)
    cols = jnp.concatenate([cols, jnp.broadcast_to(meta, (meta_rows, shards, col_width))], axis=0)
    cols = lax.all_to_all(cols, "dp", split_axis=1, concat_axis=0, tiled=True)
    cols = cols.reshape(shards, tok_rows + meta_rows, col_width)
    piece_xor = jnp.array([0, 2, 1, 3], jnp.int32)
    cols = jnp.take(cols, piece_xor ^ my_dp, axis=0)

    hidden_shape = hidden.shape
    hidden = hidden.reshape(-1, hidden_width)
    hidden_sent, cols = lax.optimization_barrier((hidden, cols))
    near = lax.ppermute(hidden_sent, "dp", [(j, j ^ 1) for j in range(shards)])
    far = lax.ppermute(hidden_sent, "dp", [(j, j ^ 2) for j in range(shards)])
    near_far = lax.ppermute(far, "dp", [(j, j ^ 1) for j in range(shards)])
    got = lax.all_gather(cols, "expert", axis=0, tiled=False)
    got = got.reshape(block_count, tok_rows + meta_rows, col_width)
    grad_all = got[:, :tok_rows]
    meta_all = got[:, tok_rows:].reshape(block_count, meta_rows * col_width)[:, :meta_len]
    meta_all = meta_all.reshape(block_count, tok_rows, 2 * top_count)
    ids_all = meta_all[:, :, :top_count].astype(jnp.int32)
    gate_all = meta_all[:, :, top_count:]

    my_experts = lax.axis_index("expert") * local_count + jnp.arange(local_count, dtype=jnp.int32)
    hit = ids_all[:, :, :, None] == my_experts[None, None, None, :]
    chose = jnp.any(hit, axis=2)
    gate_hit = jnp.sum(jnp.where(hit, gate_all.astype(f32)[:, :, :, None], 0.0), axis=2)
    before = (jnp.arange(tok_rows)[:, None] < jnp.arange(tok_rows)[None, :]).astype(bf16)
    rank = jnp.einsum(
        "bul,ut->btl", chose.astype(bf16), before, preferred_element_type=f32
    ).astype(jnp.int32)
    padded = -(-capacity // 8) * 8
    slot_ids = jnp.arange(padded, dtype=jnp.int32)
    chose_t = chose.transpose(0, 2, 1)
    rank_t = rank.transpose(0, 2, 1)
    gate_t = gate_hit.transpose(0, 2, 1)
    slot_row = jnp.where(chose_t, rank_t, -1)[:, :, None, :]
    gate_row = gate_t[:, :, None, :]
    weight_grad, slot_part = expert_kernel(
        (hidden, far, near, near_far), got, slot_row, gate_row, down_weight, padded, hidden_shape
    )
    slot_part = slot_part.reshape(local_count, block_count, padded)[:, :, :capacity]
    slot_part = slot_part.transpose(1, 0, 2).reshape(peer_count, shards, local_count, capacity)
    piece_of = jnp.array([0, 2, 1, 3], jnp.int32)[jnp.arange(shards, dtype=jnp.int32) ^ my_dp]
    slot_part = jnp.take(slot_part, piece_of, axis=1)
    send_back = slot_part.reshape(block_count, local_count, capacity)
    returned = lax.all_to_all(
        send_back, ("expert", "dp"), split_axis=0, concat_axis=0, tiled=True
    )
    returned = returned.reshape(peer_count, shards, local_count, capacity)
    slot_grad = jnp.sum(returned, axis=1).reshape(expert_count, capacity)

    own_hit = expert_ids[:, :, None] == jnp.arange(expert_count, dtype=jnp.int32)[None, None, :]
    own_chose = jnp.any(own_hit, axis=1)
    own_rank = jnp.einsum(
        "ue,ut->te", own_chose.astype(bf16), before, preferred_element_type=f32
    ).astype(jnp.int32)
    own_slot = jnp.sum(jnp.where(own_hit, own_rank[:, None, :], 0), axis=2)
    by_slot = jnp.sum(jnp.where(own_hit[:, :, :, None], slot_grad[None, None], 0.0), axis=2)
    gate_grad = jnp.sum(
        jnp.where(own_slot[:, :, None] == slot_ids[None, None, :capacity], by_slot, 0.0), axis=2
    )
    return (weight_grad, gate_grad)


def solution(mesh):
    return jax.shard_map(
        per_device,
        mesh=mesh,
        in_specs=(
            P(("groups", "expert", "dp"), None),
            P(("groups", "expert", "dp"), None),
            P(("groups", "expert", "dp"), None),
            P("expert", ("groups", "dp"), None, None, None),
            P("expert", None, "dp"),
        ),
        out_specs=(P(("groups", "expert"), None, "dp"), P(("groups", "expert", "dp"), None)),
        check_vma=False,
    )
```

```python
import jax
import jax.numpy as jnp
from jax import lax
from jax.experimental import pallas as pl
from jax.experimental.pallas import tpu as pltpu
from jax.sharding import PartitionSpec as P


def expert_body(own_ref, far_ref, near_ref, near_far_ref, tok_ref, sel_ref, gate_ref, w_ref,
                wg_ref, slot_ref, h_scr, s_scr, g_scr):
    expert = pl.program_id(0)
    chunk = pl.program_id(1)
    blocks = sel_ref.shape[0]
    padded = s_scr.shape[0] // blocks
    sources = blocks // 4
    capacity = own_ref.shape[0] // sources
    col_width = tok_ref.shape[2]
    pieces = (own_ref, far_ref, near_ref, near_far_ref)

    @pl.when((expert == 0) & (chunk == 0))
    def _():
        h_scr[...] = jnp.zeros(h_scr.shape, h_scr.dtype)

    for src in range(sources):
        for j, ref in enumerate(pieces):
            row = (src * len(pieces) + j) * padded
            h_scr[row:row + capacity, :] = ref[src * capacity:(src + 1) * capacity, :]

    slot_iota = lax.broadcasted_iota(jnp.int32, (padded, tok_ref.shape[1]), 0)
    my_dp = lax.axis_index("dp")
    for blk in range(blocks):
        src, j = divmod(blk, len(pieces))
        nat = src * len(pieces) + (my_dp ^ (0, 2, 1, 3)[j])
        hit = sel_ref[nat, 0] == slot_iota
        sel = hit.astype(jnp.bfloat16)
        rows = jnp.dot(sel, tok_ref[nat], preferred_element_type=jnp.float32)
        gate = jnp.sum(jnp.where(hit, gate_ref[nat, 0], 0.0), axis=1, keepdims=True)
        g_scr[blk * padded:(blk + 1) * padded, :] = rows
        s_scr[blk * padded:(blk + 1) * padded, :] = (gate * rows).astype(jnp.bfloat16)

    h = h_scr[...]
    part = lax.dot_general(
        h, s_scr[...], (((0,), (0,)), ((), ())),
        preferred_element_type=jnp.float32,
    )

    @pl.when(chunk == 0)
    def _():
        wg_ref[0] = part

    @pl.when(chunk != 0)
    def _():
        wg_ref[0] = wg_ref[0] + part

    out = jnp.dot(h, w_ref[0], preferred_element_type=jnp.float32)
    col = jnp.sum(g_scr[...] * out, axis=1, keepdims=True)
    wide = jnp.broadcast_to(col, (col.shape[0], 128))
    slot_ref[0] = jnp.transpose(wide)[0:1, :]


def expert_kernel(pieces, tokens, slot_row, gate_row, weight, padded, shape):
    local_count, _, source_count, capacity, hidden_width = shape
    col_width = tokens.shape[2]
    block_count, _, _, tok_rows = slot_row.shape
    per_source = block_count // source_count
    chunk = source_count
    for size in (4, 2, 1):
        if source_count % size == 0:
            chunk = size
            break
    steps = source_count // chunk
    blocks = chunk * per_source
    rows = blocks * padded
    piece_spec = pl.BlockSpec(
        (chunk * capacity, hidden_width), lambda l, r: (l * steps + r, 0)
    )
    return pl.pallas_call(
        expert_body,
        grid=(local_count, steps),
        in_specs=[piece_spec] * len(pieces) + [
            pl.BlockSpec((blocks, tok_rows, col_width), lambda l, r: (r, 0, 0)),
            pl.BlockSpec((blocks, 1, 1, tok_rows), lambda l, r: (r, l, 0, 0)),
            pl.BlockSpec((blocks, 1, 1, tok_rows), lambda l, r: (r, l, 0, 0)),
            pl.BlockSpec((1, hidden_width, col_width), lambda l, r: (l, 0, 0)),
        ],
        out_specs=[
            pl.BlockSpec((1, hidden_width, col_width), lambda l, r: (l, 0, 0)),
            pl.BlockSpec((1, 1, rows), lambda l, r: (l, 0, r)),
        ],
        out_shape=[
            jax.ShapeDtypeStruct((local_count, hidden_width, col_width), jnp.float32),
            jax.ShapeDtypeStruct((local_count, 1, block_count * padded), jnp.float32),
        ],
        scratch_shapes=[
            pltpu.VMEM((rows, hidden_width), jnp.bfloat16),
            pltpu.VMEM((rows, col_width), jnp.bfloat16),
            pltpu.VMEM((rows, col_width), jnp.float32),
        ],
    )(*pieces, tokens, slot_row, gate_row, weight)


def per_device(out_grad, gate_weights, expert_ids, hidden, down_weight):
    tok_rows, top_count = expert_ids.shape
    row_width = out_grad.shape[1]
    local_count = hidden.shape[0]
    capacity = hidden.shape[3]
    hidden_width = hidden.shape[4]
    peer_count = lax.axis_size("expert")
    shards = lax.axis_size("dp")
    expert_count = local_count * peer_count
    col_width = row_width // shards
    block_count = peer_count * shards
    f32 = jnp.float32
    bf16 = jnp.bfloat16
    my_dp = lax.axis_index("dp")

    meta = jnp.concatenate([expert_ids.astype(bf16), gate_weights], axis=1).reshape(-1)
    meta_len = meta.shape[0]
    meta_rows = -(-meta_len // col_width)
    meta = jnp.pad(meta, (0, meta_rows * col_width - meta_len)).reshape(meta_rows, 1, col_width)
    cols = out_grad.reshape(tok_rows, shards, col_width)
    cols = jnp.concatenate([cols, jnp.broadcast_to(meta, (meta_rows, shards, col_width))], axis=0)
    cols = lax.all_to_all(cols, "dp", split_axis=1, concat_axis=0, tiled=True)
    cols = cols.reshape(shards, tok_rows + meta_rows, col_width)

    hidden_shape = hidden.shape
    hidden = hidden.reshape(-1, hidden_width)
    hidden_sent, cols = lax.optimization_barrier((hidden, cols))
    near = lax.ppermute(hidden_sent, "dp", [(j, j ^ 1) for j in range(shards)])
    far = lax.ppermute(hidden_sent, "dp", [(j, j ^ 2) for j in range(shards)])
    near_far = lax.ppermute(far, "dp", [(j, j ^ 1) for j in range(shards)])
    got = lax.all_gather(cols, "expert", axis=0, tiled=False)
    got = got.reshape(block_count, tok_rows + meta_rows, col_width)
    grad_all = got[:, :tok_rows]
    meta_all = got[:, tok_rows:].reshape(block_count, meta_rows * col_width)[:, :meta_len]
    meta_all = meta_all.reshape(block_count, tok_rows, 2 * top_count)
    ids_all = meta_all[:, :, :top_count].astype(jnp.int32)
    gate_all = meta_all[:, :, top_count:]

    my_experts = lax.axis_index("expert") * local_count + jnp.arange(local_count, dtype=jnp.int32)
    hit = ids_all[:, :, :, None] == my_experts[None, None, None, :]
    chose = jnp.any(hit, axis=2)
    gate_hit = jnp.sum(jnp.where(hit, gate_all.astype(f32)[:, :, :, None], 0.0), axis=2)
    before = (jnp.arange(tok_rows)[:, None] < jnp.arange(tok_rows)[None, :]).astype(bf16)
    rank = jnp.einsum(
        "bul,ut->btl", chose.astype(bf16), before, preferred_element_type=f32
    ).astype(jnp.int32)
    padded = -(-capacity // 8) * 8
    slot_ids = jnp.arange(padded, dtype=jnp.int32)
    chose_t = chose.transpose(0, 2, 1)
    rank_t = rank.transpose(0, 2, 1)
    gate_t = gate_hit.transpose(0, 2, 1)
    slot_row = jnp.where(chose_t, rank_t, -1)[:, :, None, :]
    gate_row = gate_t[:, :, None, :]
    weight_grad, slot_part = expert_kernel(
        (hidden, far, near, near_far), got, slot_row, gate_row, down_weight, padded, hidden_shape
    )
    slot_part = slot_part.reshape(local_count, block_count, padded)[:, :, :capacity]
    slot_part = slot_part.transpose(1, 0, 2).reshape(peer_count, shards, local_count, capacity)
    piece_of = jnp.array([0, 2, 1, 3], jnp.int32)[jnp.arange(shards, dtype=jnp.int32) ^ my_dp]
    slot_part = jnp.take(slot_part, piece_of, axis=1)
    send_back = slot_part.reshape(block_count, local_count, capacity)
    returned = lax.all_to_all(
        send_back, ("expert", "dp"), split_axis=0, concat_axis=0, tiled=True
    )
    returned = returned.reshape(peer_count, shards, local_count, capacity)
    slot_grad = jnp.sum(returned, axis=1).reshape(expert_count, capacity)

    own_hit = expert_ids[:, :, None] == jnp.arange(expert_count, dtype=jnp.int32)[None, None, :]
    own_chose = jnp.any(own_hit, axis=1)
    own_rank = jnp.einsum(
        "ue,ut->te", own_chose.astype(bf16), before, preferred_element_type=f32
    ).astype(jnp.int32)
    own_slot = jnp.sum(jnp.where(own_hit, own_rank[:, None, :], 0), axis=2)
    by_slot = jnp.sum(jnp.where(own_hit[:, :, :, None], slot_grad[None, None], 0.0), axis=2)
    gate_grad = jnp.sum(
        jnp.where(own_slot[:, :, None] == slot_ids[None, None, :capacity], by_slot, 0.0), axis=2
    )
    return (weight_grad, gate_grad)


def solution(mesh):
    return jax.shard_map(
        per_device,
        mesh=mesh,
        in_specs=(
            P(("groups", "expert", "dp"), None),
            P(("groups", "expert", "dp"), None),
            P(("groups", "expert", "dp"), None),
            P("expert", ("groups", "dp"), None, None, None),
            P("expert", None, "dp"),
        ),
        out_specs=(P(("groups", "expert"), None, "dp"), P(("groups", "expert", "dp"), None)),
        check_vma=False,
    )
```

```python
import jax
import jax.numpy as jnp
from jax import lax
from jax.experimental import pallas as pl
from jax.experimental.pallas import tpu as pltpu
from jax.sharding import PartitionSpec as P


def expert_body(own_ref, far_ref, near_ref, near_far_ref, tok_ref, sel_ref, gate_ref, w_ref,
                wg_ref, slot_ref, h_scr, s_scr, g_scr):
    expert = pl.program_id(0)
    chunk = pl.program_id(1)
    blocks = sel_ref.shape[0]
    padded = s_scr.shape[0] // blocks
    sources = blocks // 4
    capacity = own_ref.shape[0] // sources
    col_width = tok_ref.shape[2]
    pieces = (own_ref, far_ref, near_ref, near_far_ref)

    @pl.when((expert == 0) & (chunk == 0))
    def _():
        h_scr[...] = jnp.zeros(h_scr.shape, h_scr.dtype)

    for src in range(sources):
        for j, ref in enumerate(pieces):
            row = (src * len(pieces) + j) * padded
            h_scr[row:row + capacity, :] = ref[src * capacity:(src + 1) * capacity, :]

    slot_iota = lax.broadcasted_iota(jnp.int32, (padded, tok_ref.shape[1]), 0)
    for blk in range(blocks):
        hit = sel_ref[blk, 0] == slot_iota
        sel = hit.astype(jnp.bfloat16)
        rows = jnp.dot(sel, tok_ref[blk], preferred_element_type=jnp.float32)
        gate = jnp.sum(jnp.where(hit, gate_ref[blk, 0], 0.0), axis=1, keepdims=True)
        g_scr[blk * padded:(blk + 1) * padded, :] = rows
        s_scr[blk * padded:(blk + 1) * padded, :] = (gate * rows).astype(jnp.bfloat16)

    h = h_scr[...]
    part = lax.dot_general(
        h, s_scr[...], (((0,), (0,)), ((), ())),
        preferred_element_type=jnp.float32,
    )

    @pl.when(chunk == 0)
    def _():
        wg_ref[0] = part

    @pl.when(chunk != 0)
    def _():
        wg_ref[0] = wg_ref[0] + part

    out = jnp.dot(h, w_ref[0], preferred_element_type=jnp.float32)
    col = jnp.sum(g_scr[...] * out, axis=1, keepdims=True)
    wide = jnp.broadcast_to(col, (col.shape[0], 128))
    slot_ref[0] = jnp.transpose(wide)[0:1, :]


def expert_kernel(pieces, tokens, slot_row, gate_row, weight, padded, shape):
    local_count, _, source_count, capacity, hidden_width = shape
    col_width = tokens.shape[2]
    block_count, _, _, tok_rows = slot_row.shape
    per_source = block_count // source_count
    chunk = source_count
    for size in (4, 2, 1):
        if source_count % size == 0:
            chunk = size
            break
    steps = source_count // chunk
    blocks = chunk * per_source
    rows = blocks * padded
    piece_spec = pl.BlockSpec(
        (chunk * capacity, hidden_width), lambda l, r: (l * steps + r, 0)
    )
    return pl.pallas_call(
        expert_body,
        grid=(local_count, steps),
        in_specs=[piece_spec] * len(pieces) + [
            pl.BlockSpec((blocks, tok_rows, col_width), lambda l, r: (r, 0, 0)),
            pl.BlockSpec((blocks, 1, 1, tok_rows), lambda l, r: (r, l, 0, 0)),
            pl.BlockSpec((blocks, 1, 1, tok_rows), lambda l, r: (r, l, 0, 0)),
            pl.BlockSpec((1, hidden_width, col_width), lambda l, r: (l, 0, 0)),
        ],
        out_specs=[
            pl.BlockSpec((1, hidden_width, col_width), lambda l, r: (l, 0, 0)),
            pl.BlockSpec((1, 1, rows), lambda l, r: (l, 0, r)),
        ],
        out_shape=[
            jax.ShapeDtypeStruct((local_count, hidden_width, col_width), jnp.float32),
            jax.ShapeDtypeStruct((local_count, 1, block_count * padded), jnp.float32),
        ],
        scratch_shapes=[
            pltpu.VMEM((rows, hidden_width), jnp.bfloat16),
            pltpu.VMEM((rows, col_width), jnp.bfloat16),
            pltpu.VMEM((rows, col_width), jnp.float32),
        ],
    )(*pieces, tokens, slot_row, gate_row, weight)


def per_device(out_grad, gate_weights, expert_ids, hidden, down_weight):
    tok_rows, top_count = expert_ids.shape
    row_width = out_grad.shape[1]
    local_count = hidden.shape[0]
    capacity = hidden.shape[3]
    hidden_width = hidden.shape[4]
    peer_count = lax.axis_size("expert")
    shards = lax.axis_size("dp")
    expert_count = local_count * peer_count
    col_width = row_width // shards
    block_count = peer_count * shards
    f32 = jnp.float32
    bf16 = jnp.bfloat16
    my_dp = lax.axis_index("dp")

    meta = jnp.concatenate([expert_ids.astype(bf16), gate_weights], axis=1).reshape(-1)
    meta_len = meta.shape[0]
    meta_rows = -(-meta_len // col_width)
    meta = jnp.pad(meta, (0, meta_rows * col_width - meta_len)).reshape(meta_rows, 1, col_width)
    cols = out_grad.reshape(tok_rows, shards, col_width)
    cols = jnp.concatenate([cols, jnp.broadcast_to(meta, (meta_rows, shards, col_width))], axis=0)
    cols = lax.all_to_all(cols, "dp", split_axis=1, concat_axis=0, tiled=True)
    cols = cols.reshape(shards, tok_rows + meta_rows, col_width)
    piece_xor = jnp.array([0, 2, 1, 3], jnp.int32)
    cols = jnp.take(cols, piece_xor ^ my_dp, axis=0)

    hidden_shape = hidden.shape
    hidden = hidden.reshape(-1, hidden_width)
    hidden_sent, cols = lax.optimization_barrier((hidden, cols))
    near = lax.ppermute(hidden_sent, "dp", [(j, j ^ 1) for j in range(shards)])
    far = lax.ppermute(hidden_sent, "dp", [(j, j ^ 2) for j in range(shards)])
    near_far = lax.ppermute(far, "dp", [(j, j ^ 1) for j in range(shards)])
    got = lax.all_gather(cols, "expert", axis=0, tiled=False)
    got = got.reshape(block_count, tok_rows + meta_rows, col_width)
    grad_all = got[:, :tok_rows]
    meta_all = got[:, tok_rows:].reshape(block_count, meta_rows * col_width)[:, :meta_len]
    meta_all = meta_all.reshape(block_count, tok_rows, 2 * top_count)
    ids_all = meta_all[:, :, :top_count].astype(jnp.int32)
    gate_all = meta_all[:, :, top_count:]

    my_experts = lax.axis_index("expert") * local_count + jnp.arange(local_count, dtype=jnp.int32)
    hit = ids_all[:, :, :, None] == my_experts[None, None, None, :]
    chose = jnp.any(hit, axis=2)
    gate_hit = jnp.sum(jnp.where(hit, gate_all.astype(f32)[:, :, :, None], 0.0), axis=2)
    before = (jnp.arange(tok_rows)[:, None] < jnp.arange(tok_rows)[None, :]).astype(bf16)
    rank = jnp.einsum(
        "bul,ut->btl", chose.astype(bf16), before, preferred_element_type=f32
    ).astype(jnp.int32)
    padded = -(-capacity // 8) * 8
    slot_ids = jnp.arange(padded, dtype=jnp.int32)
    chose_t = chose.transpose(0, 2, 1)
    rank_t = rank.transpose(0, 2, 1)
    gate_t = gate_hit.transpose(0, 2, 1)
    slot_row = jnp.where(chose_t, rank_t, -1)[:, :, None, :]
    gate_row = gate_t[:, :, None, :]
    weight_grad, slot_part = expert_kernel(
        (hidden, far, near, near_far), got, slot_row, gate_row, down_weight, padded, hidden_shape
    )
    slot_part = slot_part.reshape(local_count, peer_count, shards, padded)
    piece_of = jnp.array([0, 2, 1, 3], jnp.int32)[jnp.arange(shards, dtype=jnp.int32) ^ my_dp]
    slot_part = jnp.take(slot_part, piece_of, axis=2)[:, :, :, :capacity]
    send_back = slot_part.reshape(local_count, block_count, capacity)
    returned = lax.all_to_all(
        send_back, ("expert", "dp"), split_axis=1, concat_axis=1, tiled=True
    )
    returned = returned.reshape(local_count, peer_count, shards, capacity)
    slot_grad = jnp.sum(returned, axis=2).transpose(1, 0, 2).reshape(expert_count, capacity)

    own_hit = expert_ids[:, :, None] == jnp.arange(expert_count, dtype=jnp.int32)[None, None, :]
    own_chose = jnp.any(own_hit, axis=1)
    own_rank = jnp.einsum(
        "ue,ut->te", own_chose.astype(bf16), before, preferred_element_type=f32
    ).astype(jnp.int32)
    own_slot = jnp.sum(jnp.where(own_hit, own_rank[:, None, :], 0), axis=2)
    by_slot = jnp.sum(jnp.where(own_hit[:, :, :, None], slot_grad[None, None], 0.0), axis=2)
    gate_grad = jnp.sum(
        jnp.where(own_slot[:, :, None] == slot_ids[None, None, :capacity], by_slot, 0.0), axis=2
    )
    return (weight_grad, gate_grad)


def solution(mesh):
    return jax.shard_map(
        per_device,
        mesh=mesh,
        in_specs=(
            P(("groups", "expert", "dp"), None),
            P(("groups", "expert", "dp"), None),
            P(("groups", "expert", "dp"), None),
            P("expert", ("groups", "dp"), None, None, None),
            P("expert", None, "dp"),
        ),
        out_specs=(P(("groups", "expert"), None, "dp"), P(("groups", "expert", "dp"), None)),
        check_vma=False,
    )
```
